128 devices in a mesh: seq: 32 (over z_hi, x, y), vocab: 4 (over z_lo, core).
Axes of the slice: x: 4, y: 4, z: 4 (z_hi: 2, z_lo: 2; z = z_hi * 2 + z_lo), core: 2. Of those that a mesh axis runs over, the one named last changes fastest.
Arguments:
- policy_hidden: bfloat16 [8192, 2560], P('seq'), may hold values from -45 to 45
- reference_hidden: bfloat16 [8192, 2560], P('seq'), may hold values from -45 to 45
- targets: int32 [8192], P('seq'), may hold values from 0 to 2559
- lengths: int32 [4], replicated, may hold values from 1 to 4096, 8192 in all
- block_source: int32 [64], P('seq'), may hold values from 0 to 63, each once
- rollout_prompt: int32 [4], replicated, may hold values from 0 to 3, each once
- rollout_slot: int32 [4], replicated, may hold values from 0 to 3, each once
- policy_input_gain: float32 [2560], replicated, may hold values from 0.3 to 3
- policy_query_weight: bfloat16 [2560, 2048], P(None, 'vocab'), may hold values from -0.125 to 0.125
- policy_key_weight: bfloat16 [2560, 512], P(None, 'vocab'), may hold values from -0.125 to 0.125
- policy_value_weight: bfloat16 [2560, 512], P(None, 'vocab'), may hold values from -0.125 to 0.125
- policy_query_gain: float32 [128], replicated, may hold values from 0.5 to 9, as said below
- policy_key_gain: float32 [128], replicated, may hold values from 0.5 to 9, as said below
- policy_out_weight: bfloat16 [2048, 2560], P('vocab'), may hold values from -0.5 to 0.5
- policy_final_gain: float32 [2560], replicated, may hold values from 1.5 to 60, as said below
- policy_head: bfloat16 [2560, 2560], P(None, 'vocab'), may hold values from -0.125 to 0.125
- policy_prompt_keys: bfloat16 [4, 256, 512], P(None, 'seq', 'vocab'), may hold values from -6 to 6
- policy_prompt_values: bfloat16 [4, 256, 512], P(None, 'seq', 'vocab'), may hold values from -6 to 6
- reference_input_gain: float32 [2560], replicated, may hold values from 0.3 to 3
- reference_query_weight: bfloat16 [2560, 2048], P(None, 'vocab'), may hold values from -0.125 to 0.125
- reference_key_weight: bfloat16 [2560, 512], P(None, 'vocab'), may hold values from -0.125 to 0.125
- reference_value_weight: bfloat16 [2560, 512], P(None, 'vocab'), may hold values from -0.125 to 0.125
- reference_query_gain: float32 [128], replicated, may hold values from 0.5 to 9, as said below
- reference_key_gain: float32 [128], replicated, may hold values from 0.5 to 9, as said below
- reference_out_weight: bfloat16 [2048, 2560], P('vocab'), may hold values from -0.5 to 0.5
- reference_final_gain: float32 [2560], replicated, may hold values from 1.5 to 60, as said below
- reference_head: bfloat16 [2560, 2560], P(None, 'vocab'), may hold values from -0.125 to 0.125
- reference_prompt_keys: bfloat16 [4, 256, 512], P(None, 'seq', 'vocab'), may hold values from -6 to 6
- reference_prompt_values: bfloat16 [4, 256, 512], P(None, 'seq', 'vocab'), may hold values from -6 to 6
Outputs:
- token_diff: float32 [8192], P('seq')
- rollout_mean: float32 [4], replicated
The draws below stay inside these ranges and needn't reach their ends.
Inputs may be any that keep to these rules, and one draw needn't show every extreme that they name: `policy_query_gain`: positive. `policy_key_gain`: positive. `reference_query_gain`: positive. `reference_key_gain`: positive. `policy_final_gain`: positive. `reference_final_gain`: positive.
All inputs are finite; a program needn't handle non-finite values.
Results may differ from the reference program's by a relative error of at most 0.04.
The reference program's roundings to bfloat16 on the way count: a program that leaves them out, or rounds other values in their place, can miss the bound.
Values may be sent and summed in bfloat16 or wider, within the bound.
No kernel may reach another device: no remote copies, remote signals or barrier semaphores. Data moves between devices by JAX's collectives and lax.ppermute only.
A program may use at most 128 MiB of HBM per device.

```python
import math
import jax
import jax.numpy as jnp
import numpy as np
from jax import lax

D = 2560
HEADS = 16
KV_HEADS = 4
HD = 128
TOK_DEV = 256
BLOCK = 128
ROLLOUTS = 4
TOKENS = 8192
LEN = 4096
NBLK = 64
PROMPTS = 4
PREFIX = 256
VOCAB = 2560
N_SEQ = 32


def log_between(key, shape, low, high):
    unit = jax.random.uniform(key, shape, jnp.float32)
    return jnp.exp(jnp.log(low) + unit * (jnp.log(high) - jnp.log(low)))


def rows_normal(key):
    parts = jax.random.split(key, 3)
    base = jnp.clip(jax.random.normal(parts[0], (TOKENS, D), jnp.float32), -5.0, 5.0)
    row_scale = log_between(parts[1], (TOKENS, 1), 0.3, 3.0)
    col_scale = log_between(parts[2], (1, D), 0.3, 3.0)
    return base * row_scale * col_scale


def draw_policy_hidden(key, part):
    return rows_normal(jax.random.fold_in(key, 1)).astype(jnp.bfloat16)


def draw_reference_hidden(key, part):
    return rows_normal(jax.random.fold_in(key, 2)).astype(jnp.bfloat16)


def gain_drawn(key):
    return log_between(key, (HD,), 0.5, 2.0)


def final_drawn(key):
    return log_between(key, (D,), 1.5, 8.0)


def draw_policy_query_gain(key, part):
    return gain_drawn(jax.random.fold_in(key, 11))


def draw_policy_key_gain(key, part):
    return gain_drawn(jax.random.fold_in(key, 12))


def draw_reference_query_gain(key, part):
    return gain_drawn(jax.random.fold_in(key, 13))


def draw_reference_key_gain(key, part):
    return gain_drawn(jax.random.fold_in(key, 14))


def draw_policy_final_gain(key, part):
    return final_drawn(jax.random.fold_in(key, 21))


def draw_reference_final_gain(key, part):
    return final_drawn(jax.random.fold_in(key, 22))


def place_ends(result, key, least, largest):
    extent = result.shape
    spot = [jax.random.randint(jax.random.fold_in(key, axis), (), 0, extent[axis]) for axis in range(len(extent))]
    result = result.at[tuple(spot)].set(least)
    longest = extent.index(max(extent))
    spot[longest] = (spot[longest] + 1) % extent[longest]
    return result.at[tuple(spot)].set(largest)


def block_scale(own_key, extent, pieces, least, largest):
    factor_of = 1.0
    for dim, blocks in pieces:
        draws = jax.random.uniform(jax.random.fold_in(jax.random.fold_in(own_key, 6), dim), (blocks,), jnp.float32, least / len(pieces), largest / len(pieces))
        factor_of = factor_of * jnp.repeat(jnp.exp(draws), extent[dim] // blocks).reshape((-1,) + (1,) * (len(extent) - 1 - dim))
    return factor_of


def rank_table(number_of, lean):
    portions = [(1 << 20) // math.isqrt(grade ** lean) + 1 for grade in range(1, number_of + 1)]
    deviation = 1 + sum(portions) // (1 << 30)
    return np.cumsum(np.array([max(1, weight // deviation) for weight in portions]))


def ranked(rng, dims, amount, lean):
    table = rank_table(amount, lean)
    pick = jax.random.randint(jax.random.fold_in(rng, 1), dims, 0, int(table[amount - 1]))
    standing = jnp.searchsorted(jnp.asarray(table, jnp.int32), pick, side="right")
    return jax.random.permutation(jax.random.fold_in(rng, 2), amount)[standing].astype(jnp.int32)


def profile(number_of, total, most, lean):
    portions = [(1 << 20) // math.isqrt(rank ** lean) + 1 for rank in range(2, number_of + 1)]
    surplus, given = total - most - (number_of - 1), [1] * (number_of - 1)
    while surplus > 0:
        candidates = [i for i in range(number_of - 1) if given[i] < most]
        whole, remaining = sum([portions[i] for i in candidates]), surplus
        for i in candidates:
            extra = min(most - given[i], max(1, remaining * portions[i] // whole), surplus)
            given[i] = given[i] + extra
            surplus = surplus - extra
    return np.array([most] + given)


def uneven_parts(rng, number_of, total, bound, skew):
    if number_of == 2:
        one = jax.random.randint(rng, (), max(1, total - bound), min(bound, total - 1) + 1)
        return jnp.stack([one, total - one])
    tallies = jnp.asarray(profile(number_of, total, bound, skew), jnp.int32)
    couples = (number_of - 1) // 2
    giver, sink = tallies[1:1 + 2 * couples:2], tallies[2:2 + 2 * couples:2]
    slack = jnp.minimum(giver - 1, bound - sink)
    shifted = jax.random.randint(jax.random.fold_in(rng, 1), (couples,), 0, 1 << 20) % (slack + 1)
    tallies = tallies.at[1:1 + 2 * couples:2].set(giver - shifted).at[2:2 + 2 * couples:2].set(sink + shifted)
    return tallies[jax.random.permutation(jax.random.fold_in(rng, 2), number_of)]


def centred(own_key, dims, width, limit, shards=(), kind=jnp.bfloat16):
    factor_of = block_scale(own_key, dims, shards, -0.22, 0.18) if shards else 1.0
    entries = jax.random.normal(own_key, dims, jnp.float32) * width * factor_of
    return jnp.minimum(jnp.maximum(entries, -limit), limit).astype(kind)


def setup_inputs(seed: int = 0) -> dict:
    arg_keys = jax.random.split(jax.random.key(seed), 30)
    policy_hidden = draw_policy_hidden(jax.random.fold_in(arg_keys[29], 71), 0)
    reference_hidden = draw_reference_hidden(jax.random.fold_in(arg_keys[29], 71), 0)
    targets = place_ends(ranked(arg_keys[2], (TOKENS,), VOCAB, 2), jax.random.fold_in(arg_keys[2], 3), 0, VOCAB - 1).astype(jnp.int32)
    lengths = uneven_parts(arg_keys[3], ROLLOUTS, TOKENS, LEN, 2).astype(jnp.int32)
    block_source = jax.random.permutation(arg_keys[4], NBLK).astype(jnp.int32)
    rollout_prompt = jax.random.permutation(arg_keys[5], PROMPTS).astype(jnp.int32)
    rollout_slot = jax.random.permutation(arg_keys[6], ROLLOUTS).astype(jnp.int32)
    policy_input_gain = jnp.clip(jnp.exp(jax.random.uniform(arg_keys[7], (D,), jnp.float32, math.log(0.3), math.log(3.0))), 0.3, 3.0)
    policy_query_weight = centred(arg_keys[8], (D, HEADS * HD), D ** -0.5, 0.125, ((1, 4),))
    policy_key_weight = centred(arg_keys[9], (D, KV_HEADS * HD), D ** -0.5, 0.125, ((1, 4),))
    policy_value_weight = centred(arg_keys[10], (D, KV_HEADS * HD), D ** -0.5, 0.125, ((1, 4),))
    policy_query_gain = draw_policy_query_gain(jax.random.fold_in(arg_keys[29], 71), 0)
    policy_key_gain = draw_policy_key_gain(jax.random.fold_in(arg_keys[29], 71), 0)
    policy_out_weight = centred(arg_keys[13], (HEADS * HD, D), HD ** -0.5, 0.5, ((0, 4),))
    policy_final_gain = draw_policy_final_gain(jax.random.fold_in(arg_keys[29], 71), 0)
    policy_head = centred(arg_keys[15], (D, VOCAB), D ** -0.5, 0.125, ((1, 4),))
    policy_prompt_keys = centred(arg_keys[16], (PROMPTS, PREFIX, KV_HEADS * HD), 1.0, 6.0, ((1, 32), (2, 4)))
    policy_prompt_values = centred(arg_keys[17], (PROMPTS, PREFIX, KV_HEADS * HD), 1.0, 6.0, ((1, 32), (2, 4)))
    reference_input_gain = jnp.clip(jnp.exp(jax.random.uniform(arg_keys[18], (D,), jnp.float32, math.log(0.3), math.log(3.0))), 0.3, 3.0)
    reference_query_weight = centred(arg_keys[19], (D, HEADS * HD), D ** -0.5, 0.125, ((1, 4),))
    reference_key_weight = centred(arg_keys[20], (D, KV_HEADS * HD), D ** -0.5, 0.125, ((1, 4),))
    reference_value_weight = centred(arg_keys[21], (D, KV_HEADS * HD), D ** -0.5, 0.125, ((1, 4),))
    reference_query_gain = draw_reference_query_gain(jax.random.fold_in(arg_keys[29], 71), 0)
    reference_key_gain = draw_reference_key_gain(jax.random.fold_in(arg_keys[29], 71), 0)
    reference_out_weight = centred(arg_keys[24], (HEADS * HD, D), HD ** -0.5, 0.5, ((0, 4),))
    reference_final_gain = draw_reference_final_gain(jax.random.fold_in(arg_keys[29], 71), 0)
    reference_head = centred(arg_keys[26], (D, VOCAB), D ** -0.5, 0.125, ((1, 4),))
    reference_prompt_keys = centred(arg_keys[27], (PROMPTS, PREFIX, KV_HEADS * HD), 1.0, 6.0, ((1, 32), (2, 4)))
    reference_prompt_values = centred(arg_keys[28], (PROMPTS, PREFIX, KV_HEADS * HD), 1.0, 6.0, ((1, 32), (2, 4)))
    return {"policy_hidden": policy_hidden, "reference_hidden": reference_hidden, "targets": targets, "lengths": lengths, "block_source": block_source, "rollout_prompt": rollout_prompt, "rollout_slot": rollout_slot, "policy_input_gain": policy_input_gain, "policy_query_weight": policy_query_weight, "policy_key_weight": policy_key_weight, "policy_value_weight": policy_value_weight, "policy_query_gain": policy_query_gain, "policy_key_gain": policy_key_gain, "policy_out_weight": policy_out_weight, "policy_final_gain": policy_final_gain, "policy_head": policy_head, "policy_prompt_keys": policy_prompt_keys, "policy_prompt_values": policy_prompt_values, "reference_input_gain": reference_input_gain, "reference_query_weight": reference_query_weight, "reference_key_weight": reference_key_weight, "reference_value_weight": reference_value_weight, "reference_query_gain": reference_query_gain, "reference_key_gain": reference_key_gain, "reference_out_weight": reference_out_weight, "reference_final_gain": reference_final_gain, "reference_head": reference_head, "reference_prompt_keys": reference_prompt_keys, "reference_prompt_values": reference_prompt_values}


EPSILON = 1e-06
ROPE_BASE = 1000000.0
NEGATIVE_FILL = -1e+30

def rms_scale(values, gain_row):
    values = values.astype(jnp.float32)
    return values * lax.rsqrt(lax.optimization_barrier(jnp.mean(values * values, axis=-1, keepdims=True)) + EPSILON) * gain_row.astype(jnp.float32)

def rotate(values, positions):
    half_width = values.shape[-1] // 2
    frequency = ROPE_BASE ** (-2.0 * jnp.arange(half_width, dtype=jnp.float32) / values.shape[-1])
    angles = positions.astype(jnp.float32)[:, None] * frequency[None, :]
    cosine = jnp.cos(angles)
    sine_part = jnp.sin(angles)
    cosine = jnp.concatenate([cosine, cosine], axis=-1)[:, None, :]
    sine_part = jnp.concatenate([sine_part, sine_part], axis=-1)[:, None, :]
    turned = jnp.concatenate([-values[..., half_width:], values[..., :half_width]], axis=-1)
    return values * cosine + turned * sine_part

def layout(block_source, lengths):
    slot_ids = jnp.arange(TOKENS, dtype=jnp.int32)
    packed = block_source[slot_ids // BLOCK] * BLOCK + slot_ids % BLOCK
    end_points = jnp.cumsum(lengths).astype(jnp.int32)
    rollout = lax.optimization_barrier(jnp.sum((packed[:, None] >= end_points[None, :]).astype(jnp.int32), axis=1))
    starts = end_points - lengths
    position = packed - starts[rollout]
    return (rollout.astype(jnp.int32), position.astype(jnp.int32))

def score_model(hidden, rollout, position, prompt_of, targets, input_gain, query_weight, key_weight, value_weight, query_gain, key_gain, out_weight, final_gain, head_weight, prompt_keys, prompt_values):
    group_size = HEADS // KV_HEADS
    normed = rms_scale(hidden, input_gain).astype(jnp.bfloat16)
    rope_position = position + PREFIX
    query_rows = jnp.dot(normed, query_weight, preferred_element_type=jnp.float32).reshape(TOKENS, HEADS, HD)
    query_rows = rotate(rms_scale(query_rows, query_gain), rope_position).astype(jnp.bfloat16)
    key_rows = jnp.dot(normed, key_weight, preferred_element_type=jnp.float32).reshape(TOKENS, KV_HEADS, HD)
    key_rows = rotate(rms_scale(key_rows, key_gain), rope_position).astype(jnp.bfloat16)
    value_rows = jnp.dot(normed, value_weight, preferred_element_type=jnp.float32).astype(jnp.bfloat16).reshape(TOKENS, KV_HEADS, HD)
    all_keys = jnp.concatenate([key_rows, prompt_keys.reshape(PROMPTS * PREFIX, KV_HEADS, HD)], axis=0).astype(jnp.float32)
    all_values = jnp.concatenate([value_rows, prompt_values.reshape(PROMPTS * PREFIX, KV_HEADS, HD)], axis=0).astype(jnp.float32)
    prompt_ids = (jnp.arange(PROMPTS * PREFIX, dtype=jnp.int32) // PREFIX).astype(jnp.int32)
    key_tag = jnp.concatenate([rollout, -1 - prompt_ids])
    key_position = jnp.concatenate([position, jnp.full((PROMPTS * PREFIX,), -1, jnp.int32)])
    scale_factor = HD ** (-0.5)

    def one_block(block_items):
        block_query, block_tag, block_position, block_prompt = block_items
        visible = (key_tag[None, :] == block_tag[:, None]) & (key_position[None, :] <= block_position[:, None]) | (key_tag[None, :] == -1 - block_prompt[:, None])
        shaped = block_query.astype(jnp.float32).reshape(-1, KV_HEADS, group_size, HD)
        scores = jnp.einsum('qkgd,skd->kgqs', shaped, all_keys) * scale_factor
        masked = jnp.where(visible[None, None], scores, NEGATIVE_FILL)
        highest = lax.optimization_barrier(jnp.max(masked, axis=-1, keepdims=True))
        weights = jnp.where(visible[None, None], jnp.exp(scores - highest), 0.0)
        weight_sum = lax.optimization_barrier(jnp.sum(weights, axis=-1))
        rounded = lax.optimization_barrier(weights.astype(jnp.bfloat16)).astype(jnp.float32)
        attended = jnp.einsum('kgqs,skd->qkgd', rounded, all_values) / jnp.transpose(weight_sum, (2, 0, 1))[..., None]
        return attended.reshape(-1, HEADS * HD).astype(jnp.bfloat16)
    attended = lax.map(one_block, (query_rows.reshape(N_SEQ, TOK_DEV, HEADS, HD), rollout.reshape(N_SEQ, TOK_DEV), position.reshape(N_SEQ, TOK_DEV), prompt_of.reshape(N_SEQ, TOK_DEV)))
    attended = attended.reshape(TOKENS, HEADS * HD)
    mixed_rows = jnp.dot(attended, out_weight, preferred_element_type=jnp.float32)
    final_rows = rms_scale(hidden.astype(jnp.float32) + mixed_rows, final_gain).astype(jnp.bfloat16)
    logits = jnp.dot(final_rows, head_weight, preferred_element_type=jnp.float32)
    highest = lax.optimization_barrier(jnp.max(logits, axis=-1))
    log_total = highest + jnp.log(lax.optimization_barrier(jnp.sum(jnp.exp(logits - highest[:, None]), axis=-1)))
    target_logit = jnp.take_along_axis(logits, targets[:, None], axis=1)[:, 0]
    return target_logit - log_total

def reference(policy_hidden, reference_hidden, targets, lengths, block_source, rollout_prompt, rollout_slot, policy_input_gain, policy_query_weight, policy_key_weight, policy_value_weight, policy_query_gain, policy_key_gain, policy_out_weight, policy_final_gain, policy_head, policy_prompt_keys, policy_prompt_values, reference_input_gain, reference_query_weight, reference_key_weight, reference_value_weight, reference_query_gain, reference_key_gain, reference_out_weight, reference_final_gain, reference_head, reference_prompt_keys, reference_prompt_values):
    rollout, position = layout(block_source, lengths)
    prompt_of = rollout_prompt[rollout].astype(jnp.int32)
    policy_score = score_model(policy_hidden, rollout, position, prompt_of, targets, policy_input_gain, policy_query_weight, policy_key_weight, policy_value_weight, policy_query_gain, policy_key_gain, policy_out_weight, policy_final_gain, policy_head, policy_prompt_keys, policy_prompt_values)
    reference_score = score_model(reference_hidden, rollout, position, prompt_of, targets, reference_input_gain, reference_query_weight, reference_key_weight, reference_value_weight, reference_query_gain, reference_key_gain, reference_out_weight, reference_final_gain, reference_head, reference_prompt_keys, reference_prompt_values)
    token_diff = policy_score - reference_score
    per_token = token_diff / lengths[rollout].astype(jnp.float32)
    rollout_sums = jax.ops.segment_sum(per_token, rollout, num_segments=ROLLOUTS)
    rollout_mean = jnp.zeros((ROLLOUTS,), jnp.float32).at[rollout_slot].set(rollout_sums)
    return (token_diff, rollout_mean)
```

```python
import jax
import jax.numpy as jnp
from jax import lax
from jax.sharding import PartitionSpec as P

HD = 128
BLOCK = 128


EPSILON = 1e-06
ROPE_BASE = 1000000.0
NEGATIVE_FILL = -1e30


def rms_scale(values, gain_row):
    values = values.astype(jnp.float32)
    return (
        values * lax.rsqrt(jnp.mean(values * values, axis=-1, keepdims=True) + EPSILON) * gain_row
    )


def rotate(values, positions):
    half_width = values.shape[-1] // 2
    frequency = ROPE_BASE ** (-2.0 * jnp.arange(half_width, dtype=jnp.float32) / values.shape[-1])
    angles = positions.astype(jnp.float32)[:, None] * frequency[None, :]
    cosine = jnp.cos(angles)
    sine_part = jnp.sin(angles)
    cosine = jnp.concatenate([cosine, cosine], axis=-1)[:, None, :]
    sine_part = jnp.concatenate([sine_part, sine_part], axis=-1)[:, None, :]
    turned = jnp.concatenate([-values[..., half_width:], values[..., :half_width]], axis=-1)
    return values * cosine + turned * sine_part


def lookup(member, lookup_table):
    return jnp.sum(jnp.where(member, lookup_table[None, :], 0), axis=1)


def project(
    hidden,
    input_gain,
    query_weight,
    key_weight,
    value_weight,
    query_gain,
    key_gain,
    prompt_keys,
    prompt_values,
    positions,
    rope_offset,
):
    tok_rows = hidden.shape[0]
    kv_local = key_weight.shape[1] // HD
    normed = rms_scale(hidden, input_gain).astype(jnp.bfloat16)
    query_rows = jnp.dot(normed, query_weight, preferred_element_type=jnp.float32).reshape(
        tok_rows, -1, HD
    )
    query_rows = rotate(rms_scale(query_rows, query_gain), positions + rope_offset).astype(
        jnp.bfloat16
    )
    key_rows = jnp.dot(normed, key_weight, preferred_element_type=jnp.float32).reshape(
        tok_rows, kv_local, HD
    )
    key_rows = (
        rotate(rms_scale(key_rows, key_gain), positions + rope_offset)
        .astype(jnp.bfloat16)
        .reshape(tok_rows, kv_local * HD)
    )
    value_rows = jnp.dot(normed, value_weight, preferred_element_type=jnp.float32).astype(
        jnp.bfloat16
    )
    key_block = jnp.concatenate([key_rows, prompt_keys.reshape(-1, kv_local * HD)], axis=0)
    value_block = jnp.concatenate([value_rows, prompt_values.reshape(-1, kv_local * HD)], axis=0)
    stacked = jnp.concatenate([key_block, value_block], axis=1)
    return (query_rows.reshape(tok_rows, kv_local, -1, HD), stacked)


def empty_state(query_rows):
    tok_rows, kv_local, group_size = (query_rows.shape[0], query_rows.shape[1], query_rows.shape[2])
    running_max = jnp.full((kv_local, group_size, tok_rows), NEGATIVE_FILL, jnp.float32)
    weight_sum = jnp.zeros((kv_local, group_size, tok_rows), jnp.float32)
    accumulated = jnp.zeros((tok_rows, kv_local, group_size, HD), jnp.float32)
    return (running_max, weight_sum, accumulated)


def update_state(model_state, query_rows, stacked, visible):
    running_max, weight_sum, accumulated = model_state
    half_columns = stacked.shape[1] // 2
    kv_local = query_rows.shape[1]
    key_part = stacked[:, :half_columns].reshape(-1, kv_local, HD)
    value_part = stacked[:, half_columns:].reshape(-1, kv_local, HD)
    scores = jnp.einsum(
        "qkgd,skd->kgqs", query_rows, key_part, preferred_element_type=jnp.float32
    ) * HD ** (-0.5)
    masked = jnp.where(visible[None, None], scores, NEGATIVE_FILL)
    new_max = jnp.maximum(running_max, jnp.max(masked, axis=-1))
    weights = jnp.where(visible[None, None], jnp.exp(scores - new_max[..., None]), 0.0)
    factor = jnp.exp(running_max - new_max)
    new_sum = weight_sum * factor + jnp.sum(weights, axis=-1)
    product = jnp.einsum(
        "kgqs,skd->qkgd",
        weights.astype(jnp.bfloat16),
        value_part,
        preferred_element_type=jnp.float32,
    )
    new_accumulated = accumulated * jnp.transpose(factor, (2, 0, 1))[..., None] + product
    return (new_max, new_sum, new_accumulated)


def attend(states, queries, pieces, query_tag, query_position, query_prompt):
    stacked_list = pieces[:-2]
    key_tag = pieces[-2]
    key_position = pieces[-1]
    visible = (key_tag[None, :] == query_tag[:, None]) & (
        key_position[None, :] <= query_position[:, None]
    ) | (key_tag[None, :] == -1 - query_prompt[:, None])

    def compute(current):
        updated = []
        for model_state, query_rows, stacked in zip(current, queries, stacked_list):
            updated.append(update_state(model_state, query_rows, stacked, visible))
        return tuple(updated)

    def unchanged(current):
        return current

    return lax.cond(jnp.any(visible), compute, unchanged, states)


def make_fold(queries, query_tag, query_position, query_prompt, shard_rows):

    def fold_pieces(states, pieces, start_row):
        rows_here = pieces[0].shape[0]
        shard_count = rows_here // shard_rows
        split_pieces = tuple(
            (
                member_piece.reshape((shard_count, shard_rows) + member_piece.shape[1:])
                for member_piece in pieces
            )
        )

        def scan_step(carry_states, piece_item):
            return (
                attend(carry_states, queries, piece_item, query_tag, query_position, query_prompt),
                None,
            )

        return lax.scan(scan_step, states, split_pieces)[0]

    return fold_pieces


def finish(model_state, out_weight):
    running_max, weight_sum, accumulated = model_state
    attended = accumulated / jnp.transpose(weight_sum, (2, 0, 1))[..., None]
    attended = attended.reshape(accumulated.shape[0], -1).astype(jnp.bfloat16)
    return jnp.dot(attended, out_weight, preferred_element_type=jnp.float32)


def head_terms(final_rows, head_weight, targets, vocab_start):
    logits = jnp.dot(final_rows, head_weight, preferred_element_type=jnp.float32)
    local_max = jnp.max(logits, axis=-1)
    word_ids = vocab_start + jnp.arange(logits.shape[1], dtype=jnp.int32)
    target_logit = jnp.sum(jnp.where(word_ids[None, :] == targets[:, None], logits, 0.0), axis=-1)
    return (logits, local_max, target_logit)


def local(
    policy_hidden,
    reference_hidden,
    targets,
    lengths,
    block_source,
    rollout_prompt,
    rollout_slot,
    policy_input_gain,
    policy_query_weight,
    policy_key_weight,
    policy_value_weight,
    policy_query_gain,
    policy_key_gain,
    policy_out_weight,
    policy_final_gain,
    policy_head,
    policy_prompt_keys,
    policy_prompt_values,
    reference_input_gain,
    reference_query_weight,
    reference_key_weight,
    reference_value_weight,
    reference_query_gain,
    reference_key_gain,
    reference_out_weight,
    reference_final_gain,
    reference_head,
    reference_prompt_keys,
    reference_prompt_values,
):
    tok_rows = policy_hidden.shape[0]
    roll_ids = jnp.arange(lengths.shape[0], dtype=jnp.int32)
    slot_ids = jnp.arange(tok_rows, dtype=jnp.int32)
    packed = jnp.repeat(block_source, BLOCK) * BLOCK + slot_ids % BLOCK
    end_points = jnp.cumsum(lengths)
    rollout = jnp.sum((packed[:, None] >= end_points[None, :]).astype(jnp.int32), axis=1)
    member = rollout[:, None] == roll_ids[None, :]
    position = packed - lookup(member, end_points - lengths)
    query_prompt = lookup(member, rollout_prompt)
    slot_of = lookup(member, rollout_slot)
    length_of = lookup(member, lengths)
    prompt_count = policy_prompt_keys.shape[0]
    prefix_local = policy_prompt_keys.shape[1]
    prompt_rows = prompt_count * prefix_local
    rope_offset = prefix_local * lax.axis_size("seq")
    prompt_ids = jnp.arange(prompt_rows, dtype=jnp.int32) // prefix_local
    seq_count = lax.axis_size("seq")
    lead = lax.axis_index("vocab") == 0
    source_slots = jnp.zeros((seq_count, block_source.shape[0]), jnp.int32)
    source_slots = lax.dynamic_update_slice(
        source_slots, jnp.where(lead, block_source, 0)[None, :], (lax.axis_index("seq"), 0)
    )
    all_source = lax.psum(source_slots, ("seq", "vocab")).reshape(-1)
    all_ids = jnp.arange(tok_rows * seq_count, dtype=jnp.int32)
    all_packed = jnp.repeat(all_source, BLOCK) * BLOCK + all_ids % BLOCK
    all_rollout = jnp.sum((all_packed[:, None] >= end_points[None, :]).astype(jnp.int32), axis=1)
    all_member = all_rollout[:, None] == roll_ids[None, :]
    all_position = all_packed - lookup(all_member, end_points - lengths)
    key_tag = jnp.concatenate(
        [
            all_rollout.reshape(seq_count, tok_rows),
            jnp.broadcast_to(-1 - prompt_ids, (seq_count, prompt_rows)),
        ],
        axis=1,
    ).reshape(-1)
    key_position = jnp.concatenate(
        [
            all_position.reshape(seq_count, tok_rows),
            jnp.full((seq_count, prompt_rows), -1, jnp.int32),
        ],
        axis=1,
    ).reshape(-1)
    shard_rows = tok_rows + prompt_rows
    policy_query, policy_stack = project(
        policy_hidden,
        policy_input_gain,
        policy_query_weight,
        policy_key_weight,
        policy_value_weight,
        policy_query_gain,
        policy_key_gain,
        policy_prompt_keys,
        policy_prompt_values,
        position,
        rope_offset,
    )
    reference_query, reference_stack = project(
        reference_hidden,
        reference_input_gain,
        reference_query_weight,
        reference_key_weight,
        reference_value_weight,
        reference_query_gain,
        reference_key_gain,
        reference_prompt_keys,
        reference_prompt_values,
        position,
        rope_offset,
    )
    fold_policy = make_fold((policy_query,), rollout, position, query_prompt, shard_rows)
    (policy_state,) = fold_policy(
        (empty_state(policy_query),),
        (
            lax.all_gather(policy_stack, "seq", axis=0, tiled=True),
            key_tag,
            key_position,
        ),
        jnp.int32(0),
    )
    fold_reference = make_fold((reference_query,), rollout, position, query_prompt, shard_rows)
    (reference_state,) = fold_reference(
        (empty_state(reference_query),),
        (
            lax.all_gather(reference_stack, "seq", axis=0, tiled=True),
            key_tag,
            key_position,
        ),
        jnp.int32(0),
    )
    policy_part = finish(policy_state, policy_out_weight)
    reference_part = finish(reference_state, reference_out_weight)
    policy_mixed, reference_mixed = (
        lax.psum(policy_part.astype(jnp.bfloat16), "vocab").astype(jnp.float32),
        lax.psum(reference_part.astype(jnp.bfloat16), "vocab").astype(jnp.float32),
    )
    policy_final = rms_scale(
        policy_hidden.astype(jnp.float32) + policy_mixed, policy_final_gain
    ).astype(jnp.bfloat16)
    reference_final = rms_scale(
        reference_hidden.astype(jnp.float32) + reference_mixed, reference_final_gain
    ).astype(jnp.bfloat16)
    vocab_start = lax.axis_index("vocab") * policy_head.shape[1]
    policy_logits, policy_max, policy_target = head_terms(
        policy_final, policy_head, targets, vocab_start
    )
    reference_logits, reference_max, reference_target = head_terms(
        reference_final, reference_head, targets, vocab_start
    )
    policy_top, reference_top = lax.pmax((policy_max, reference_max), "vocab")
    policy_local = jnp.sum(jnp.exp(policy_logits - policy_top[:, None]), axis=-1)
    reference_local = jnp.sum(jnp.exp(reference_logits - reference_top[:, None]), axis=-1)
    totals = lax.psum((policy_local, reference_local, policy_target, reference_target), "vocab")
    policy_score = totals[2] - (policy_top + jnp.log(totals[0]))
    reference_score = totals[3] - (reference_top + jnp.log(totals[1]))
    token_diff = policy_score - reference_score
    per_token = token_diff / length_of.astype(jnp.float32)
    partial_sums = jnp.sum(
        jnp.where(slot_of[:, None] == roll_ids[None, :], per_token[:, None], 0.0), axis=0
    )
    rollout_mean = lax.psum(jnp.where(lead, partial_sums, 0.0), ("seq", "vocab"))
    return (token_diff, rollout_mean)


def solution(mesh):
    return jax.shard_map(
        local,
        mesh=mesh,
        in_specs=(
            P("seq", None),
            P("seq", None),
            P("seq"),
            P(),
            P("seq"),
            P(),
            P(),
            P(),
            P(None, "vocab"),
            P(None, "vocab"),
            P(None, "vocab"),
            P(),
            P(),
            P("vocab", None),
            P(),
            P(None, "vocab"),
            P(None, "seq", "vocab"),
            P(None, "seq", "vocab"),
            P(),
            P(None, "vocab"),
            P(None, "vocab"),
            P(None, "vocab"),
            P(),
            P(),
            P("vocab", None),
            P(),
            P(None, "vocab"),
            P(None, "seq", "vocab"),
            P(None, "seq", "vocab"),
        ),
        out_specs=(P("seq"), P()),
        check_vma=False,
    )
```

```python
import jax
import jax.numpy as jnp
from jax import lax
from jax.sharding import PartitionSpec as P
from jax.experimental import pallas as pl
from jax.experimental.pallas import tpu as pltpu

HD = 128
BLOCK = 128


EPSILON = 1e-06
ROPE_BASE = 1000000.0
NEGATIVE_FILL = -1e30


def rms_scale(values, gain_row):
    values = values.astype(jnp.float32)
    return (
        values * lax.rsqrt(jnp.mean(values * values, axis=-1, keepdims=True) + EPSILON) * gain_row
    )


def rotate(values, positions):
    half_width = values.shape[-1] // 2
    frequency = ROPE_BASE ** (-2.0 * jnp.arange(half_width, dtype=jnp.float32) / values.shape[-1])
    angles = positions.astype(jnp.float32)[:, None] * frequency[None, :]
    cosine = jnp.cos(angles)
    sine_part = jnp.sin(angles)
    cosine = jnp.concatenate([cosine, cosine], axis=-1)[:, None, :]
    sine_part = jnp.concatenate([sine_part, sine_part], axis=-1)[:, None, :]
    turned = jnp.concatenate([-values[..., half_width:], values[..., :half_width]], axis=-1)
    return values * cosine + turned * sine_part


def lookup(member, lookup_table):
    return jnp.sum(jnp.where(member, lookup_table[None, :], 0), axis=1)


def project(
    hidden,
    input_gain,
    query_weight,
    key_weight,
    value_weight,
    query_gain,
    key_gain,
    prompt_keys,
    prompt_values,
    positions,
    rope_offset,
):
    tok_rows = hidden.shape[0]
    kv_local = key_weight.shape[1] // HD
    normed = rms_scale(hidden, input_gain).astype(jnp.bfloat16)
    query_rows = jnp.dot(normed, query_weight, preferred_element_type=jnp.float32).reshape(
        tok_rows, -1, HD
    )
    query_rows = rotate(rms_scale(query_rows, query_gain), positions + rope_offset).astype(
        jnp.bfloat16
    )
    key_rows = jnp.dot(normed, key_weight, preferred_element_type=jnp.float32).reshape(
        tok_rows, kv_local, HD
    )
    key_rows = (
        rotate(rms_scale(key_rows, key_gain), positions + rope_offset)
        .astype(jnp.bfloat16)
        .reshape(tok_rows, kv_local * HD)
    )
    value_rows = jnp.dot(normed, value_weight, preferred_element_type=jnp.float32).astype(
        jnp.bfloat16
    )
    key_block = jnp.concatenate([key_rows, prompt_keys.reshape(-1, kv_local * HD)], axis=0)
    value_block = jnp.concatenate([value_rows, prompt_values.reshape(-1, kv_local * HD)], axis=0)
    stacked = jnp.concatenate([key_block, value_block], axis=1)
    return (query_rows.reshape(tok_rows, kv_local, -1, HD), stacked)


def empty_state(query_rows):
    tok_rows, kv_local, group_size = (query_rows.shape[0], query_rows.shape[1], query_rows.shape[2])
    running_max = jnp.full((kv_local, group_size, tok_rows), NEGATIVE_FILL, jnp.float32)
    weight_sum = jnp.zeros((kv_local, group_size, tok_rows), jnp.float32)
    accumulated = jnp.zeros((tok_rows, kv_local, group_size, HD), jnp.float32)
    return (running_max, weight_sum, accumulated)


def update_state(model_state, query_rows, stacked, visible):
    running_max, weight_sum, accumulated = model_state
    half_columns = stacked.shape[1] // 2
    kv_local = query_rows.shape[1]
    key_part = stacked[:, :half_columns].reshape(-1, kv_local, HD)
    value_part = stacked[:, half_columns:].reshape(-1, kv_local, HD)
    scores = jnp.einsum(
        "qkgd,skd->kgqs", query_rows, key_part, preferred_element_type=jnp.float32
    ) * HD ** (-0.5)
    masked = jnp.where(visible[None, None], scores, NEGATIVE_FILL)
    new_max = jnp.maximum(running_max, jnp.max(masked, axis=-1))
    weights = jnp.where(visible[None, None], jnp.exp(scores - new_max[..., None]), 0.0)
    factor = jnp.exp(running_max - new_max)
    new_sum = weight_sum * factor + jnp.sum(weights, axis=-1)
    product = jnp.einsum(
        "kgqs,skd->qkgd",
        weights.astype(jnp.bfloat16),
        value_part,
        preferred_element_type=jnp.float32,
    )
    new_accumulated = accumulated * jnp.transpose(factor, (2, 0, 1))[..., None] + product
    return (new_max, new_sum, new_accumulated)


def attend(states, queries, pieces, query_tag, query_position, query_prompt):
    stacked_list = pieces[:-2]
    key_tag = pieces[-2]
    key_position = pieces[-1]
    visible = (key_tag[None, :] == query_tag[:, None]) & (
        key_position[None, :] <= query_position[:, None]
    ) | (key_tag[None, :] == -1 - query_prompt[:, None])

    def compute(current):
        updated = []
        for model_state, query_rows, stacked in zip(current, queries, stacked_list):
            updated.append(update_state(model_state, query_rows, stacked, visible))
        return tuple(updated)

    def unchanged(current):
        return current

    return lax.cond(jnp.any(visible), compute, unchanged, states)


def make_fold(queries, query_tag, query_position, query_prompt, shard_rows):

    def fold_pieces(states, pieces, start_row):
        rows_here = pieces[0].shape[0]
        shard_count = rows_here // shard_rows
        split_pieces = tuple(
            (
                member_piece.reshape((shard_count, shard_rows) + member_piece.shape[1:])
                for member_piece in pieces
            )
        )

        def scan_step(carry_states, piece_item):
            return (
                attend(carry_states, queries, piece_item, query_tag, query_position, query_prompt),
                None,
            )

        return lax.scan(scan_step, states, split_pieces)[0]

    return fold_pieces


Q_TILE = 512
K_TILE = 1024
CODE_STRIDE = 65536


def flash_kernel(flags_ref, q_ref, kv_ref, kcode_ref, qlo_ref, qhi_ref, out_ref, m_sc, l_sc, acc_sc):
    j = pl.program_id(1)

    @pl.when(j == 0)
    def _():
        m_sc[...] = jnp.full(m_sc.shape, NEGATIVE_FILL, jnp.float32)
        l_sc[...] = jnp.zeros(l_sc.shape, jnp.float32)
        acc_sc[...] = jnp.zeros(acc_sc.shape, jnp.float32)

    @pl.when(flags_ref[j] > 0)
    def _():
        kv = kv_ref[...]
        scores = lax.dot_general(
            q_ref[...], kv[:, :HD], (((1,), (1,)), ((), ())), preferred_element_type=jnp.float32
        ) * HD ** (-0.5)
        key_code = kcode_ref[...]
        visible = (key_code >= qlo_ref[...]) & (key_code <= qhi_ref[...])
        masked = jnp.where(visible, scores, NEGATIVE_FILL)
        old_max = m_sc[...]
        new_max = jnp.maximum(old_max, jnp.max(masked, axis=1, keepdims=True))
        weights = jnp.where(visible, jnp.exp(scores - new_max), 0.0)
        factor = jnp.exp(old_max - new_max)
        l_sc[...] = l_sc[...] * factor + jnp.sum(weights, axis=1, keepdims=True)
        acc_sc[...] = acc_sc[...] * factor + jnp.dot(
            weights.astype(jnp.bfloat16), kv[:, HD:], preferred_element_type=jnp.float32
        )
        m_sc[...] = new_max

    @pl.when(j == pl.num_programs(1) - 1)
    def _():
        out_ref[...] = (acc_sc[...] / l_sc[...]).astype(out_ref.dtype)


def flash_attend(flags, queries, stacked, key_code, query_low, query_high):
    q_rows = queries.shape[0]
    k_rows = stacked.shape[0]
    grid_spec = pltpu.PrefetchScalarGridSpec(
        num_scalar_prefetch=1,
        grid=(q_rows // Q_TILE, k_rows // K_TILE),
        in_specs=[
            pl.BlockSpec((Q_TILE, HD), lambda i, j, f: (i, 0)),
            pl.BlockSpec((K_TILE, 2 * HD), lambda i, j, f: (j, 0)),
            pl.BlockSpec((1, K_TILE), lambda i, j, f: (0, j)),
            pl.BlockSpec((Q_TILE, 1), lambda i, j, f: (i, 0)),
            pl.BlockSpec((Q_TILE, 1), lambda i, j, f: (i, 0)),
        ],
        out_specs=pl.BlockSpec((Q_TILE, HD), lambda i, j, f: (i, 0)),
        scratch_shapes=[
            pltpu.VMEM((Q_TILE, 1), jnp.float32),
            pltpu.VMEM((Q_TILE, 1), jnp.float32),
            pltpu.VMEM((Q_TILE, HD), jnp.float32),
        ],
    )
    return pl.pallas_call(
        flash_kernel,
        grid_spec=grid_spec,
        out_shape=jax.ShapeDtypeStruct((q_rows, HD), jnp.bfloat16),
        compiler_params=pltpu.CompilerParams(dimension_semantics=("arbitrary", "arbitrary")),
    )(flags, queries, stacked, key_code, query_low, query_high)


def attend_model(query_rows, gathered, flags, key_code, query_low, query_high, out_weight):
    tok_rows, kv_local, group_size = query_rows.shape[:3]
    flat_query = jnp.transpose(query_rows, (1, 2, 0, 3)).reshape(-1, HD)
    tiled_low = jnp.tile(query_low, kv_local * group_size)[:, None]
    tiled_high = jnp.tile(query_high, kv_local * group_size)[:, None]
    attended = flash_attend(flags, flat_query, gathered, key_code[None, :], tiled_low, tiled_high)
    attended = jnp.transpose(attended.reshape(kv_local, group_size, tok_rows, HD), (2, 0, 1, 3))
    attended = attended.reshape(tok_rows, -1)
    return jnp.dot(attended, out_weight, preferred_element_type=jnp.float32)


def finish(model_state, out_weight):
    running_max, weight_sum, accumulated = model_state
    attended = accumulated / jnp.transpose(weight_sum, (2, 0, 1))[..., None]
    attended = attended.reshape(accumulated.shape[0], -1).astype(jnp.bfloat16)
    return jnp.dot(attended, out_weight, preferred_element_type=jnp.float32)


def head_terms(final_rows, head_weight, targets, vocab_start):
    logits = jnp.dot(final_rows, head_weight, preferred_element_type=jnp.float32)
    local_max = jnp.max(logits, axis=-1)
    word_ids = vocab_start + jnp.arange(logits.shape[1], dtype=jnp.int32)
    target_logit = jnp.sum(jnp.where(word_ids[None, :] == targets[:, None], logits, 0.0), axis=-1)
    return (logits, local_max, target_logit)


def local(
    policy_hidden,
    reference_hidden,
    targets,
    lengths,
    block_source,
    rollout_prompt,
    rollout_slot,
    policy_input_gain,
    policy_query_weight,
    policy_key_weight,
    policy_value_weight,
    policy_query_gain,
    policy_key_gain,
    policy_out_weight,
    policy_final_gain,
    policy_head,
    policy_prompt_keys,
    policy_prompt_values,
    reference_input_gain,
    reference_query_weight,
    reference_key_weight,
    reference_value_weight,
    reference_query_gain,
    reference_key_gain,
    reference_out_weight,
    reference_final_gain,
    reference_head,
    reference_prompt_keys,
    reference_prompt_values,
):
    tok_rows = policy_hidden.shape[0]
    roll_ids = jnp.arange(lengths.shape[0], dtype=jnp.int32)
    slot_ids = jnp.arange(tok_rows, dtype=jnp.int32)
    packed = jnp.repeat(block_source, BLOCK) * BLOCK + slot_ids % BLOCK
    end_points = jnp.cumsum(lengths)
    rollout = jnp.sum((packed[:, None] >= end_points[None, :]).astype(jnp.int32), axis=1)
    member = rollout[:, None] == roll_ids[None, :]
    position = packed - lookup(member, end_points - lengths)
    query_prompt = lookup(member, rollout_prompt)
    slot_of = lookup(member, rollout_slot)
    length_of = lookup(member, lengths)
    prompt_count = policy_prompt_keys.shape[0]
    prefix_local = policy_prompt_keys.shape[1]
    prompt_rows = prompt_count * prefix_local
    rope_offset = prefix_local * lax.axis_size("seq")
    prompt_ids = jnp.arange(prompt_rows, dtype=jnp.int32) // prefix_local
    seq_count = lax.axis_size("seq")
    lead = lax.axis_index("vocab") == 0
    source_slots = jnp.zeros((seq_count, block_source.shape[0]), jnp.int32)
    source_slots = lax.dynamic_update_slice(
        source_slots, jnp.where(lead, block_source, 0)[None, :], (lax.axis_index("seq"), 0)
    )
    all_source = lax.psum(source_slots, ("seq", "vocab")).reshape(-1)
    all_ids = jnp.arange(tok_rows * seq_count, dtype=jnp.int32)
    all_packed = jnp.repeat(all_source, BLOCK) * BLOCK + all_ids % BLOCK
    all_rollout = jnp.sum((all_packed[:, None] >= end_points[None, :]).astype(jnp.int32), axis=1)
    all_member = all_rollout[:, None] == roll_ids[None, :]
    all_position = all_packed - lookup(all_member, end_points - lengths)
    owner = lookup(rollout_prompt[None, :] == jnp.arange(prompt_count, dtype=jnp.int32)[:, None], roll_ids)
    key_code = jnp.concatenate(
        [
            (all_rollout * CODE_STRIDE + all_position).reshape(seq_count, tok_rows),
            jnp.broadcast_to(owner[prompt_ids] * CODE_STRIDE - 1, (seq_count, prompt_rows)),
        ],
        axis=1,
    ).reshape(-1)
    query_low = rollout * CODE_STRIDE - 1
    query_high = rollout * CODE_STRIDE + position
    seen = (key_code[None, :] >= query_low[:, None]) & (key_code[None, :] <= query_high[:, None])
    flags = jnp.any(seen.reshape(tok_rows, -1, K_TILE), axis=(0, 2)).astype(jnp.int32)
    shard_rows = tok_rows + prompt_rows
    policy_query, policy_stack = project(
        policy_hidden,
        policy_input_gain,
        policy_query_weight,
        policy_key_weight,
        policy_value_weight,
        policy_query_gain,
        policy_key_gain,
        policy_prompt_keys,
        policy_prompt_values,
        position,
        rope_offset,
    )
    reference_query, reference_stack = project(
        reference_hidden,
        reference_input_gain,
        reference_query_weight,
        reference_key_weight,
        reference_value_weight,
        reference_query_gain,
        reference_key_gain,
        reference_prompt_keys,
        reference_prompt_values,
        position,
        rope_offset,
    )
    policy_part = attend_model(
        policy_query,
        lax.all_gather(policy_stack, "seq", axis=0, tiled=True),
        flags,
        key_code,
        query_low,
        query_high,
        policy_out_weight,
    )
    reference_part = attend_model(
        reference_query,
        lax.all_gather(reference_stack, "seq", axis=0, tiled=True),
        flags,
        key_code,
        query_low,
        query_high,
        reference_out_weight,
    )
    policy_mixed, reference_mixed = (
        lax.psum(policy_part.astype(jnp.bfloat16), "vocab").astype(jnp.float32),
        lax.psum(reference_part.astype(jnp.bfloat16), "vocab").astype(jnp.float32),
    )
    policy_final = rms_scale(
        policy_hidden.astype(jnp.float32) + policy_mixed, policy_final_gain
    ).astype(jnp.bfloat16)
    reference_final = rms_scale(
        reference_hidden.astype(jnp.float32) + reference_mixed, reference_final_gain
    ).astype(jnp.bfloat16)
    vocab_start = lax.axis_index("vocab") * policy_head.shape[1]
    policy_logits, policy_max, policy_target = head_terms(
        policy_final, policy_head, targets, vocab_start
    )
    reference_logits, reference_max, reference_target = head_terms(
        reference_final, reference_head, targets, vocab_start
    )
    policy_top, reference_top = lax.pmax((policy_max, reference_max), "vocab")
    policy_local = jnp.sum(jnp.exp(policy_logits - policy_top[:, None]), axis=-1)
    reference_local = jnp.sum(jnp.exp(reference_logits - reference_top[:, None]), axis=-1)
    totals = lax.psum((policy_local, reference_local, policy_target, reference_target), "vocab")
    policy_score = totals[2] - (policy_top + jnp.log(totals[0]))
    reference_score = totals[3] - (reference_top + jnp.log(totals[1]))
    token_diff = policy_score - reference_score
    per_token = token_diff / length_of.astype(jnp.float32)
    partial_sums = jnp.sum(
        jnp.where(slot_of[:, None] == roll_ids[None, :], per_token[:, None], 0.0), axis=0
    )
    rollout_mean = lax.psum(jnp.where(lead, partial_sums, 0.0), ("seq", "vocab"))
    return (token_diff, rollout_mean)


def solution(mesh):
    return jax.shard_map(
        local,
        mesh=mesh,
        in_specs=(
            P("seq", None),
            P("seq", None),
            P("seq"),
            P(),
            P("seq"),
            P(),
            P(),
            P(),
            P(None, "vocab"),
            P(None, "vocab"),
            P(None, "vocab"),
            P(),
            P(),
            P("vocab", None),
            P(),
            P(None, "vocab"),
            P(None, "seq", "vocab"),
            P(None, "seq", "vocab"),
            P(),
            P(None, "vocab"),
            P(None, "vocab"),
            P(None, "vocab"),
            P(),
            P(),
            P("vocab", None),
            P(),
            P(None, "vocab"),
            P(None, "seq", "vocab"),
            P(None, "seq", "vocab"),
        ),
        out_specs=(P("seq"), P()),
        check_vma=False,
    )
```

```python
import jax
import jax.numpy as jnp
from jax import lax
from jax.sharding import PartitionSpec as P
from jax.experimental import pallas as pl
from jax.experimental.pallas import tpu as pltpu

HD = 128
BLOCK = 128


EPSILON = 1e-06
ROPE_BASE = 1000000.0
NEGATIVE_FILL = -1e30


def rms_scale(values, gain_row):
    values = values.astype(jnp.float32)
    return (
        values * lax.rsqrt(jnp.mean(values * values, axis=-1, keepdims=True) + EPSILON) * gain_row
    )


def rotate(values, positions):
    half_width = values.shape[-1] // 2
    frequency = ROPE_BASE ** (-2.0 * jnp.arange(half_width, dtype=jnp.float32) / values.shape[-1])
    angles = positions.astype(jnp.float32)[:, None] * frequency[None, :]
    cosine = jnp.cos(angles)
    sine_part = jnp.sin(angles)
    cosine = jnp.concatenate([cosine, cosine], axis=-1)[:, None, :]
    sine_part = jnp.concatenate([sine_part, sine_part], axis=-1)[:, None, :]
    turned = jnp.concatenate([-values[..., half_width:], values[..., :half_width]], axis=-1)
    return values * cosine + turned * sine_part


def lookup(member, lookup_table):
    return jnp.sum(jnp.where(member, lookup_table[None, :], 0), axis=1)


def project(
    hidden,
    input_gain,
    query_weight,
    key_weight,
    value_weight,
    query_gain,
    key_gain,
    prompt_keys,
    prompt_values,
    positions,
    rope_offset,
):
    tok_rows = hidden.shape[0]
    kv_local = key_weight.shape[1] // HD
    normed = rms_scale(hidden, input_gain).astype(jnp.bfloat16)
    query_rows = jnp.dot(normed, query_weight, preferred_element_type=jnp.float32).reshape(
        tok_rows, -1, HD
    )
    query_rows = rotate(rms_scale(query_rows, query_gain), positions + rope_offset).astype(
        jnp.bfloat16
    )
    key_rows = jnp.dot(normed, key_weight, preferred_element_type=jnp.float32).reshape(
        tok_rows, kv_local, HD
    )
    key_rows = (
        rotate(rms_scale(key_rows, key_gain), positions + rope_offset)
        .astype(jnp.bfloat16)
        .reshape(tok_rows, kv_local * HD)
    )
    value_rows = jnp.dot(normed, value_weight, preferred_element_type=jnp.float32).astype(
        jnp.bfloat16
    )
    key_block = jnp.concatenate([key_rows, prompt_keys.reshape(-1, kv_local * HD)], axis=0)
    value_block = jnp.concatenate([value_rows, prompt_values.reshape(-1, kv_local * HD)], axis=0)
    stacked = jnp.concatenate([key_block, value_block], axis=1)
    return (query_rows.reshape(tok_rows, kv_local, -1, HD), stacked)


def empty_state(query_rows):
    tok_rows, kv_local, group_size = (query_rows.shape[0], query_rows.shape[1], query_rows.shape[2])
    running_max = jnp.full((kv_local, group_size, tok_rows), NEGATIVE_FILL, jnp.float32)
    weight_sum = jnp.zeros((kv_local, group_size, tok_rows), jnp.float32)
    accumulated = jnp.zeros((tok_rows, kv_local, group_size, HD), jnp.float32)
    return (running_max, weight_sum, accumulated)


def update_state(model_state, query_rows, stacked, visible):
    running_max, weight_sum, accumulated = model_state
    half_columns = stacked.shape[1] // 2
    kv_local = query_rows.shape[1]
    key_part = stacked[:, :half_columns].reshape(-1, kv_local, HD)
    value_part = stacked[:, half_columns:].reshape(-1, kv_local, HD)
    scores = jnp.einsum(
        "qkgd,skd->kgqs", query_rows, key_part, preferred_element_type=jnp.float32
    ) * HD ** (-0.5)
    masked = jnp.where(visible[None, None], scores, NEGATIVE_FILL)
    new_max = jnp.maximum(running_max, jnp.max(masked, axis=-1))
    weights = jnp.where(visible[None, None], jnp.exp(scores - new_max[..., None]), 0.0)
    factor = jnp.exp(running_max - new_max)
    new_sum = weight_sum * factor + jnp.sum(weights, axis=-1)
    product = jnp.einsum(
        "kgqs,skd->qkgd",
        weights.astype(jnp.bfloat16),
        value_part,
        preferred_element_type=jnp.float32,
    )
    new_accumulated = accumulated * jnp.transpose(factor, (2, 0, 1))[..., None] + product
    return (new_max, new_sum, new_accumulated)


def attend(states, queries, pieces, query_tag, query_position, query_prompt):
    stacked_list = pieces[:-2]
    key_tag = pieces[-2]
    key_position = pieces[-1]
    visible = (key_tag[None, :] == query_tag[:, None]) & (
        key_position[None, :] <= query_position[:, None]
    ) | (key_tag[None, :] == -1 - query_prompt[:, None])

    def compute(current):
        updated = []
        for model_state, query_rows, stacked in zip(current, queries, stacked_list):
            updated.append(update_state(model_state, query_rows, stacked, visible))
        return tuple(updated)

    def unchanged(current):
        return current

    return lax.cond(jnp.any(visible), compute, unchanged, states)


def make_fold(queries, query_tag, query_position, query_prompt, shard_rows):

    def fold_pieces(states, pieces, start_row):
        rows_here = pieces[0].shape[0]
        shard_count = rows_here // shard_rows
        split_pieces = tuple(
            (
                member_piece.reshape((shard_count, shard_rows) + member_piece.shape[1:])
                for member_piece in pieces
            )
        )

        def scan_step(carry_states, piece_item):
            return (
                attend(carry_states, queries, piece_item, query_tag, query_position, query_prompt),
                None,
            )

        return lax.scan(scan_step, states, split_pieces)[0]

    return fold_pieces


Q_TILE = 512
K_TILE = 1024
CODE_STRIDE = 65536


def flash_kernel(flags_ref, q_ref, kv_ref, kcode_ref, qlo_ref, qhi_ref, out_ref, m_sc, l_sc, acc_sc):
    j = pl.program_id(1)

    @pl.when(j == 0)
    def _():
        m_sc[...] = jnp.full(m_sc.shape, NEGATIVE_FILL, jnp.float32)
        l_sc[...] = jnp.zeros(l_sc.shape, jnp.float32)
        acc_sc[...] = jnp.zeros(acc_sc.shape, jnp.float32)

    @pl.when(flags_ref[j] > 0)
    def _():
        kv = kv_ref[...]
        scores = lax.dot_general(
            q_ref[...], kv[:, :HD], (((1,), (1,)), ((), ())), preferred_element_type=jnp.float32
        ) * HD ** (-0.5)
        key_code = kcode_ref[...]
        visible = (key_code >= qlo_ref[...]) & (key_code <= qhi_ref[...])
        masked = jnp.where(visible, scores, NEGATIVE_FILL)
        old_max = m_sc[...]
        new_max = jnp.maximum(old_max, jnp.max(masked, axis=1, keepdims=True))
        weights = jnp.where(visible, jnp.exp(scores - new_max), 0.0)
        factor = jnp.exp(old_max - new_max)
        l_sc[...] = l_sc[...] * factor + jnp.sum(weights, axis=1, keepdims=True)
        acc_sc[...] = acc_sc[...] * factor + jnp.dot(
            weights.astype(jnp.bfloat16), kv[:, HD:], preferred_element_type=jnp.float32
        )
        m_sc[...] = new_max

    @pl.when(j == pl.num_programs(1) - 1)
    def _():
        out_ref[...] = (acc_sc[...] / l_sc[...]).astype(out_ref.dtype)


def flash_attend(flags, queries, stacked, key_code, query_low, query_high):
    q_rows = queries.shape[0]
    k_rows = stacked.shape[0]
    grid_spec = pltpu.PrefetchScalarGridSpec(
        num_scalar_prefetch=1,
        grid=(q_rows // Q_TILE, k_rows // K_TILE),
        in_specs=[
            pl.BlockSpec((Q_TILE, HD), lambda i, j, f: (i, 0)),
            pl.BlockSpec((K_TILE, 2 * HD), lambda i, j, f: (j, 0)),
            pl.BlockSpec((1, K_TILE), lambda i, j, f: (0, j)),
            pl.BlockSpec((Q_TILE, 1), lambda i, j, f: (i, 0)),
            pl.BlockSpec((Q_TILE, 1), lambda i, j, f: (i, 0)),
        ],
        out_specs=pl.BlockSpec((Q_TILE, HD), lambda i, j, f: (i, 0)),
        scratch_shapes=[
            pltpu.VMEM((Q_TILE, 1), jnp.float32),
            pltpu.VMEM((Q_TILE, 1), jnp.float32),
            pltpu.VMEM((Q_TILE, HD), jnp.float32),
        ],
    )
    return pl.pallas_call(
        flash_kernel,
        grid_spec=grid_spec,
        out_shape=jax.ShapeDtypeStruct((q_rows, HD), jnp.bfloat16),
        compiler_params=pltpu.CompilerParams(dimension_semantics=("arbitrary", "arbitrary")),
    )(flags, queries, stacked, key_code, query_low, query_high)


def tile_flags(key_code, query_low, query_high):
    seen = (key_code[None, :] >= query_low[:, None]) & (key_code[None, :] <= query_high[:, None])
    return jnp.any(seen.reshape(query_low.shape[0], -1, K_TILE), axis=(0, 2)).astype(jnp.int32)


def attend_model(query_rows, gathered, flags, key_code, query_low, query_high, out_weight):
    tok_rows, kv_local, group_size = query_rows.shape[:3]
    flat_query = jnp.transpose(query_rows, (1, 2, 0, 3)).reshape(-1, HD)
    tiled_low = jnp.tile(query_low, kv_local * group_size)[:, None]
    tiled_high = jnp.tile(query_high, kv_local * group_size)[:, None]
    attended = flash_attend(flags, flat_query, gathered, key_code[None, :], tiled_low, tiled_high)
    attended = jnp.transpose(attended.reshape(kv_local, group_size, tok_rows, HD), (2, 0, 1, 3))
    attended = attended.reshape(tok_rows, -1)
    return jnp.dot(attended, out_weight, preferred_element_type=jnp.float32)


def finish(model_state, out_weight):
    running_max, weight_sum, accumulated = model_state
    attended = accumulated / jnp.transpose(weight_sum, (2, 0, 1))[..., None]
    attended = attended.reshape(accumulated.shape[0], -1).astype(jnp.bfloat16)
    return jnp.dot(attended, out_weight, preferred_element_type=jnp.float32)


def head_terms(final_rows, head_weight, targets, vocab_start):
    logits = jnp.dot(final_rows, head_weight, preferred_element_type=jnp.float32)
    local_max = jnp.max(logits, axis=-1)
    word_ids = vocab_start + jnp.arange(logits.shape[1], dtype=jnp.int32)
    target_logit = jnp.sum(jnp.where(word_ids[None, :] == targets[:, None], logits, 0.0), axis=-1)
    return (logits, local_max, target_logit)


def local(
    policy_hidden,
    reference_hidden,
    targets,
    lengths,
    block_source,
    rollout_prompt,
    rollout_slot,
    policy_input_gain,
    policy_query_weight,
    policy_key_weight,
    policy_value_weight,
    policy_query_gain,
    policy_key_gain,
    policy_out_weight,
    policy_final_gain,
    policy_head,
    policy_prompt_keys,
    policy_prompt_values,
    reference_input_gain,
    reference_query_weight,
    reference_key_weight,
    reference_value_weight,
    reference_query_gain,
    reference_key_gain,
    reference_out_weight,
    reference_final_gain,
    reference_head,
    reference_prompt_keys,
    reference_prompt_values,
):
    tok_rows = policy_hidden.shape[0]
    roll_ids = jnp.arange(lengths.shape[0], dtype=jnp.int32)
    slot_ids = jnp.arange(tok_rows, dtype=jnp.int32)
    packed = jnp.repeat(block_source, BLOCK) * BLOCK + slot_ids % BLOCK
    end_points = jnp.cumsum(lengths)
    rollout = jnp.sum((packed[:, None] >= end_points[None, :]).astype(jnp.int32), axis=1)
    member = rollout[:, None] == roll_ids[None, :]
    position = packed - lookup(member, end_points - lengths)
    query_prompt = lookup(member, rollout_prompt)
    slot_of = lookup(member, rollout_slot)
    length_of = lookup(member, lengths)
    prompt_count = policy_prompt_keys.shape[0]
    prefix_local = policy_prompt_keys.shape[1]
    prompt_rows = prompt_count * prefix_local
    rope_offset = prefix_local * lax.axis_size("seq")
    prompt_ids = jnp.arange(prompt_rows, dtype=jnp.int32) // prefix_local
    seq_count = lax.axis_size("seq")
    shard_rows = tok_rows + prompt_rows
    policy_query, policy_stack = project(
        policy_hidden,
        policy_input_gain,
        policy_query_weight,
        policy_key_weight,
        policy_value_weight,
        policy_query_gain,
        policy_key_gain,
        policy_prompt_keys,
        policy_prompt_values,
        position,
        rope_offset,
    )
    reference_query, reference_stack = project(
        reference_hidden,
        reference_input_gain,
        reference_query_weight,
        reference_key_weight,
        reference_value_weight,
        reference_query_gain,
        reference_key_gain,
        reference_prompt_keys,
        reference_prompt_values,
        position,
        rope_offset,
    )
    pad_rows = prompt_rows
    carrier = jnp.zeros((pad_rows, policy_stack.shape[1]), jnp.bfloat16)
    carrier = carrier.at[0, : block_source.shape[0]].set(block_source.astype(jnp.bfloat16))
    policy_gathered = lax.all_gather(
        jnp.concatenate([policy_stack, carrier], axis=0), "seq", axis=0, tiled=True
    )
    policy_rows = policy_stack.shape[0] + pad_rows
    all_source = (
        policy_gathered.reshape(seq_count, policy_rows, -1)[:, policy_stack.shape[0], : block_source.shape[0]]
        .astype(jnp.int32)
        .reshape(-1)
    )
    all_ids = jnp.arange(tok_rows * seq_count, dtype=jnp.int32)
    all_packed = jnp.repeat(all_source, BLOCK) * BLOCK + all_ids % BLOCK
    all_rollout = jnp.sum((all_packed[:, None] >= end_points[None, :]).astype(jnp.int32), axis=1)
    all_member = all_rollout[:, None] == roll_ids[None, :]
    all_position = all_packed - lookup(all_member, end_points - lengths)
    owner = lookup(rollout_prompt[None, :] == jnp.arange(prompt_count, dtype=jnp.int32)[:, None], roll_ids)
    token_code = (all_rollout * CODE_STRIDE + all_position).reshape(seq_count, tok_rows)
    prompt_code = jnp.broadcast_to(owner[prompt_ids] * CODE_STRIDE - 1, (seq_count, prompt_rows))
    never_code = jnp.full((seq_count, pad_rows), -(1 << 30), jnp.int32)
    key_code = jnp.concatenate([token_code, prompt_code], axis=1).reshape(-1)
    policy_code = jnp.concatenate([token_code, prompt_code, never_code], axis=1).reshape(-1)
    query_low = rollout * CODE_STRIDE - 1
    query_high = rollout * CODE_STRIDE + position
    flags = tile_flags(key_code, query_low, query_high)
    policy_flags = tile_flags(policy_code, query_low, query_high)
    policy_part = attend_model(
        policy_query,
        policy_gathered,
        policy_flags,
        policy_code,
        query_low,
        query_high,
        policy_out_weight,
    )
    reference_part = attend_model(
        reference_query,
        lax.all_gather(reference_stack, "seq", axis=0, tiled=True),
        flags,
        key_code,
        query_low,
        query_high,
        reference_out_weight,
    )
    policy_mixed, reference_mixed = (
        lax.psum(policy_part.astype(jnp.bfloat16), "vocab").astype(jnp.float32),
        lax.psum(reference_part.astype(jnp.bfloat16), "vocab").astype(jnp.float32),
    )
    policy_final = rms_scale(
        policy_hidden.astype(jnp.float32) + policy_mixed, policy_final_gain
    ).astype(jnp.bfloat16)
    reference_final = rms_scale(
        reference_hidden.astype(jnp.float32) + reference_mixed, reference_final_gain
    ).astype(jnp.bfloat16)
    vocab_start = lax.axis_index("vocab") * policy_head.shape[1]
    policy_logits, policy_max, policy_target = head_terms(
        policy_final, policy_head, targets, vocab_start
    )
    reference_logits, reference_max, reference_target = head_terms(
        reference_final, reference_head, targets, vocab_start
    )
    policy_top, reference_top = lax.pmax((policy_max, reference_max), "vocab")
    policy_local = jnp.sum(jnp.exp(policy_logits - policy_top[:, None]), axis=-1)
    reference_local = jnp.sum(jnp.exp(reference_logits - reference_top[:, None]), axis=-1)
    totals = lax.psum((policy_local, reference_local, policy_target, reference_target), "vocab")
    policy_score = totals[2] - (policy_top + jnp.log(totals[0]))
    reference_score = totals[3] - (reference_top + jnp.log(totals[1]))
    token_diff = policy_score - reference_score
    per_token = token_diff / length_of.astype(jnp.float32)
    partial_sums = jnp.sum(
        jnp.where(slot_of[:, None] == roll_ids[None, :], per_token[:, None], 0.0), axis=0
    )
    rollout_mean = partial_sums
    stride = 1
    while stride < seq_count:
        rollout_mean = rollout_mean + lax.ppermute(
            rollout_mean, "seq", [(i, i ^ stride) for i in range(seq_count)]
        )
        stride *= 2
    return (token_diff, rollout_mean)


def solution(mesh):
    return jax.shard_map(
        local,
        mesh=mesh,
        in_specs=(
            P("seq", None),
            P("seq", None),
            P("seq"),
            P(),
            P("seq"),
            P(),
            P(),
            P(),
            P(None, "vocab"),
            P(None, "vocab"),
            P(None, "vocab"),
            P(),
            P(),
            P("vocab", None),
            P(),
            P(None, "vocab"),
            P(None, "seq", "vocab"),
            P(None, "seq", "vocab"),
            P(),
            P(None, "vocab"),
            P(None, "vocab"),
            P(None, "vocab"),
            P(),
            P(),
            P("vocab", None),
            P(),
            P(None, "vocab"),
            P(None, "seq", "vocab"),
            P(None, "seq", "vocab"),
        ),
        out_specs=(P("seq"), P()),
        check_vma=False,
    )
```

```python
import jax
import jax.numpy as jnp
from jax import lax
from jax.sharding import PartitionSpec as P
from jax.experimental import pallas as pl
from jax.experimental.pallas import tpu as pltpu

HD = 128
BLOCK = 128


EPSILON = 1e-06
ROPE_BASE = 1000000.0
NEGATIVE_FILL = -1e30


def rms_scale(values, gain_row):
    values = values.astype(jnp.float32)
    return (
        values * lax.rsqrt(jnp.mean(values * values, axis=-1, keepdims=True) + EPSILON) * gain_row
    )


def rotate(values, positions):
    half_width = values.shape[-1] // 2
    frequency = ROPE_BASE ** (-2.0 * jnp.arange(half_width, dtype=jnp.float32) / values.shape[-1])
    angles = positions.astype(jnp.float32)[:, None] * frequency[None, :]
    cosine = jnp.cos(angles)
    sine_part = jnp.sin(angles)
    cosine = jnp.concatenate([cosine, cosine], axis=-1)[:, None, :]
    sine_part = jnp.concatenate([sine_part, sine_part], axis=-1)[:, None, :]
    turned = jnp.concatenate([-values[..., half_width:], values[..., :half_width]], axis=-1)
    return values * cosine + turned * sine_part


def lookup(member, lookup_table):
    return jnp.sum(jnp.where(member, lookup_table[None, :], 0), axis=1)


def project(
    hidden,
    input_gain,
    query_weight,
    key_weight,
    value_weight,
    query_gain,
    key_gain,
    prompt_keys,
    prompt_values,
    positions,
    rope_offset,
):
    tok_rows = hidden.shape[0]
    kv_local = key_weight.shape[1] // HD
    normed = rms_scale(hidden, input_gain).astype(jnp.bfloat16)
    query_rows = jnp.dot(normed, query_weight, preferred_element_type=jnp.float32).reshape(
        tok_rows, -1, HD
    )
    query_rows = rotate(rms_scale(query_rows, query_gain), positions + rope_offset).astype(
        jnp.bfloat16
    )
    key_rows = jnp.dot(normed, key_weight, preferred_element_type=jnp.float32).reshape(
        tok_rows, kv_local, HD
    )
    key_rows = (
        rotate(rms_scale(key_rows, key_gain), positions + rope_offset)
        .astype(jnp.bfloat16)
        .reshape(tok_rows, kv_local * HD)
    )
    value_rows = jnp.dot(normed, value_weight, preferred_element_type=jnp.float32).astype(
        jnp.bfloat16
    )
    key_block = jnp.concatenate([key_rows, prompt_keys.reshape(-1, kv_local * HD)], axis=0)
    value_block = jnp.concatenate([value_rows, prompt_values.reshape(-1, kv_local * HD)], axis=0)
    stacked = jnp.concatenate([key_block, value_block], axis=1)
    return (query_rows.reshape(tok_rows, kv_local, -1, HD), stacked)


def empty_state(query_rows):
    tok_rows, kv_local, group_size = (query_rows.shape[0], query_rows.shape[1], query_rows.shape[2])
    running_max = jnp.full((kv_local, group_size, tok_rows), NEGATIVE_FILL, jnp.float32)
    weight_sum = jnp.zeros((kv_local, group_size, tok_rows), jnp.float32)
    accumulated = jnp.zeros((tok_rows, kv_local, group_size, HD), jnp.float32)
    return (running_max, weight_sum, accumulated)


def update_state(model_state, query_rows, stacked, visible):
    running_max, weight_sum, accumulated = model_state
    half_columns = stacked.shape[1] // 2
    kv_local = query_rows.shape[1]
    key_part = stacked[:, :half_columns].reshape(-1, kv_local, HD)
    value_part = stacked[:, half_columns:].reshape(-1, kv_local, HD)
    scores = jnp.einsum(
        "qkgd,skd->kgqs", query_rows, key_part, preferred_element_type=jnp.float32
    ) * HD ** (-0.5)
    masked = jnp.where(visible[None, None], scores, NEGATIVE_FILL)
    new_max = jnp.maximum(running_max, jnp.max(masked, axis=-1))
    weights = jnp.where(visible[None, None], jnp.exp(scores - new_max[..., None]), 0.0)
    factor = jnp.exp(running_max - new_max)
    new_sum = weight_sum * factor + jnp.sum(weights, axis=-1)
    product = jnp.einsum(
        "kgqs,skd->qkgd",
        weights.astype(jnp.bfloat16),
        value_part,
        preferred_element_type=jnp.float32,
    )
    new_accumulated = accumulated * jnp.transpose(factor, (2, 0, 1))[..., None] + product
    return (new_max, new_sum, new_accumulated)


def attend(states, queries, pieces, query_tag, query_position, query_prompt):
    stacked_list = pieces[:-2]
    key_tag = pieces[-2]
    key_position = pieces[-1]
    visible = (key_tag[None, :] == query_tag[:, None]) & (
        key_position[None, :] <= query_position[:, None]
    ) | (key_tag[None, :] == -1 - query_prompt[:, None])

    def compute(current):
        updated = []
        for model_state, query_rows, stacked in zip(current, queries, stacked_list):
            updated.append(update_state(model_state, query_rows, stacked, visible))
        return tuple(updated)

    def unchanged(current):
        return current

    return lax.cond(jnp.any(visible), compute, unchanged, states)


def make_fold(queries, query_tag, query_position, query_prompt, shard_rows):

    def fold_pieces(states, pieces, start_row):
        rows_here = pieces[0].shape[0]
        shard_count = rows_here // shard_rows
        split_pieces = tuple(
            (
                member_piece.reshape((shard_count, shard_rows) + member_piece.shape[1:])
                for member_piece in pieces
            )
        )

        def scan_step(carry_states, piece_item):
            return (
                attend(carry_states, queries, piece_item, query_tag, query_position, query_prompt),
                None,
            )

        return lax.scan(scan_step, states, split_pieces)[0]

    return fold_pieces


Q_TILE = 512
K_TILE = 1024
CODE_STRIDE = 65536


def flash_kernel(flags_ref, q_ref, kv_ref, kcode_ref, qlo_ref, qhi_ref, out_ref, m_sc, l_sc, acc_sc):
    j = pl.program_id(1)

    @pl.when(j == 0)
    def _():
        m_sc[...] = jnp.full(m_sc.shape, NEGATIVE_FILL, jnp.float32)
        l_sc[...] = jnp.zeros(l_sc.shape, jnp.float32)
        acc_sc[...] = jnp.zeros(acc_sc.shape, jnp.float32)

    @pl.when(flags_ref[j] > 0)
    def _():
        kv = kv_ref[...]
        scores = lax.dot_general(
            q_ref[...], kv[:, :HD], (((1,), (1,)), ((), ())), preferred_element_type=jnp.float32
        ) * HD ** (-0.5)
        key_code = kcode_ref[...]
        visible = (key_code >= qlo_ref[...]) & (key_code <= qhi_ref[...])
        masked = jnp.where(visible, scores, NEGATIVE_FILL)
        old_max = m_sc[...]
        new_max = jnp.maximum(old_max, jnp.max(masked, axis=1, keepdims=True))
        weights = jnp.where(visible, jnp.exp(scores - new_max), 0.0)
        factor = jnp.exp(old_max - new_max)
        l_sc[...] = l_sc[...] * factor + jnp.sum(weights, axis=1, keepdims=True)
        acc_sc[...] = acc_sc[...] * factor + jnp.dot(
            weights.astype(jnp.bfloat16), kv[:, HD:], preferred_element_type=jnp.float32
        )
        m_sc[...] = new_max

    @pl.when(j == pl.num_programs(1) - 1)
    def _():
        out_ref[...] = (acc_sc[...] / l_sc[...]).astype(out_ref.dtype)


def flash_attend(flags, queries, stacked, key_code, query_low, query_high):
    q_rows = queries.shape[0]
    k_rows = stacked.shape[0]
    grid_spec = pltpu.PrefetchScalarGridSpec(
        num_scalar_prefetch=1,
        grid=(q_rows // Q_TILE, k_rows // K_TILE),
        in_specs=[
            pl.BlockSpec((Q_TILE, HD), lambda i, j, f: (i, 0)),
            pl.BlockSpec((K_TILE, 2 * HD), lambda i, j, f: (j, 0)),
            pl.BlockSpec((1, K_TILE), lambda i, j, f: (0, j)),
            pl.BlockSpec((Q_TILE, 1), lambda i, j, f: (i, 0)),
            pl.BlockSpec((Q_TILE, 1), lambda i, j, f: (i, 0)),
        ],
        out_specs=pl.BlockSpec((Q_TILE, HD), lambda i, j, f: (i, 0)),
        scratch_shapes=[
            pltpu.VMEM((Q_TILE, 1), jnp.float32),
            pltpu.VMEM((Q_TILE, 1), jnp.float32),
            pltpu.VMEM((Q_TILE, HD), jnp.float32),
        ],
    )
    return pl.pallas_call(
        flash_kernel,
        grid_spec=grid_spec,
        out_shape=jax.ShapeDtypeStruct((q_rows, HD), jnp.bfloat16),
        compiler_params=pltpu.CompilerParams(dimension_semantics=("arbitrary", "arbitrary")),
    )(flags, queries, stacked, key_code, query_low, query_high)


def tile_flags(key_code, query_low, query_high):
    seen = (key_code[None, :] >= query_low[:, None]) & (key_code[None, :] <= query_high[:, None])
    return jnp.any(seen.reshape(query_low.shape[0], -1, K_TILE), axis=(0, 2)).astype(jnp.int32)


def attend_model(query_rows, gathered, flags, key_code, query_low, query_high, out_weight):
    tok_rows, kv_local, group_size = query_rows.shape[:3]
    flat_query = jnp.transpose(query_rows, (1, 2, 0, 3)).reshape(-1, HD)
    tiled_low = jnp.tile(query_low, kv_local * group_size)[:, None]
    tiled_high = jnp.tile(query_high, kv_local * group_size)[:, None]
    attended = flash_attend(flags, flat_query, gathered, key_code[None, :], tiled_low, tiled_high)
    attended = jnp.transpose(attended.reshape(kv_local, group_size, tok_rows, HD), (2, 0, 1, 3))
    attended = attended.reshape(tok_rows, -1)
    return jnp.dot(attended, out_weight, preferred_element_type=jnp.float32)


def finish(model_state, out_weight):
    running_max, weight_sum, accumulated = model_state
    attended = accumulated / jnp.transpose(weight_sum, (2, 0, 1))[..., None]
    attended = attended.reshape(accumulated.shape[0], -1).astype(jnp.bfloat16)
    return jnp.dot(attended, out_weight, preferred_element_type=jnp.float32)


def head_terms(final_rows, head_weight, targets, vocab_start):
    logits = jnp.dot(final_rows, head_weight, preferred_element_type=jnp.float32)
    local_max = jnp.max(logits, axis=-1)
    word_ids = vocab_start + jnp.arange(logits.shape[1], dtype=jnp.int32)
    target_logit = jnp.sum(jnp.where(word_ids[None, :] == targets[:, None], logits, 0.0), axis=-1)
    return (logits, local_max, target_logit)


def local(
    policy_hidden,
    reference_hidden,
    targets,
    lengths,
    block_source,
    rollout_prompt,
    rollout_slot,
    policy_input_gain,
    policy_query_weight,
    policy_key_weight,
    policy_value_weight,
    policy_query_gain,
    policy_key_gain,
    policy_out_weight,
    policy_final_gain,
    policy_head,
    policy_prompt_keys,
    policy_prompt_values,
    reference_input_gain,
    reference_query_weight,
    reference_key_weight,
    reference_value_weight,
    reference_query_gain,
    reference_key_gain,
    reference_out_weight,
    reference_final_gain,
    reference_head,
    reference_prompt_keys,
    reference_prompt_values,
):
    tok_rows = policy_hidden.shape[0]
    roll_ids = jnp.arange(lengths.shape[0], dtype=jnp.int32)
    slot_ids = jnp.arange(tok_rows, dtype=jnp.int32)
    packed = jnp.repeat(block_source, BLOCK) * BLOCK + slot_ids % BLOCK
    end_points = jnp.cumsum(lengths)
    rollout = jnp.sum((packed[:, None] >= end_points[None, :]).astype(jnp.int32), axis=1)
    member = rollout[:, None] == roll_ids[None, :]
    position = packed - lookup(member, end_points - lengths)
    query_prompt = lookup(member, rollout_prompt)
    slot_of = lookup(member, rollout_slot)
    length_of = lookup(member, lengths)
    prompt_count = policy_prompt_keys.shape[0]
    prefix_local = policy_prompt_keys.shape[1]
    prompt_rows = prompt_count * prefix_local
    rope_offset = prefix_local * lax.axis_size("seq")
    prompt_ids = jnp.arange(prompt_rows, dtype=jnp.int32) // prefix_local
    seq_count = lax.axis_size("seq")
    shard_rows = tok_rows + prompt_rows
    policy_query, policy_stack = project(
        policy_hidden,
        policy_input_gain,
        policy_query_weight,
        policy_key_weight,
        policy_value_weight,
        policy_query_gain,
        policy_key_gain,
        policy_prompt_keys,
        policy_prompt_values,
        position,
        rope_offset,
    )
    reference_query, reference_stack = project(
        reference_hidden,
        reference_input_gain,
        reference_query_weight,
        reference_key_weight,
        reference_value_weight,
        reference_query_gain,
        reference_key_gain,
        reference_prompt_keys,
        reference_prompt_values,
        position,
        rope_offset,
    )
    pad_rows = prompt_rows
    carrier = jnp.zeros((pad_rows, policy_stack.shape[1]), jnp.bfloat16)
    carrier = carrier.at[0, : block_source.shape[0]].set(block_source.astype(jnp.bfloat16))
    policy_gathered = lax.all_gather(
        jnp.concatenate([policy_stack, carrier], axis=0), "seq", axis=0, tiled=True
    )
    policy_rows = policy_stack.shape[0] + pad_rows
    all_source = (
        policy_gathered.reshape(seq_count, policy_rows, -1)[:, policy_stack.shape[0], : block_source.shape[0]]
        .astype(jnp.int32)
        .reshape(-1)
    )
    all_ids = jnp.arange(tok_rows * seq_count, dtype=jnp.int32)
    all_packed = jnp.repeat(all_source, BLOCK) * BLOCK + all_ids % BLOCK
    all_rollout = jnp.sum((all_packed[:, None] >= end_points[None, :]).astype(jnp.int32), axis=1)
    all_member = all_rollout[:, None] == roll_ids[None, :]
    all_position = all_packed - lookup(all_member, end_points - lengths)
    owner = lookup(rollout_prompt[None, :] == jnp.arange(prompt_count, dtype=jnp.int32)[:, None], roll_ids)
    token_code = (all_rollout * CODE_STRIDE + all_position).reshape(seq_count, tok_rows)
    prompt_code = jnp.broadcast_to(owner[prompt_ids] * CODE_STRIDE - 1, (seq_count, prompt_rows))
    never_code = jnp.full((seq_count, pad_rows), -(1 << 30), jnp.int32)
    key_code = jnp.concatenate([token_code, prompt_code], axis=1).reshape(-1)
    policy_code = jnp.concatenate([token_code, prompt_code, never_code], axis=1).reshape(-1)
    query_low = rollout * CODE_STRIDE - 1
    query_high = rollout * CODE_STRIDE + position
    flags = tile_flags(key_code, query_low, query_high)
    policy_flags = tile_flags(policy_code, query_low, query_high)
    policy_part = attend_model(
        policy_query,
        policy_gathered,
        policy_flags,
        policy_code,
        query_low,
        query_high,
        policy_out_weight,
    )
    reference_part = attend_model(
        reference_query,
        lax.all_gather(reference_stack, "seq", axis=0, tiled=True),
        flags,
        key_code,
        query_low,
        query_high,
        reference_out_weight,
    )
    policy_summed = lax.psum(policy_part.astype(jnp.bfloat16), "vocab")
    policy_summed, reference_part = lax.optimization_barrier((policy_summed, reference_part))
    policy_mixed = policy_summed.astype(jnp.float32)
    reference_mixed = lax.psum(reference_part.astype(jnp.bfloat16), "vocab").astype(jnp.float32)
    policy_final = rms_scale(
        policy_hidden.astype(jnp.float32) + policy_mixed, policy_final_gain
    ).astype(jnp.bfloat16)
    reference_final = rms_scale(
        reference_hidden.astype(jnp.float32) + reference_mixed, reference_final_gain
    ).astype(jnp.bfloat16)
    vocab_start = lax.axis_index("vocab") * policy_head.shape[1]
    policy_logits, policy_max, policy_target = head_terms(
        policy_final, policy_head, targets, vocab_start
    )
    reference_logits, reference_max, reference_target = head_terms(
        reference_final, reference_head, targets, vocab_start
    )
    policy_top, reference_top = lax.pmax((policy_max, reference_max), "vocab")
    policy_local = jnp.sum(jnp.exp(policy_logits - policy_top[:, None]), axis=-1)
    reference_local = jnp.sum(jnp.exp(reference_logits - reference_top[:, None]), axis=-1)
    totals = lax.psum((policy_local, reference_local, policy_target, reference_target), "vocab")
    policy_score = totals[2] - (policy_top + jnp.log(totals[0]))
    reference_score = totals[3] - (reference_top + jnp.log(totals[1]))
    token_diff = policy_score - reference_score
    per_token = token_diff / length_of.astype(jnp.float32)
    partial_sums = jnp.sum(
        jnp.where(slot_of[:, None] == roll_ids[None, :], per_token[:, None], 0.0), axis=0
    )
    rollout_mean = partial_sums
    stride = 1
    while stride < seq_count:
        rollout_mean = rollout_mean + lax.ppermute(
            rollout_mean, "seq", [(i, i ^ stride) for i in range(seq_count)]
        )
        stride *= 2
    return (token_diff, rollout_mean)


def solution(mesh):
    return jax.shard_map(
        local,
        mesh=mesh,
        in_specs=(
            P("seq", None),
            P("seq", None),
            P("seq"),
            P(),
            P("seq"),
            P(),
            P(),
            P(),
            P(None, "vocab"),
            P(None, "vocab"),
            P(None, "vocab"),
            P(),
            P(),
            P("vocab", None),
            P(),
            P(None, "vocab"),
            P(None, "seq", "vocab"),
            P(None, "seq", "vocab"),
            P(),
            P(None, "vocab"),
            P(None, "vocab"),
            P(None, "vocab"),
            P(),
            P(),
            P("vocab", None),
            P(),
            P(None, "vocab"),
            P(None, "seq", "vocab"),
            P(None, "seq", "vocab"),
        ),
        out_specs=(P("seq"), P()),
        check_vma=False,
    )
```

```python
import jax
import jax.numpy as jnp
from jax import lax
from jax.sharding import PartitionSpec as P
from jax.experimental import pallas as pl
from jax.experimental.pallas import tpu as pltpu

HD = 128
BLOCK = 128


EPSILON = 1e-06
ROPE_BASE = 1000000.0
NEGATIVE_FILL = -1e30


def rms_scale(values, gain_row):
    values = values.astype(jnp.float32)
    return (
        values * lax.rsqrt(jnp.mean(values * values, axis=-1, keepdims=True) + EPSILON) * gain_row
    )


def rotate(values, positions):
    half_width = values.shape[-1] // 2
    frequency = ROPE_BASE ** (-2.0 * jnp.arange(half_width, dtype=jnp.float32) / values.shape[-1])
    angles = positions.astype(jnp.float32)[:, None] * frequency[None, :]
    cosine = jnp.cos(angles)
    sine_part = jnp.sin(angles)
    cosine = jnp.concatenate([cosine, cosine], axis=-1)[:, None, :]
    sine_part = jnp.concatenate([sine_part, sine_part], axis=-1)[:, None, :]
    turned = jnp.concatenate([-values[..., half_width:], values[..., :half_width]], axis=-1)
    return values * cosine + turned * sine_part


def lookup(member, lookup_table):
    return jnp.sum(jnp.where(member, lookup_table[None, :], 0), axis=1)


def project(
    hidden,
    input_gain,
    query_weight,
    key_weight,
    value_weight,
    query_gain,
    key_gain,
    prompt_keys,
    prompt_values,
    positions,
    rope_offset,
):
    tok_rows = hidden.shape[0]
    kv_local = key_weight.shape[1] // HD
    normed = rms_scale(hidden, input_gain).astype(jnp.bfloat16)
    query_rows = jnp.dot(normed, query_weight, preferred_element_type=jnp.float32).reshape(
        tok_rows, -1, HD
    )
    query_rows = rotate(rms_scale(query_rows, query_gain), positions + rope_offset).astype(
        jnp.bfloat16
    )
    key_rows = jnp.dot(normed, key_weight, preferred_element_type=jnp.float32).reshape(
        tok_rows, kv_local, HD
    )
    key_rows = (
        rotate(rms_scale(key_rows, key_gain), positions + rope_offset)
        .astype(jnp.bfloat16)
        .reshape(tok_rows, kv_local * HD)
    )
    value_rows = jnp.dot(normed, value_weight, preferred_element_type=jnp.float32).astype(
        jnp.bfloat16
    )
    key_block = jnp.concatenate([key_rows, prompt_keys.reshape(-1, kv_local * HD)], axis=0)
    value_block = jnp.concatenate([value_rows, prompt_values.reshape(-1, kv_local * HD)], axis=0)
    stacked = jnp.concatenate([key_block, value_block], axis=1)
    return (query_rows.reshape(tok_rows, kv_local, -1, HD), stacked)


def empty_state(query_rows):
    tok_rows, kv_local, group_size = (query_rows.shape[0], query_rows.shape[1], query_rows.shape[2])
    running_max = jnp.full((kv_local, group_size, tok_rows), NEGATIVE_FILL, jnp.float32)
    weight_sum = jnp.zeros((kv_local, group_size, tok_rows), jnp.float32)
    accumulated = jnp.zeros((tok_rows, kv_local, group_size, HD), jnp.float32)
    return (running_max, weight_sum, accumulated)


def update_state(model_state, query_rows, stacked, visible):
    running_max, weight_sum, accumulated = model_state
    half_columns = stacked.shape[1] // 2
    kv_local = query_rows.shape[1]
    key_part = stacked[:, :half_columns].reshape(-1, kv_local, HD)
    value_part = stacked[:, half_columns:].reshape(-1, kv_local, HD)
    scores = jnp.einsum(
        "qkgd,skd->kgqs", query_rows, key_part, preferred_element_type=jnp.float32
    ) * HD ** (-0.5)
    masked = jnp.where(visible[None, None], scores, NEGATIVE_FILL)
    new_max = jnp.maximum(running_max, jnp.max(masked, axis=-1))
    weights = jnp.where(visible[None, None], jnp.exp(scores - new_max[..., None]), 0.0)
    factor = jnp.exp(running_max - new_max)
    new_sum = weight_sum * factor + jnp.sum(weights, axis=-1)
    product = jnp.einsum(
        "kgqs,skd->qkgd",
        weights.astype(jnp.bfloat16),
        value_part,
        preferred_element_type=jnp.float32,
    )
    new_accumulated = accumulated * jnp.transpose(factor, (2, 0, 1))[..., None] + product
    return (new_max, new_sum, new_accumulated)


def attend(states, queries, pieces, query_tag, query_position, query_prompt):
    stacked_list = pieces[:-2]
    key_tag = pieces[-2]
    key_position = pieces[-1]
    visible = (key_tag[None, :] == query_tag[:, None]) & (
        key_position[None, :] <= query_position[:, None]
    ) | (key_tag[None, :] == -1 - query_prompt[:, None])

    def compute(current):
        updated = []
        for model_state, query_rows, stacked in zip(current, queries, stacked_list):
            updated.append(update_state(model_state, query_rows, stacked, visible))
        return tuple(updated)

    def unchanged(current):
        return current

    return lax.cond(jnp.any(visible), compute, unchanged, states)


def make_fold(queries, query_tag, query_position, query_prompt, shard_rows):

    def fold_pieces(states, pieces, start_row):
        rows_here = pieces[0].shape[0]
        shard_count = rows_here // shard_rows
        split_pieces = tuple(
            (
                member_piece.reshape((shard_count, shard_rows) + member_piece.shape[1:])
                for member_piece in pieces
            )
        )

        def scan_step(carry_states, piece_item):
            return (
                attend(carry_states, queries, piece_item, query_tag, query_position, query_prompt),
                None,
            )

        return lax.scan(scan_step, states, split_pieces)[0]

    return fold_pieces


Q_TILE = 512
K_TILE = 1024
CODE_STRIDE = 65536


def flash_kernel(flags_ref, q_ref, kv_ref, kcode_ref, qlo_ref, qhi_ref, out_ref, m_sc, l_sc, acc_sc):
    j = pl.program_id(1)

    @pl.when(j == 0)
    def _():
        m_sc[...] = jnp.full(m_sc.shape, NEGATIVE_FILL, jnp.float32)
        l_sc[...] = jnp.zeros(l_sc.shape, jnp.float32)
        acc_sc[...] = jnp.zeros(acc_sc.shape, jnp.float32)

    @pl.when(flags_ref[j] > 0)
    def _():
        kv = kv_ref[...]
        scores = lax.dot_general(
            q_ref[...], kv[:, :HD], (((1,), (1,)), ((), ())), preferred_element_type=jnp.float32
        ) * HD ** (-0.5)
        key_code = kcode_ref[...]
        visible = (key_code >= qlo_ref[...]) & (key_code <= qhi_ref[...])
        masked = jnp.where(visible, scores, NEGATIVE_FILL)
        old_max = m_sc[...]
        new_max = jnp.maximum(old_max, jnp.max(masked, axis=1, keepdims=True))
        weights = jnp.where(visible, jnp.exp(scores - new_max), 0.0)
        factor = jnp.exp(old_max - new_max)
        l_sc[...] = l_sc[...] * factor + jnp.sum(weights, axis=1, keepdims=True)
        acc_sc[...] = acc_sc[...] * factor + jnp.dot(
            weights.astype(jnp.bfloat16), kv[:, HD:], preferred_element_type=jnp.float32
        )
        m_sc[...] = new_max

    @pl.when(j == pl.num_programs(1) - 1)
    def _():
        out_ref[...] = (acc_sc[...] / l_sc[...]).astype(out_ref.dtype)


def flash_attend(flags, queries, stacked, key_code, query_low, query_high):
    q_rows = queries.shape[0]
    k_rows = stacked.shape[0]
    grid_spec = pltpu.PrefetchScalarGridSpec(
        num_scalar_prefetch=1,
        grid=(q_rows // Q_TILE, k_rows // K_TILE),
        in_specs=[
            pl.BlockSpec((Q_TILE, HD), lambda i, j, f: (i, 0)),
            pl.BlockSpec((K_TILE, 2 * HD), lambda i, j, f: (j, 0)),
            pl.BlockSpec((1, K_TILE), lambda i, j, f: (0, j)),
            pl.BlockSpec((Q_TILE, 1), lambda i, j, f: (i, 0)),
            pl.BlockSpec((Q_TILE, 1), lambda i, j, f: (i, 0)),
        ],
        out_specs=pl.BlockSpec((Q_TILE, HD), lambda i, j, f: (i, 0)),
        scratch_shapes=[
            pltpu.VMEM((Q_TILE, 1), jnp.float32),
            pltpu.VMEM((Q_TILE, 1), jnp.float32),
            pltpu.VMEM((Q_TILE, HD), jnp.float32),
        ],
    )
    return pl.pallas_call(
        flash_kernel,
        grid_spec=grid_spec,
        out_shape=jax.ShapeDtypeStruct((q_rows, HD), jnp.bfloat16),
        compiler_params=pltpu.CompilerParams(dimension_semantics=("arbitrary", "arbitrary")),
    )(flags, queries, stacked, key_code, query_low, query_high)


def doubling_gather(block, axis_name):
    count = lax.axis_size(axis_name)
    gathered = block
    stride = 1
    while stride < count:
        received = lax.ppermute(gathered, axis_name, [(i, i ^ stride) for i in range(count)])
        upper = (lax.axis_index(axis_name) // stride) % 2 == 1
        gathered = jnp.concatenate(
            [jnp.where(upper, received, gathered), jnp.where(upper, gathered, received)], axis=0
        )
        stride *= 2
    return gathered


def tile_flags(key_code, query_low, query_high):
    seen = (key_code[None, :] >= query_low[:, None]) & (key_code[None, :] <= query_high[:, None])
    return jnp.any(seen.reshape(query_low.shape[0], -1, K_TILE), axis=(0, 2)).astype(jnp.int32)


def attend_model(query_rows, gathered, flags, key_code, query_low, query_high, out_weight):
    tok_rows, kv_local, group_size = query_rows.shape[:3]
    flat_query = jnp.transpose(query_rows, (1, 2, 0, 3)).reshape(-1, HD)
    tiled_low = jnp.tile(query_low, kv_local * group_size)[:, None]
    tiled_high = jnp.tile(query_high, kv_local * group_size)[:, None]
    attended = flash_attend(flags, flat_query, gathered, key_code[None, :], tiled_low, tiled_high)
    attended = jnp.transpose(attended.reshape(kv_local, group_size, tok_rows, HD), (2, 0, 1, 3))
    attended = attended.reshape(tok_rows, -1)
    return jnp.dot(attended, out_weight, preferred_element_type=jnp.float32)


def finish(model_state, out_weight):
    running_max, weight_sum, accumulated = model_state
    attended = accumulated / jnp.transpose(weight_sum, (2, 0, 1))[..., None]
    attended = attended.reshape(accumulated.shape[0], -1).astype(jnp.bfloat16)
    return jnp.dot(attended, out_weight, preferred_element_type=jnp.float32)


def head_terms(final_rows, head_weight, targets, vocab_start):
    logits = jnp.dot(final_rows, head_weight, preferred_element_type=jnp.float32)
    local_max = jnp.max(logits, axis=-1)
    word_ids = vocab_start + jnp.arange(logits.shape[1], dtype=jnp.int32)
    target_logit = jnp.sum(jnp.where(word_ids[None, :] == targets[:, None], logits, 0.0), axis=-1)
    return (logits, local_max, target_logit)


def local(
    policy_hidden,
    reference_hidden,
    targets,
    lengths,
    block_source,
    rollout_prompt,
    rollout_slot,
    policy_input_gain,
    policy_query_weight,
    policy_key_weight,
    policy_value_weight,
    policy_query_gain,
    policy_key_gain,
    policy_out_weight,
    policy_final_gain,
    policy_head,
    policy_prompt_keys,
    policy_prompt_values,
    reference_input_gain,
    reference_query_weight,
    reference_key_weight,
    reference_value_weight,
    reference_query_gain,
    reference_key_gain,
    reference_out_weight,
    reference_final_gain,
    reference_head,
    reference_prompt_keys,
    reference_prompt_values,
):
    tok_rows = policy_hidden.shape[0]
    roll_ids = jnp.arange(lengths.shape[0], dtype=jnp.int32)
    slot_ids = jnp.arange(tok_rows, dtype=jnp.int32)
    packed = jnp.repeat(block_source, BLOCK) * BLOCK + slot_ids % BLOCK
    end_points = jnp.cumsum(lengths)
    rollout = jnp.sum((packed[:, None] >= end_points[None, :]).astype(jnp.int32), axis=1)
    member = rollout[:, None] == roll_ids[None, :]
    position = packed - lookup(member, end_points - lengths)
    query_prompt = lookup(member, rollout_prompt)
    slot_of = lookup(member, rollout_slot)
    length_of = lookup(member, lengths)
    prompt_count = policy_prompt_keys.shape[0]
    prefix_local = policy_prompt_keys.shape[1]
    prompt_rows = prompt_count * prefix_local
    rope_offset = prefix_local * lax.axis_size("seq")
    prompt_ids = jnp.arange(prompt_rows, dtype=jnp.int32) // prefix_local
    seq_count = lax.axis_size("seq")
    shard_rows = tok_rows + prompt_rows
    policy_query, policy_stack = project(
        policy_hidden,
        policy_input_gain,
        policy_query_weight,
        policy_key_weight,
        policy_value_weight,
        policy_query_gain,
        policy_key_gain,
        policy_prompt_keys,
        policy_prompt_values,
        position,
        rope_offset,
    )
    reference_query, reference_stack = project(
        reference_hidden,
        reference_input_gain,
        reference_query_weight,
        reference_key_weight,
        reference_value_weight,
        reference_query_gain,
        reference_key_gain,
        reference_prompt_keys,
        reference_prompt_values,
        position,
        rope_offset,
    )
    pad_rows = prompt_rows
    carrier = jnp.zeros((pad_rows, policy_stack.shape[1]), jnp.bfloat16)
    carrier = carrier.at[0, : block_source.shape[0]].set(block_source.astype(jnp.bfloat16))
    policy_gathered = lax.all_gather(
        jnp.concatenate([policy_stack, carrier], axis=0), "seq", axis=0, tiled=True
    )
    policy_rows = policy_stack.shape[0] + pad_rows
    all_source = (
        policy_gathered.reshape(seq_count, policy_rows, -1)[:, policy_stack.shape[0], : block_source.shape[0]]
        .astype(jnp.int32)
        .reshape(-1)
    )
    all_ids = jnp.arange(tok_rows * seq_count, dtype=jnp.int32)
    all_packed = jnp.repeat(all_source, BLOCK) * BLOCK + all_ids % BLOCK
    all_rollout = jnp.sum((all_packed[:, None] >= end_points[None, :]).astype(jnp.int32), axis=1)
    all_member = all_rollout[:, None] == roll_ids[None, :]
    all_position = all_packed - lookup(all_member, end_points - lengths)
    owner = lookup(rollout_prompt[None, :] == jnp.arange(prompt_count, dtype=jnp.int32)[:, None], roll_ids)
    token_code = (all_rollout * CODE_STRIDE + all_position).reshape(seq_count, tok_rows)
    prompt_code = jnp.broadcast_to(owner[prompt_ids] * CODE_STRIDE - 1, (seq_count, prompt_rows))
    never_code = jnp.full((seq_count, pad_rows), -(1 << 30), jnp.int32)
    key_code = jnp.concatenate([token_code, prompt_code], axis=1).reshape(-1)
    policy_code = jnp.concatenate([token_code, prompt_code, never_code], axis=1).reshape(-1)
    query_low = rollout * CODE_STRIDE - 1
    query_high = rollout * CODE_STRIDE + position
    flags = tile_flags(key_code, query_low, query_high)
    policy_flags = tile_flags(policy_code, query_low, query_high)
    policy_part = attend_model(
        policy_query,
        policy_gathered,
        policy_flags,
        policy_code,
        query_low,
        query_high,
        policy_out_weight,
    )
    reference_part = attend_model(
        reference_query,
        doubling_gather(reference_stack, "seq"),
        flags,
        key_code,
        query_low,
        query_high,
        reference_out_weight,
    )
    policy_summed = lax.psum(policy_part.astype(jnp.bfloat16), "vocab")
    policy_summed, reference_part = lax.optimization_barrier((policy_summed, reference_part))
    policy_mixed = policy_summed.astype(jnp.float32)
    reference_mixed = lax.psum(reference_part.astype(jnp.bfloat16), "vocab").astype(jnp.float32)
    policy_final = rms_scale(
        policy_hidden.astype(jnp.float32) + policy_mixed, policy_final_gain
    ).astype(jnp.bfloat16)
    reference_final = rms_scale(
        reference_hidden.astype(jnp.float32) + reference_mixed, reference_final_gain
    ).astype(jnp.bfloat16)
    vocab_start = lax.axis_index("vocab") * policy_head.shape[1]
    policy_logits, policy_max, policy_target = head_terms(
        policy_final, policy_head, targets, vocab_start
    )
    reference_logits, reference_max, reference_target = head_terms(
        reference_final, reference_head, targets, vocab_start
    )
    policy_top, reference_top = lax.pmax((policy_max, reference_max), "vocab")
    policy_local = jnp.sum(jnp.exp(policy_logits - policy_top[:, None]), axis=-1)
    reference_local = jnp.sum(jnp.exp(reference_logits - reference_top[:, None]), axis=-1)
    totals = lax.psum((policy_local, reference_local, policy_target, reference_target), "vocab")
    policy_score = totals[2] - (policy_top + jnp.log(totals[0]))
    reference_score = totals[3] - (reference_top + jnp.log(totals[1]))
    token_diff = policy_score - reference_score
    per_token = token_diff / length_of.astype(jnp.float32)
    partial_sums = jnp.sum(
        jnp.where(slot_of[:, None] == roll_ids[None, :], per_token[:, None], 0.0), axis=0
    )
    rollout_mean = partial_sums
    stride = 1
    while stride < seq_count:
        rollout_mean = rollout_mean + lax.ppermute(
            rollout_mean, "seq", [(i, i ^ stride) for i in range(seq_count)]
        )
        stride *= 2
    return (token_diff, rollout_mean)


def solution(mesh):
    return jax.shard_map(
        local,
        mesh=mesh,
        in_specs=(
            P("seq", None),
            P("seq", None),
            P("seq"),
            P(),
            P("seq"),
            P(),
            P(),
            P(),
            P(None, "vocab"),
            P(None, "vocab"),
            P(None, "vocab"),
            P(),
            P(),
            P("vocab", None),
            P(),
            P(None, "vocab"),
            P(None, "seq", "vocab"),
            P(None, "seq", "vocab"),
            P(),
            P(None, "vocab"),
            P(None, "vocab"),
            P(None, "vocab"),
            P(),
            P(),
            P("vocab", None),
            P(),
            P(None, "vocab"),
            P(None, "seq", "vocab"),
            P(None, "seq", "vocab"),
        ),
        out_specs=(P("seq"), P()),
        check_vma=False,
    )
```

```python
import jax
import jax.numpy as jnp
from jax import lax
from jax.sharding import PartitionSpec as P
from jax.experimental import pallas as pl
from jax.experimental.pallas import tpu as pltpu

HD = 128
BLOCK = 128


EPSILON = 1e-06
ROPE_BASE = 1000000.0
NEGATIVE_FILL = -1e30


def rms_scale(values, gain_row):
    values = values.astype(jnp.float32)
    return (
        values * lax.rsqrt(jnp.mean(values * values, axis=-1, keepdims=True) + EPSILON) * gain_row
    )


def rotate(values, positions):
    half_width = values.shape[-1] // 2
    frequency = ROPE_BASE ** (-2.0 * jnp.arange(half_width, dtype=jnp.float32) / values.shape[-1])
    angles = positions.astype(jnp.float32)[:, None] * frequency[None, :]
    cosine = jnp.cos(angles)
    sine_part = jnp.sin(angles)
    cosine = jnp.concatenate([cosine, cosine], axis=-1)[:, None, :]
    sine_part = jnp.concatenate([sine_part, sine_part], axis=-1)[:, None, :]
    turned = jnp.concatenate([-values[..., half_width:], values[..., :half_width]], axis=-1)
    return values * cosine + turned * sine_part


def lookup(member, lookup_table):
    return jnp.sum(jnp.where(member, lookup_table[None, :], 0), axis=1)


def project(
    hidden,
    input_gain,
    query_weight,
    key_weight,
    value_weight,
    query_gain,
    key_gain,
    prompt_keys,
    prompt_values,
    positions,
    rope_offset,
):
    tok_rows = hidden.shape[0]
    kv_local = key_weight.shape[1] // HD
    normed = rms_scale(hidden, input_gain).astype(jnp.bfloat16)
    query_rows = jnp.dot(normed, query_weight, preferred_element_type=jnp.float32).reshape(
        tok_rows, -1, HD
    )
    query_rows = rotate(rms_scale(query_rows, query_gain), positions + rope_offset).astype(
        jnp.bfloat16
    )
    key_rows = jnp.dot(normed, key_weight, preferred_element_type=jnp.float32).reshape(
        tok_rows, kv_local, HD
    )
    key_rows = (
        rotate(rms_scale(key_rows, key_gain), positions + rope_offset)
        .astype(jnp.bfloat16)
        .reshape(tok_rows, kv_local * HD)
    )
    value_rows = jnp.dot(normed, value_weight, preferred_element_type=jnp.float32).astype(
        jnp.bfloat16
    )
    key_block = jnp.concatenate([key_rows, prompt_keys.reshape(-1, kv_local * HD)], axis=0)
    value_block = jnp.concatenate([value_rows, prompt_values.reshape(-1, kv_local * HD)], axis=0)
    stacked = jnp.concatenate([key_block, value_block], axis=1)
    return (query_rows.reshape(tok_rows, kv_local, -1, HD), stacked)


def empty_state(query_rows):
    tok_rows, kv_local, group_size = (query_rows.shape[0], query_rows.shape[1], query_rows.shape[2])
    running_max = jnp.full((kv_local, group_size, tok_rows), NEGATIVE_FILL, jnp.float32)
    weight_sum = jnp.zeros((kv_local, group_size, tok_rows), jnp.float32)
    accumulated = jnp.zeros((tok_rows, kv_local, group_size, HD), jnp.float32)
    return (running_max, weight_sum, accumulated)


def update_state(model_state, query_rows, stacked, visible):
    running_max, weight_sum, accumulated = model_state
    half_columns = stacked.shape[1] // 2
    kv_local = query_rows.shape[1]
    key_part = stacked[:, :half_columns].reshape(-1, kv_local, HD)
    value_part = stacked[:, half_columns:].reshape(-1, kv_local, HD)
    scores = jnp.einsum(
        "qkgd,skd->kgqs", query_rows, key_part, preferred_element_type=jnp.float32
    ) * HD ** (-0.5)
    masked = jnp.where(visible[None, None], scores, NEGATIVE_FILL)
    new_max = jnp.maximum(running_max, jnp.max(masked, axis=-1))
    weights = jnp.where(visible[None, None], jnp.exp(scores - new_max[..., None]), 0.0)
    factor = jnp.exp(running_max - new_max)
    new_sum = weight_sum * factor + jnp.sum(weights, axis=-1)
    product = jnp.einsum(
        "kgqs,skd->qkgd",
        weights.astype(jnp.bfloat16),
        value_part,
        preferred_element_type=jnp.float32,
    )
    new_accumulated = accumulated * jnp.transpose(factor, (2, 0, 1))[..., None] + product
    return (new_max, new_sum, new_accumulated)


def attend(states, queries, pieces, query_tag, query_position, query_prompt):
    stacked_list = pieces[:-2]
    key_tag = pieces[-2]
    key_position = pieces[-1]
    visible = (key_tag[None, :] == query_tag[:, None]) & (
        key_position[None, :] <= query_position[:, None]
    ) | (key_tag[None, :] == -1 - query_prompt[:, None])

    def compute(current):
        updated = []
        for model_state, query_rows, stacked in zip(current, queries, stacked_list):
            updated.append(update_state(model_state, query_rows, stacked, visible))
        return tuple(updated)

    def unchanged(current):
        return current

    return lax.cond(jnp.any(visible), compute, unchanged, states)


def make_fold(queries, query_tag, query_position, query_prompt, shard_rows):

    def fold_pieces(states, pieces, start_row):
        rows_here = pieces[0].shape[0]
        shard_count = rows_here // shard_rows
        split_pieces = tuple(
            (
                member_piece.reshape((shard_count, shard_rows) + member_piece.shape[1:])
                for member_piece in pieces
            )
        )

        def scan_step(carry_states, piece_item):
            return (
                attend(carry_states, queries, piece_item, query_tag, query_position, query_prompt),
                None,
            )

        return lax.scan(scan_step, states, split_pieces)[0]

    return fold_pieces


Q_TILE = 512
K_TILE = 1024
CODE_STRIDE = 65536


def flash_kernel(flags_ref, q_ref, kv_ref, kcode_ref, qlo_ref, qhi_ref, out_ref, m_sc, l_sc, acc_sc):
    j = pl.program_id(1)

    @pl.when(j == 0)
    def _():
        m_sc[...] = jnp.full(m_sc.shape, NEGATIVE_FILL, jnp.float32)
        l_sc[...] = jnp.zeros(l_sc.shape, jnp.float32)
        acc_sc[...] = jnp.zeros(acc_sc.shape, jnp.float32)

    @pl.when(flags_ref[j] > 0)
    def _():
        kv = kv_ref[...]
        scores = lax.dot_general(
            q_ref[...], kv[:, :HD], (((1,), (1,)), ((), ())), preferred_element_type=jnp.float32
        ) * HD ** (-0.5)
        key_code = kcode_ref[...]
        visible = (key_code >= qlo_ref[...]) & (key_code <= qhi_ref[...])
        masked = jnp.where(visible, scores, NEGATIVE_FILL)
        old_max = m_sc[...]
        new_max = jnp.maximum(old_max, jnp.max(masked, axis=1, keepdims=True))
        weights = jnp.where(visible, jnp.exp(scores - new_max), 0.0)
        factor = jnp.exp(old_max - new_max)
        l_sc[...] = l_sc[...] * factor + jnp.sum(weights, axis=1, keepdims=True)
        acc_sc[...] = acc_sc[...] * factor + jnp.dot(
            weights.astype(jnp.bfloat16), kv[:, HD:], preferred_element_type=jnp.float32
        )
        m_sc[...] = new_max

    @pl.when(j == pl.num_programs(1) - 1)
    def _():
        out_ref[...] = (acc_sc[...] / l_sc[...]).astype(out_ref.dtype)


def flash_attend(flags, queries, stacked, key_code, query_low, query_high):
    q_rows = queries.shape[0]
    k_rows = stacked.shape[0]
    grid_spec = pltpu.PrefetchScalarGridSpec(
        num_scalar_prefetch=1,
        grid=(q_rows // Q_TILE, k_rows // K_TILE),
        in_specs=[
            pl.BlockSpec((Q_TILE, HD), lambda i, j, f: (i, 0)),
            pl.BlockSpec((K_TILE, 2 * HD), lambda i, j, f: (j, 0)),
            pl.BlockSpec((1, K_TILE), lambda i, j, f: (0, j)),
            pl.BlockSpec((Q_TILE, 1), lambda i, j, f: (i, 0)),
            pl.BlockSpec((Q_TILE, 1), lambda i, j, f: (i, 0)),
        ],
        out_specs=pl.BlockSpec((Q_TILE, HD), lambda i, j, f: (i, 0)),
        scratch_shapes=[
            pltpu.VMEM((Q_TILE, 1), jnp.float32),
            pltpu.VMEM((Q_TILE, 1), jnp.float32),
            pltpu.VMEM((Q_TILE, HD), jnp.float32),
        ],
    )
    return pl.pallas_call(
        flash_kernel,
        grid_spec=grid_spec,
        out_shape=jax.ShapeDtypeStruct((q_rows, HD), jnp.bfloat16),
        compiler_params=pltpu.CompilerParams(dimension_semantics=("arbitrary", "arbitrary")),
    )(flags, queries, stacked, key_code, query_low, query_high)


def exchange_sum(values, axis_name):
    count = lax.axis_size(axis_name)
    stride = 1
    while stride < count:
        received = lax.ppermute(values, axis_name, [(i, i ^ stride) for i in range(count)])
        values = (values.astype(jnp.float32) + received.astype(jnp.float32)).astype(values.dtype)
        stride *= 2
    return values


def tile_flags(key_code, query_low, query_high):
    seen = (key_code[None, :] >= query_low[:, None]) & (key_code[None, :] <= query_high[:, None])
    return jnp.any(seen.reshape(query_low.shape[0], -1, K_TILE), axis=(0, 2)).astype(jnp.int32)


def attend_model(query_rows, gathered, flags, key_code, query_low, query_high, out_weight):
    tok_rows, kv_local, group_size = query_rows.shape[:3]
    flat_query = jnp.transpose(query_rows, (1, 2, 0, 3)).reshape(-1, HD)
    tiled_low = jnp.tile(query_low, kv_local * group_size)[:, None]
    tiled_high = jnp.tile(query_high, kv_local * group_size)[:, None]
    attended = flash_attend(flags, flat_query, gathered, key_code[None, :], tiled_low, tiled_high)
    attended = jnp.transpose(attended.reshape(kv_local, group_size, tok_rows, HD), (2, 0, 1, 3))
    attended = attended.reshape(tok_rows, -1)
    return jnp.dot(attended, out_weight, preferred_element_type=jnp.float32)


def finish(model_state, out_weight):
    running_max, weight_sum, accumulated = model_state
    attended = accumulated / jnp.transpose(weight_sum, (2, 0, 1))[..., None]
    attended = attended.reshape(accumulated.shape[0], -1).astype(jnp.bfloat16)
    return jnp.dot(attended, out_weight, preferred_element_type=jnp.float32)


def head_terms(final_rows, head_weight, targets, vocab_start):
    logits = jnp.dot(final_rows, head_weight, preferred_element_type=jnp.float32)
    local_max = jnp.max(logits, axis=-1)
    word_ids = vocab_start + jnp.arange(logits.shape[1], dtype=jnp.int32)
    target_logit = jnp.sum(jnp.where(word_ids[None, :] == targets[:, None], logits, 0.0), axis=-1)
    return (logits, local_max, target_logit)


def local(
    policy_hidden,
    reference_hidden,
    targets,
    lengths,
    block_source,
    rollout_prompt,
    rollout_slot,
    policy_input_gain,
    policy_query_weight,
    policy_key_weight,
    policy_value_weight,
    policy_query_gain,
    policy_key_gain,
    policy_out_weight,
    policy_final_gain,
    policy_head,
    policy_prompt_keys,
    policy_prompt_values,
    reference_input_gain,
    reference_query_weight,
    reference_key_weight,
    reference_value_weight,
    reference_query_gain,
    reference_key_gain,
    reference_out_weight,
    reference_final_gain,
    reference_head,
    reference_prompt_keys,
    reference_prompt_values,
):
    tok_rows = policy_hidden.shape[0]
    roll_ids = jnp.arange(lengths.shape[0], dtype=jnp.int32)
    slot_ids = jnp.arange(tok_rows, dtype=jnp.int32)
    packed = jnp.repeat(block_source, BLOCK) * BLOCK + slot_ids % BLOCK
    end_points = jnp.cumsum(lengths)
    rollout = jnp.sum((packed[:, None] >= end_points[None, :]).astype(jnp.int32), axis=1)
    member = rollout[:, None] == roll_ids[None, :]
    position = packed - lookup(member, end_points - lengths)
    query_prompt = lookup(member, rollout_prompt)
    slot_of = lookup(member, rollout_slot)
    length_of = lookup(member, lengths)
    prompt_count = policy_prompt_keys.shape[0]
    prefix_local = policy_prompt_keys.shape[1]
    prompt_rows = prompt_count * prefix_local
    rope_offset = prefix_local * lax.axis_size("seq")
    prompt_ids = jnp.arange(prompt_rows, dtype=jnp.int32) // prefix_local
    seq_count = lax.axis_size("seq")
    shard_rows = tok_rows + prompt_rows
    policy_query, policy_stack = project(
        policy_hidden,
        policy_input_gain,
        policy_query_weight,
        policy_key_weight,
        policy_value_weight,
        policy_query_gain,
        policy_key_gain,
        policy_prompt_keys,
        policy_prompt_values,
        position,
        rope_offset,
    )
    reference_query, reference_stack = project(
        reference_hidden,
        reference_input_gain,
        reference_query_weight,
        reference_key_weight,
        reference_value_weight,
        reference_query_gain,
        reference_key_gain,
        reference_prompt_keys,
        reference_prompt_values,
        position,
        rope_offset,
    )
    pad_rows = prompt_rows
    carrier = jnp.zeros((pad_rows, policy_stack.shape[1]), jnp.bfloat16)
    carrier = carrier.at[0, : block_source.shape[0]].set(block_source.astype(jnp.bfloat16))
    policy_gathered = lax.all_gather(
        jnp.concatenate([policy_stack, carrier], axis=0), "seq", axis=0, tiled=True
    )
    policy_rows = policy_stack.shape[0] + pad_rows
    all_source = (
        policy_gathered.reshape(seq_count, policy_rows, -1)[:, policy_stack.shape[0], : block_source.shape[0]]
        .astype(jnp.int32)
        .reshape(-1)
    )
    all_ids = jnp.arange(tok_rows * seq_count, dtype=jnp.int32)
    all_packed = jnp.repeat(all_source, BLOCK) * BLOCK + all_ids % BLOCK
    all_rollout = jnp.sum((all_packed[:, None] >= end_points[None, :]).astype(jnp.int32), axis=1)
    all_member = all_rollout[:, None] == roll_ids[None, :]
    all_position = all_packed - lookup(all_member, end_points - lengths)
    owner = lookup(rollout_prompt[None, :] == jnp.arange(prompt_count, dtype=jnp.int32)[:, None], roll_ids)
    token_code = (all_rollout * CODE_STRIDE + all_position).reshape(seq_count, tok_rows)
    prompt_code = jnp.broadcast_to(owner[prompt_ids] * CODE_STRIDE - 1, (seq_count, prompt_rows))
    never_code = jnp.full((seq_count, pad_rows), -(1 << 30), jnp.int32)
    key_code = jnp.concatenate([token_code, prompt_code], axis=1).reshape(-1)
    policy_code = jnp.concatenate([token_code, prompt_code, never_code], axis=1).reshape(-1)
    query_low = rollout * CODE_STRIDE - 1
    query_high = rollout * CODE_STRIDE + position
    flags = tile_flags(key_code, query_low, query_high)
    policy_flags = tile_flags(policy_code, query_low, query_high)
    policy_part = attend_model(
        policy_query,
        policy_gathered,
        policy_flags,
        policy_code,
        query_low,
        query_high,
        policy_out_weight,
    )
    reference_part = attend_model(
        reference_query,
        lax.all_gather(reference_stack, "seq", axis=0, tiled=True),
        flags,
        key_code,
        query_low,
        query_high,
        reference_out_weight,
    )
    policy_summed = lax.psum(policy_part.astype(jnp.bfloat16), "vocab")
    policy_summed, reference_part = lax.optimization_barrier((policy_summed, reference_part))
    policy_mixed = policy_summed.astype(jnp.float32)
    reference_mixed = exchange_sum(reference_part.astype(jnp.bfloat16), "vocab").astype(jnp.float32)
    policy_final = rms_scale(
        policy_hidden.astype(jnp.float32) + policy_mixed, policy_final_gain
    ).astype(jnp.bfloat16)
    reference_final = rms_scale(
        reference_hidden.astype(jnp.float32) + reference_mixed, reference_final_gain
    ).astype(jnp.bfloat16)
    vocab_start = lax.axis_index("vocab") * policy_head.shape[1]
    policy_logits, policy_max, policy_target = head_terms(
        policy_final, policy_head, targets, vocab_start
    )
    reference_logits, reference_max, reference_target = head_terms(
        reference_final, reference_head, targets, vocab_start
    )
    policy_top, reference_top = lax.pmax((policy_max, reference_max), "vocab")
    policy_local = jnp.sum(jnp.exp(policy_logits - policy_top[:, None]), axis=-1)
    reference_local = jnp.sum(jnp.exp(reference_logits - reference_top[:, None]), axis=-1)
    totals = lax.psum((policy_local, reference_local, policy_target, reference_target), "vocab")
    policy_score = totals[2] - (policy_top + jnp.log(totals[0]))
    reference_score = totals[3] - (reference_top + jnp.log(totals[1]))
    token_diff = policy_score - reference_score
    per_token = token_diff / length_of.astype(jnp.float32)
    partial_sums = jnp.sum(
        jnp.where(slot_of[:, None] == roll_ids[None, :], per_token[:, None], 0.0), axis=0
    )
    rollout_mean = partial_sums
    stride = 1
    while stride < seq_count:
        rollout_mean = rollout_mean + lax.ppermute(
            rollout_mean, "seq", [(i, i ^ stride) for i in range(seq_count)]
        )
        stride *= 2
    return (token_diff, rollout_mean)


def solution(mesh):
    return jax.shard_map(
        local,
        mesh=mesh,
        in_specs=(
            P("seq", None),
            P("seq", None),
            P("seq"),
            P(),
            P("seq"),
            P(),
            P(),
            P(),
            P(None, "vocab"),
            P(None, "vocab"),
            P(None, "vocab"),
            P(),
            P(),
            P("vocab", None),
            P(),
            P(None, "vocab"),
            P(None, "seq", "vocab"),
            P(None, "seq", "vocab"),
            P(),
            P(None, "vocab"),
            P(None, "vocab"),
            P(None, "vocab"),
            P(),
            P(),
            P("vocab", None),
            P(),
            P(None, "vocab"),
            P(None, "seq", "vocab"),
            P(None, "seq", "vocab"),
        ),
        out_specs=(P("seq"), P()),
        check_vma=False,
    )
```

```python
import jax
import jax.numpy as jnp
from jax import lax
from jax.sharding import PartitionSpec as P
from jax.experimental import pallas as pl
from jax.experimental.pallas import tpu as pltpu

HD = 128
BLOCK = 128


EPSILON = 1e-06
ROPE_BASE = 1000000.0
NEGATIVE_FILL = -1e30


def rms_scale(values, gain_row):
    values = values.astype(jnp.float32)
    return (
        values * lax.rsqrt(jnp.mean(values * values, axis=-1, keepdims=True) + EPSILON) * gain_row
    )


def rotate(values, positions):
    half_width = values.shape[-1] // 2
    frequency = ROPE_BASE ** (-2.0 * jnp.arange(half_width, dtype=jnp.float32) / values.shape[-1])
    angles = positions.astype(jnp.float32)[:, None] * frequency[None, :]
    cosine = jnp.cos(angles)
    sine_part = jnp.sin(angles)
    cosine = jnp.concatenate([cosine, cosine], axis=-1)[:, None, :]
    sine_part = jnp.concatenate([sine_part, sine_part], axis=-1)[:, None, :]
    turned = jnp.concatenate([-values[..., half_width:], values[..., :half_width]], axis=-1)
    return values * cosine + turned * sine_part


def lookup(member, lookup_table):
    return jnp.sum(jnp.where(member, lookup_table[None, :], 0), axis=1)


def project(
    hidden,
    input_gain,
    query_weight,
    key_weight,
    value_weight,
    query_gain,
    key_gain,
    prompt_keys,
    prompt_values,
    positions,
    rope_offset,
):
    tok_rows = hidden.shape[0]
    kv_local = key_weight.shape[1] // HD
    normed = rms_scale(hidden, input_gain).astype(jnp.bfloat16)
    query_rows = jnp.dot(normed, query_weight, preferred_element_type=jnp.float32).reshape(
        tok_rows, -1, HD
    )
    query_rows = rotate(rms_scale(query_rows, query_gain), positions + rope_offset).astype(
        jnp.bfloat16
    )
    key_rows = jnp.dot(normed, key_weight, preferred_element_type=jnp.float32).reshape(
        tok_rows, kv_local, HD
    )
    key_rows = (
        rotate(rms_scale(key_rows, key_gain), positions + rope_offset)
        .astype(jnp.bfloat16)
        .reshape(tok_rows, kv_local * HD)
    )
    value_rows = jnp.dot(normed, value_weight, preferred_element_type=jnp.float32).astype(
        jnp.bfloat16
    )
    key_block = jnp.concatenate([key_rows, prompt_keys.reshape(-1, kv_local * HD)], axis=0)
    value_block = jnp.concatenate([value_rows, prompt_values.reshape(-1, kv_local * HD)], axis=0)
    stacked = jnp.concatenate([key_block, value_block], axis=1)
    return (query_rows.reshape(tok_rows, kv_local, -1, HD), stacked)


def empty_state(query_rows):
    tok_rows, kv_local, group_size = (query_rows.shape[0], query_rows.shape[1], query_rows.shape[2])
    running_max = jnp.full((kv_local, group_size, tok_rows), NEGATIVE_FILL, jnp.float32)
    weight_sum = jnp.zeros((kv_local, group_size, tok_rows), jnp.float32)
    accumulated = jnp.zeros((tok_rows, kv_local, group_size, HD), jnp.float32)
    return (running_max, weight_sum, accumulated)


def update_state(model_state, query_rows, stacked, visible):
    running_max, weight_sum, accumulated = model_state
    half_columns = stacked.shape[1] // 2
    kv_local = query_rows.shape[1]
    key_part = stacked[:, :half_columns].reshape(-1, kv_local, HD)
    value_part = stacked[:, half_columns:].reshape(-1, kv_local, HD)
    scores = jnp.einsum(
        "qkgd,skd->kgqs", query_rows, key_part, preferred_element_type=jnp.float32
    ) * HD ** (-0.5)
    masked = jnp.where(visible[None, None], scores, NEGATIVE_FILL)
    new_max = jnp.maximum(running_max, jnp.max(masked, axis=-1))
    weights = jnp.where(visible[None, None], jnp.exp(scores - new_max[..., None]), 0.0)
    factor = jnp.exp(running_max - new_max)
    new_sum = weight_sum * factor + jnp.sum(weights, axis=-1)
    product = jnp.einsum(
        "kgqs,skd->qkgd",
        weights.astype(jnp.bfloat16),
        value_part,
        preferred_element_type=jnp.float32,
    )
    new_accumulated = accumulated * jnp.transpose(factor, (2, 0, 1))[..., None] + product
    return (new_max, new_sum, new_accumulated)


def attend(states, queries, pieces, query_tag, query_position, query_prompt):
    stacked_list = pieces[:-2]
    key_tag = pieces[-2]
    key_position = pieces[-1]
    visible = (key_tag[None, :] == query_tag[:, None]) & (
        key_position[None, :] <= query_position[:, None]
    ) | (key_tag[None, :] == -1 - query_prompt[:, None])

    def compute(current):
        updated = []
        for model_state, query_rows, stacked in zip(current, queries, stacked_list):
            updated.append(update_state(model_state, query_rows, stacked, visible))
        return tuple(updated)

    def unchanged(current):
        return current

    return lax.cond(jnp.any(visible), compute, unchanged, states)


def make_fold(queries, query_tag, query_position, query_prompt, shard_rows):

    def fold_pieces(states, pieces, start_row):
        rows_here = pieces[0].shape[0]
        shard_count = rows_here // shard_rows
        split_pieces = tuple(
            (
                member_piece.reshape((shard_count, shard_rows) + member_piece.shape[1:])
                for member_piece in pieces
            )
        )

        def scan_step(carry_states, piece_item):
            return (
                attend(carry_states, queries, piece_item, query_tag, query_position, query_prompt),
                None,
            )

        return lax.scan(scan_step, states, split_pieces)[0]

    return fold_pieces


Q_TILE = 1024
K_TILE = 512
CODE_STRIDE = 65536


def flash_kernel(flags_ref, q_ref, kv_ref, kcode_ref, qlo_ref, qhi_ref, out_ref, m_sc, l_sc, acc_sc):
    j = pl.program_id(1)
    heads, tokens = m_sc.shape[0], m_sc.shape[1]

    @pl.when(j == 0)
    def _():
        m_sc[...] = jnp.full(m_sc.shape, NEGATIVE_FILL, jnp.float32)
        l_sc[...] = jnp.zeros(l_sc.shape, jnp.float32)
        acc_sc[...] = jnp.zeros(acc_sc.shape, jnp.float32)

    @pl.when(flags_ref[j] > 0)
    def _():
        kv = kv_ref[...]
        scores = lax.dot_general(
            q_ref[...], kv[:, :HD], (((1,), (1,)), ((), ())), preferred_element_type=jnp.float32
        ) * HD ** (-0.5)
        scores = scores.reshape(heads, tokens, scores.shape[1])
        key_code = kcode_ref[...]
        visible = ((key_code >= qlo_ref[...]) & (key_code <= qhi_ref[...]))[None]
        masked = jnp.where(visible, scores, NEGATIVE_FILL)
        old_max = m_sc[...]
        new_max = jnp.maximum(old_max, jnp.max(masked, axis=2, keepdims=True))
        weights = jnp.where(visible, jnp.exp(scores - new_max), 0.0)
        factor = jnp.exp(old_max - new_max)
        l_sc[...] = l_sc[...] * factor + jnp.sum(weights, axis=2, keepdims=True)
        product = jnp.dot(
            weights.reshape(heads * tokens, -1).astype(jnp.bfloat16),
            kv[:, HD:],
            preferred_element_type=jnp.float32,
        )
        acc_sc[...] = acc_sc[...] * factor + product.reshape(heads, tokens, HD)
        m_sc[...] = new_max

    @pl.when(j == pl.num_programs(1) - 1)
    def _():
        out_ref[...] = (acc_sc[...] / l_sc[...]).reshape(heads * tokens, HD).astype(out_ref.dtype)


def flash_attend(flags, queries, stacked, key_code, query_low, query_high):
    q_rows = queries.shape[0]
    k_rows = stacked.shape[0]
    tokens = query_low.shape[0]
    heads = q_rows // tokens
    grid_spec = pltpu.PrefetchScalarGridSpec(
        num_scalar_prefetch=1,
        grid=(1, k_rows // K_TILE),
        in_specs=[
            pl.BlockSpec((q_rows, HD), lambda i, j, f: (0, 0)),
            pl.BlockSpec((K_TILE, 2 * HD), lambda i, j, f: (j, 0)),
            pl.BlockSpec((1, K_TILE), lambda i, j, f: (0, j)),
            pl.BlockSpec((tokens, 1), lambda i, j, f: (0, 0)),
            pl.BlockSpec((tokens, 1), lambda i, j, f: (0, 0)),
        ],
        out_specs=pl.BlockSpec((q_rows, HD), lambda i, j, f: (0, 0)),
        scratch_shapes=[
            pltpu.VMEM((heads, tokens, 1), jnp.float32),
            pltpu.VMEM((heads, tokens, 1), jnp.float32),
            pltpu.VMEM((heads, tokens, HD), jnp.float32),
        ],
    )
    return pl.pallas_call(
        flash_kernel,
        grid_spec=grid_spec,
        out_shape=jax.ShapeDtypeStruct((q_rows, HD), jnp.bfloat16),
        compiler_params=pltpu.CompilerParams(dimension_semantics=("arbitrary", "arbitrary")),
    )(flags, queries, stacked, key_code, query_low, query_high)


def exchange_sum(values, axis_name):
    count = lax.axis_size(axis_name)
    stride = 1
    while stride < count:
        received = lax.ppermute(values, axis_name, [(i, i ^ stride) for i in range(count)])
        values = (values.astype(jnp.float32) + received.astype(jnp.float32)).astype(values.dtype)
        stride *= 2
    return values


def tile_flags(key_code, query_low, query_high):
    seen = (key_code[None, :] >= query_low[:, None]) & (key_code[None, :] <= query_high[:, None])
    return jnp.any(seen.reshape(query_low.shape[0], -1, K_TILE), axis=(0, 2)).astype(jnp.int32)


def attend_model(query_rows, gathered, flags, key_code, query_low, query_high, out_weight):
    tok_rows, kv_local, group_size = query_rows.shape[:3]
    flat_query = jnp.transpose(query_rows, (1, 2, 0, 3)).reshape(-1, HD)
    attended = flash_attend(
        flags, flat_query, gathered, key_code[None, :], query_low[:, None], query_high[:, None]
    )
    attended = jnp.transpose(attended.reshape(kv_local, group_size, tok_rows, HD), (2, 0, 1, 3))
    attended = attended.reshape(tok_rows, -1)
    return jnp.dot(attended, out_weight, preferred_element_type=jnp.float32)


def finish(model_state, out_weight):
    running_max, weight_sum, accumulated = model_state
    attended = accumulated / jnp.transpose(weight_sum, (2, 0, 1))[..., None]
    attended = attended.reshape(accumulated.shape[0], -1).astype(jnp.bfloat16)
    return jnp.dot(attended, out_weight, preferred_element_type=jnp.float32)


def head_terms(final_rows, head_weight, targets, vocab_start):
    logits = jnp.dot(final_rows, head_weight, preferred_element_type=jnp.float32)
    local_max = jnp.max(logits, axis=-1)
    word_ids = vocab_start + jnp.arange(logits.shape[1], dtype=jnp.int32)
    target_logit = jnp.sum(jnp.where(word_ids[None, :] == targets[:, None], logits, 0.0), axis=-1)
    return (logits, local_max, target_logit)


def local(
    policy_hidden,
    reference_hidden,
    targets,
    lengths,
    block_source,
    rollout_prompt,
    rollout_slot,
    policy_input_gain,
    policy_query_weight,
    policy_key_weight,
    policy_value_weight,
    policy_query_gain,
    policy_key_gain,
    policy_out_weight,
    policy_final_gain,
    policy_head,
    policy_prompt_keys,
    policy_prompt_values,
    reference_input_gain,
    reference_query_weight,
    reference_key_weight,
    reference_value_weight,
    reference_query_gain,
    reference_key_gain,
    reference_out_weight,
    reference_final_gain,
    reference_head,
    reference_prompt_keys,
    reference_prompt_values,
):
    tok_rows = policy_hidden.shape[0]
    roll_ids = jnp.arange(lengths.shape[0], dtype=jnp.int32)
    slot_ids = jnp.arange(tok_rows, dtype=jnp.int32)
    packed = jnp.repeat(block_source, BLOCK) * BLOCK + slot_ids % BLOCK
    end_points = jnp.cumsum(lengths)
    rollout = jnp.sum((packed[:, None] >= end_points[None, :]).astype(jnp.int32), axis=1)
    member = rollout[:, None] == roll_ids[None, :]
    position = packed - lookup(member, end_points - lengths)
    query_prompt = lookup(member, rollout_prompt)
    slot_of = lookup(member, rollout_slot)
    length_of = lookup(member, lengths)
    prompt_count = policy_prompt_keys.shape[0]
    prefix_local = policy_prompt_keys.shape[1]
    prompt_rows = prompt_count * prefix_local
    rope_offset = prefix_local * lax.axis_size("seq")
    prompt_ids = jnp.arange(prompt_rows, dtype=jnp.int32) // prefix_local
    seq_count = lax.axis_size("seq")
    shard_rows = tok_rows + prompt_rows
    policy_query, policy_stack = project(
        policy_hidden,
        policy_input_gain,
        policy_query_weight,
        policy_key_weight,
        policy_value_weight,
        policy_query_gain,
        policy_key_gain,
        policy_prompt_keys,
        policy_prompt_values,
        position,
        rope_offset,
    )
    reference_query, reference_stack = project(
        reference_hidden,
        reference_input_gain,
        reference_query_weight,
        reference_key_weight,
        reference_value_weight,
        reference_query_gain,
        reference_key_gain,
        reference_prompt_keys,
        reference_prompt_values,
        position,
        rope_offset,
    )
    pad_rows = prompt_rows
    carrier = jnp.zeros((pad_rows, policy_stack.shape[1]), jnp.bfloat16)
    carrier = carrier.at[0, : block_source.shape[0]].set(block_source.astype(jnp.bfloat16))
    policy_gathered = lax.all_gather(
        jnp.concatenate([policy_stack, carrier], axis=0), "seq", axis=0, tiled=True
    )
    policy_rows = policy_stack.shape[0] + pad_rows
    all_source = (
        policy_gathered.reshape(seq_count, policy_rows, -1)[:, policy_stack.shape[0], : block_source.shape[0]]
        .astype(jnp.int32)
        .reshape(-1)
    )
    all_ids = jnp.arange(tok_rows * seq_count, dtype=jnp.int32)
    all_packed = jnp.repeat(all_source, BLOCK) * BLOCK + all_ids % BLOCK
    all_rollout = jnp.sum((all_packed[:, None] >= end_points[None, :]).astype(jnp.int32), axis=1)
    all_member = all_rollout[:, None] == roll_ids[None, :]
    all_position = all_packed - lookup(all_member, end_points - lengths)
    owner = lookup(rollout_prompt[None, :] == jnp.arange(prompt_count, dtype=jnp.int32)[:, None], roll_ids)
    token_code = (all_rollout * CODE_STRIDE + all_position).reshape(seq_count, tok_rows)
    prompt_code = jnp.broadcast_to(owner[prompt_ids] * CODE_STRIDE - 1, (seq_count, prompt_rows))
    never_code = jnp.full((seq_count, pad_rows), -(1 << 30), jnp.int32)
    key_code = jnp.concatenate([token_code, prompt_code], axis=1).reshape(-1)
    policy_code = jnp.concatenate([token_code, prompt_code, never_code], axis=1).reshape(-1)
    query_low = rollout * CODE_STRIDE - 1
    query_high = rollout * CODE_STRIDE + position
    flags = tile_flags(key_code, query_low, query_high)
    policy_flags = tile_flags(policy_code, query_low, query_high)
    policy_part = attend_model(
        policy_query,
        policy_gathered,
        policy_flags,
        policy_code,
        query_low,
        query_high,
        policy_out_weight,
    )
    reference_part = attend_model(
        reference_query,
        lax.all_gather(reference_stack, "seq", axis=0, tiled=True),
        flags,
        key_code,
        query_low,
        query_high,
        reference_out_weight,
    )
    policy_summed = lax.psum(policy_part.astype(jnp.bfloat16), "vocab")
    policy_summed, reference_part = lax.optimization_barrier((policy_summed, reference_part))
    policy_mixed = policy_summed.astype(jnp.float32)
    reference_mixed = exchange_sum(reference_part.astype(jnp.bfloat16), "vocab").astype(jnp.float32)
    policy_final = rms_scale(
        policy_hidden.astype(jnp.float32) + policy_mixed, policy_final_gain
    ).astype(jnp.bfloat16)
    reference_final = rms_scale(
        reference_hidden.astype(jnp.float32) + reference_mixed, reference_final_gain
    ).astype(jnp.bfloat16)
    vocab_start = lax.axis_index("vocab") * policy_head.shape[1]
    policy_logits, policy_max, policy_target = head_terms(
        policy_final, policy_head, targets, vocab_start
    )
    reference_logits, reference_max, reference_target = head_terms(
        reference_final, reference_head, targets, vocab_start
    )
    policy_top, reference_top = lax.pmax((policy_max, reference_max), "vocab")
    policy_local = jnp.sum(jnp.exp(policy_logits - policy_top[:, None]), axis=-1)
    reference_local = jnp.sum(jnp.exp(reference_logits - reference_top[:, None]), axis=-1)
    totals = lax.psum((policy_local, reference_local, policy_target, reference_target), "vocab")
    policy_score = totals[2] - (policy_top + jnp.log(totals[0]))
    reference_score = totals[3] - (reference_top + jnp.log(totals[1]))
    token_diff = policy_score - reference_score
    per_token = token_diff / length_of.astype(jnp.float32)
    partial_sums = jnp.sum(
        jnp.where(slot_of[:, None] == roll_ids[None, :], per_token[:, None], 0.0), axis=0
    )
    rollout_mean = partial_sums
    stride = 1
    while stride < seq_count:
        rollout_mean = rollout_mean + lax.ppermute(
            rollout_mean, "seq", [(i, i ^ stride) for i in range(seq_count)]
        )
        stride *= 2
    return (token_diff, rollout_mean)


def solution(mesh):
    return jax.shard_map(
        local,
        mesh=mesh,
        in_specs=(
            P("seq", None),
            P("seq", None),
            P("seq"),
            P(),
            P("seq"),
            P(),
            P(),
            P(),
            P(None, "vocab"),
            P(None, "vocab"),
            P(None, "vocab"),
            P(),
            P(),
            P("vocab", None),
            P(),
            P(None, "vocab"),
            P(None, "seq", "vocab"),
            P(None, "seq", "vocab"),
            P(),
            P(None, "vocab"),
            P(None, "vocab"),
            P(None, "vocab"),
            P(),
            P(),
            P("vocab", None),
            P(),
            P(None, "vocab"),
            P(None, "seq", "vocab"),
            P(None, "seq", "vocab"),
        ),
        out_specs=(P("seq"), P()),
        check_vma=False,
    )
```

```python
import jax
import jax.numpy as jnp
from jax import lax
from jax.sharding import PartitionSpec as P
from jax.experimental import pallas as pl
from jax.experimental.pallas import tpu as pltpu

HD = 128
BLOCK = 128


EPSILON = 1e-06
ROPE_BASE = 1000000.0
NEGATIVE_FILL = -1e30


def rms_scale(values, gain_row):
    values = values.astype(jnp.float32)
    return (
        values * lax.rsqrt(jnp.mean(values * values, axis=-1, keepdims=True) + EPSILON) * gain_row
    )


def rotate(values, positions):
    half_width = values.shape[-1] // 2
    frequency = ROPE_BASE ** (-2.0 * jnp.arange(half_width, dtype=jnp.float32) / values.shape[-1])
    angles = positions.astype(jnp.float32)[:, None] * frequency[None, :]
    cosine = jnp.cos(angles)
    sine_part = jnp.sin(angles)
    cosine = jnp.concatenate([cosine, cosine], axis=-1)[:, None, :]
    sine_part = jnp.concatenate([sine_part, sine_part], axis=-1)[:, None, :]
    turned = jnp.concatenate([-values[..., half_width:], values[..., :half_width]], axis=-1)
    return values * cosine + turned * sine_part


def lookup(member, lookup_table):
    return jnp.sum(jnp.where(member, lookup_table[None, :], 0), axis=1)


def project(
    hidden,
    input_gain,
    query_weight,
    key_weight,
    value_weight,
    query_gain,
    key_gain,
    prompt_keys,
    prompt_values,
    positions,
    rope_offset,
):
    tok_rows = hidden.shape[0]
    kv_local = key_weight.shape[1] // HD
    normed = rms_scale(hidden, input_gain).astype(jnp.bfloat16)
    query_rows = jnp.dot(normed, query_weight, preferred_element_type=jnp.float32).reshape(
        tok_rows, -1, HD
    )
    query_rows = rotate(rms_scale(query_rows, query_gain), positions + rope_offset).astype(
        jnp.bfloat16
    )
    key_rows = jnp.dot(normed, key_weight, preferred_element_type=jnp.float32).reshape(
        tok_rows, kv_local, HD
    )
    key_rows = (
        rotate(rms_scale(key_rows, key_gain), positions + rope_offset)
        .astype(jnp.bfloat16)
        .reshape(tok_rows, kv_local * HD)
    )
    value_rows = jnp.dot(normed, value_weight, preferred_element_type=jnp.float32).astype(
        jnp.bfloat16
    )
    key_block = jnp.concatenate([key_rows, prompt_keys.reshape(-1, kv_local * HD)], axis=0)
    value_block = jnp.concatenate([value_rows, prompt_values.reshape(-1, kv_local * HD)], axis=0)
    stacked = jnp.concatenate([key_block, value_block], axis=1)
    return (query_rows.reshape(tok_rows, kv_local, -1, HD), stacked)


def empty_state(query_rows):
    tok_rows, kv_local, group_size = (query_rows.shape[0], query_rows.shape[1], query_rows.shape[2])
    running_max = jnp.full((kv_local, group_size, tok_rows), NEGATIVE_FILL, jnp.float32)
    weight_sum = jnp.zeros((kv_local, group_size, tok_rows), jnp.float32)
    accumulated = jnp.zeros((tok_rows, kv_local, group_size, HD), jnp.float32)
    return (running_max, weight_sum, accumulated)


def update_state(model_state, query_rows, stacked, visible):
    running_max, weight_sum, accumulated = model_state
    half_columns = stacked.shape[1] // 2
    kv_local = query_rows.shape[1]
    key_part = stacked[:, :half_columns].reshape(-1, kv_local, HD)
    value_part = stacked[:, half_columns:].reshape(-1, kv_local, HD)
    scores = jnp.einsum(
        "qkgd,skd->kgqs", query_rows, key_part, preferred_element_type=jnp.float32
    ) * HD ** (-0.5)
    masked = jnp.where(visible[None, None], scores, NEGATIVE_FILL)
    new_max = jnp.maximum(running_max, jnp.max(masked, axis=-1))
    weights = jnp.where(visible[None, None], jnp.exp(scores - new_max[..., None]), 0.0)
    factor = jnp.exp(running_max - new_max)
    new_sum = weight_sum * factor + jnp.sum(weights, axis=-1)
    product = jnp.einsum(
        "kgqs,skd->qkgd",
        weights.astype(jnp.bfloat16),
        value_part,
        preferred_element_type=jnp.float32,
    )
    new_accumulated = accumulated * jnp.transpose(factor, (2, 0, 1))[..., None] + product
    return (new_max, new_sum, new_accumulated)


def attend(states, queries, pieces, query_tag, query_position, query_prompt):
    stacked_list = pieces[:-2]
    key_tag = pieces[-2]
    key_position = pieces[-1]
    visible = (key_tag[None, :] == query_tag[:, None]) & (
        key_position[None, :] <= query_position[:, None]
    ) | (key_tag[None, :] == -1 - query_prompt[:, None])

    def compute(current):
        updated = []
        for model_state, query_rows, stacked in zip(current, queries, stacked_list):
            updated.append(update_state(model_state, query_rows, stacked, visible))
        return tuple(updated)

    def unchanged(current):
        return current

    return lax.cond(jnp.any(visible), compute, unchanged, states)


def make_fold(queries, query_tag, query_position, query_prompt, shard_rows):

    def fold_pieces(states, pieces, start_row):
        rows_here = pieces[0].shape[0]
        shard_count = rows_here // shard_rows
        split_pieces = tuple(
            (
                member_piece.reshape((shard_count, shard_rows) + member_piece.shape[1:])
                for member_piece in pieces
            )
        )

        def scan_step(carry_states, piece_item):
            return (
                attend(carry_states, queries, piece_item, query_tag, query_position, query_prompt),
                None,
            )

        return lax.scan(scan_step, states, split_pieces)[0]

    return fold_pieces


Q_TILE = 512
K_TILE = 1024
CODE_STRIDE = 65536


def flash_kernel(flags_ref, q_ref, kv_ref, kcode_ref, qlo_ref, qhi_ref, out_ref, m_sc, l_sc, acc_sc):
    j = pl.program_id(1)

    @pl.when(j == 0)
    def _():
        m_sc[...] = jnp.full(m_sc.shape, NEGATIVE_FILL, jnp.float32)
        l_sc[...] = jnp.zeros(l_sc.shape, jnp.float32)
        acc_sc[...] = jnp.zeros(acc_sc.shape, jnp.float32)

    @pl.when(flags_ref[j] > 0)
    def _():
        kv = kv_ref[...]
        scores = lax.dot_general(
            q_ref[...], kv[:, :HD], (((1,), (1,)), ((), ())), preferred_element_type=jnp.float32
        ) * HD ** (-0.5)
        key_code = kcode_ref[...]
        visible = (key_code >= qlo_ref[...]) & (key_code <= qhi_ref[...])
        masked = jnp.where(visible, scores, NEGATIVE_FILL)
        old_max = m_sc[...]
        new_max = jnp.maximum(old_max, jnp.max(masked, axis=1, keepdims=True))
        weights = jnp.where(visible, jnp.exp(scores - new_max), 0.0)
        factor = jnp.exp(old_max - new_max)
        l_sc[...] = l_sc[...] * factor + jnp.sum(weights, axis=1, keepdims=True)
        acc_sc[...] = acc_sc[...] * factor + jnp.dot(
            weights.astype(jnp.bfloat16), kv[:, HD:], preferred_element_type=jnp.float32
        )
        m_sc[...] = new_max

    @pl.when(j == pl.num_programs(1) - 1)
    def _():
        out_ref[...] = (acc_sc[...] / l_sc[...]).astype(out_ref.dtype)


def flash_attend(flags, queries, stacked, key_code, query_low, query_high):
    q_rows = queries.shape[0]
    k_rows = stacked.shape[0]
    grid_spec = pltpu.PrefetchScalarGridSpec(
        num_scalar_prefetch=1,
        grid=(q_rows // Q_TILE, k_rows // K_TILE),
        in_specs=[
            pl.BlockSpec((Q_TILE, HD), lambda i, j, f: (i, 0)),
            pl.BlockSpec((K_TILE, 2 * HD), lambda i, j, f: (j, 0)),
            pl.BlockSpec((1, K_TILE), lambda i, j, f: (0, j)),
            pl.BlockSpec((Q_TILE, 1), lambda i, j, f: (i, 0)),
            pl.BlockSpec((Q_TILE, 1), lambda i, j, f: (i, 0)),
        ],
        out_specs=pl.BlockSpec((Q_TILE, HD), lambda i, j, f: (i, 0)),
        scratch_shapes=[
            pltpu.VMEM((Q_TILE, 1), jnp.float32),
            pltpu.VMEM((Q_TILE, 1), jnp.float32),
            pltpu.VMEM((Q_TILE, HD), jnp.float32),
        ],
    )
    return pl.pallas_call(
        flash_kernel,
        grid_spec=grid_spec,
        out_shape=jax.ShapeDtypeStruct((q_rows, HD), jnp.bfloat16),
        compiler_params=pltpu.CompilerParams(dimension_semantics=("arbitrary", "arbitrary")),
    )(flags, queries, stacked, key_code, query_low, query_high)


def exchange_sum(values, axis_name):
    count = lax.axis_size(axis_name)
    stride = 1
    while stride < count:
        received = lax.ppermute(values, axis_name, [(i, i ^ stride) for i in range(count)])
        values = (values.astype(jnp.float32) + received.astype(jnp.float32)).astype(values.dtype)
        stride *= 2
    return values


def tile_flags(key_code, query_low, query_high):
    seen = (key_code[None, :] >= query_low[:, None]) & (key_code[None, :] <= query_high[:, None])
    return jnp.any(seen.reshape(query_low.shape[0], -1, K_TILE), axis=(0, 2)).astype(jnp.int32)


def attend_model(query_rows, gathered, flags, key_code, query_low, query_high, out_weight):
    tok_rows, kv_local, group_size = query_rows.shape[:3]
    flat_query = jnp.transpose(query_rows, (1, 2, 0, 3)).reshape(-1, HD)
    tiled_low = jnp.tile(query_low, kv_local * group_size)[:, None]
    tiled_high = jnp.tile(query_high, kv_local * group_size)[:, None]
    attended = flash_attend(flags, flat_query, gathered, key_code[None, :], tiled_low, tiled_high)
    attended = jnp.transpose(attended.reshape(kv_local, group_size, tok_rows, HD), (2, 0, 1, 3))
    attended = attended.reshape(tok_rows, -1)
    return jnp.dot(attended, out_weight, preferred_element_type=jnp.float32)


def finish(model_state, out_weight):
    running_max, weight_sum, accumulated = model_state
    attended = accumulated / jnp.transpose(weight_sum, (2, 0, 1))[..., None]
    attended = attended.reshape(accumulated.shape[0], -1).astype(jnp.bfloat16)
    return jnp.dot(attended, out_weight, preferred_element_type=jnp.float32)


def head_terms(final_rows, head_weight, targets, vocab_start):
    logits = jnp.dot(final_rows, head_weight, preferred_element_type=jnp.float32)
    local_max = jnp.max(logits, axis=-1)
    word_ids = vocab_start + jnp.arange(logits.shape[1], dtype=jnp.int32)
    target_logit = jnp.sum(jnp.where(word_ids[None, :] == targets[:, None], logits, 0.0), axis=-1)
    return (logits, local_max, target_logit)


def local(
    policy_hidden,
    reference_hidden,
    targets,
    lengths,
    block_source,
    rollout_prompt,
    rollout_slot,
    policy_input_gain,
    policy_query_weight,
    policy_key_weight,
    policy_value_weight,
    policy_query_gain,
    policy_key_gain,
    policy_out_weight,
    policy_final_gain,
    policy_head,
    policy_prompt_keys,
    policy_prompt_values,
    reference_input_gain,
    reference_query_weight,
    reference_key_weight,
    reference_value_weight,
    reference_query_gain,
    reference_key_gain,
    reference_out_weight,
    reference_final_gain,
    reference_head,
    reference_prompt_keys,
    reference_prompt_values,
):
    tok_rows = policy_hidden.shape[0]
    roll_ids = jnp.arange(lengths.shape[0], dtype=jnp.int32)
    slot_ids = jnp.arange(tok_rows, dtype=jnp.int32)
    packed = jnp.repeat(block_source, BLOCK) * BLOCK + slot_ids % BLOCK
    end_points = jnp.cumsum(lengths)
    rollout = jnp.sum((packed[:, None] >= end_points[None, :]).astype(jnp.int32), axis=1)
    member = rollout[:, None] == roll_ids[None, :]
    position = packed - lookup(member, end_points - lengths)
    query_prompt = lookup(member, rollout_prompt)
    slot_of = lookup(member, rollout_slot)
    length_of = lookup(member, lengths)
    prompt_count = policy_prompt_keys.shape[0]
    prefix_local = policy_prompt_keys.shape[1]
    prompt_rows = prompt_count * prefix_local
    rope_offset = prefix_local * lax.axis_size("seq")
    prompt_ids = jnp.arange(prompt_rows, dtype=jnp.int32) // prefix_local
    seq_count = lax.axis_size("seq")
    shard_rows = tok_rows + prompt_rows
    policy_query, policy_stack = project(
        policy_hidden,
        policy_input_gain,
        policy_query_weight,
        policy_key_weight,
        policy_value_weight,
        policy_query_gain,
        policy_key_gain,
        policy_prompt_keys,
        policy_prompt_values,
        position,
        rope_offset,
    )
    reference_query, reference_stack = project(
        reference_hidden,
        reference_input_gain,
        reference_query_weight,
        reference_key_weight,
        reference_value_weight,
        reference_query_gain,
        reference_key_gain,
        reference_prompt_keys,
        reference_prompt_values,
        position,
        rope_offset,
    )
    pad_rows = prompt_rows
    carrier = jnp.zeros((pad_rows, policy_stack.shape[1]), jnp.bfloat16)
    carrier = carrier.at[0, : block_source.shape[0]].set(block_source.astype(jnp.bfloat16))
    policy_gathered = lax.all_gather(
        jnp.concatenate([policy_stack, carrier], axis=0), "seq", axis=0, tiled=True
    )
    policy_rows = policy_stack.shape[0] + pad_rows
    all_source = (
        policy_gathered.reshape(seq_count, policy_rows, -1)[:, policy_stack.shape[0], : block_source.shape[0]]
        .astype(jnp.int32)
        .reshape(-1)
    )
    all_ids = jnp.arange(tok_rows * seq_count, dtype=jnp.int32)
    all_packed = jnp.repeat(all_source, BLOCK) * BLOCK + all_ids % BLOCK
    all_rollout = jnp.sum((all_packed[:, None] >= end_points[None, :]).astype(jnp.int32), axis=1)
    all_member = all_rollout[:, None] == roll_ids[None, :]
    all_position = all_packed - lookup(all_member, end_points - lengths)
    owner = lookup(rollout_prompt[None, :] == jnp.arange(prompt_count, dtype=jnp.int32)[:, None], roll_ids)
    token_code = (all_rollout * CODE_STRIDE + all_position).reshape(seq_count, tok_rows)
    prompt_code = jnp.broadcast_to(owner[prompt_ids] * CODE_STRIDE - 1, (seq_count, prompt_rows))
    never_code = jnp.full((seq_count, pad_rows), -(1 << 30), jnp.int32)
    key_code = jnp.concatenate([token_code, prompt_code], axis=1).reshape(-1)
    policy_code = jnp.concatenate([token_code, prompt_code, never_code], axis=1).reshape(-1)
    query_low = rollout * CODE_STRIDE - 1
    query_high = rollout * CODE_STRIDE + position
    flags = tile_flags(key_code, query_low, query_high)
    policy_flags = tile_flags(policy_code, query_low, query_high)
    policy_part = attend_model(
        policy_query,
        policy_gathered,
        policy_flags,
        policy_code,
        query_low,
        query_high,
        policy_out_weight,
    )
    policy_summed = lax.psum(policy_part.astype(jnp.bfloat16), "vocab")
    policy_mixed = policy_summed.astype(jnp.float32)
    reference_gathered = lax.all_gather(reference_stack, "seq", axis=0, tiled=True)
    _, reference_gathered = lax.optimization_barrier((policy_part, reference_gathered))
    half = tok_rows // 2
    reference_halves = []
    for lo in (0, half):
        half_low = query_low[lo : lo + half]
        half_high = query_high[lo : lo + half]
        half_part = attend_model(
            reference_query[lo : lo + half],
            reference_gathered,
            tile_flags(key_code, half_low, half_high),
            key_code,
            half_low,
            half_high,
            reference_out_weight,
        )
        reference_halves.append(exchange_sum(half_part.astype(jnp.bfloat16), "vocab"))
    reference_mixed = jnp.concatenate(reference_halves, axis=0).astype(jnp.float32)
    policy_final = rms_scale(
        policy_hidden.astype(jnp.float32) + policy_mixed, policy_final_gain
    ).astype(jnp.bfloat16)
    reference_final = rms_scale(
        reference_hidden.astype(jnp.float32) + reference_mixed, reference_final_gain
    ).astype(jnp.bfloat16)
    vocab_start = lax.axis_index("vocab") * policy_head.shape[1]
    policy_logits, policy_max, policy_target = head_terms(
        policy_final, policy_head, targets, vocab_start
    )
    reference_logits, reference_max, reference_target = head_terms(
        reference_final, reference_head, targets, vocab_start
    )
    policy_top, reference_top = lax.pmax((policy_max, reference_max), "vocab")
    policy_local = jnp.sum(jnp.exp(policy_logits - policy_top[:, None]), axis=-1)
    reference_local = jnp.sum(jnp.exp(reference_logits - reference_top[:, None]), axis=-1)
    totals = lax.psum((policy_local, reference_local, policy_target, reference_target), "vocab")
    policy_score = totals[2] - (policy_top + jnp.log(totals[0]))
    reference_score = totals[3] - (reference_top + jnp.log(totals[1]))
    token_diff = policy_score - reference_score
    per_token = token_diff / length_of.astype(jnp.float32)
    partial_sums = jnp.sum(
        jnp.where(slot_of[:, None] == roll_ids[None, :], per_token[:, None], 0.0), axis=0
    )
    rollout_mean = partial_sums
    stride = 1
    while stride < seq_count:
        rollout_mean = rollout_mean + lax.ppermute(
            rollout_mean, "seq", [(i, i ^ stride) for i in range(seq_count)]
        )
        stride *= 2
    return (token_diff, rollout_mean)


def solution(mesh):
    return jax.shard_map(
        local,
        mesh=mesh,
        in_specs=(
            P("seq", None),
            P("seq", None),
            P("seq"),
            P(),
            P("seq"),
            P(),
            P(),
            P(),
            P(None, "vocab"),
            P(None, "vocab"),
            P(None, "vocab"),
            P(),
            P(),
            P("vocab", None),
            P(),
            P(None, "vocab"),
            P(None, "seq", "vocab"),
            P(None, "seq", "vocab"),
            P(),
            P(None, "vocab"),
            P(None, "vocab"),
            P(None, "vocab"),
            P(),
            P(),
            P("vocab", None),
            P(),
            P(None, "vocab"),
            P(None, "seq", "vocab"),
            P(None, "seq", "vocab"),
        ),
        out_specs=(P("seq"), P()),
        check_vma=False,
    )
```

```python
import jax
import jax.numpy as jnp
from jax import lax
from jax.sharding import PartitionSpec as P
from jax.experimental import pallas as pl
from jax.experimental.pallas import tpu as pltpu

HD = 128
BLOCK = 128


EPSILON = 1e-06
ROPE_BASE = 1000000.0
NEGATIVE_FILL = -1e30


def rms_scale(values, gain_row):
    values = values.astype(jnp.float32)
    return (
        values * lax.rsqrt(jnp.mean(values * values, axis=-1, keepdims=True) + EPSILON) * gain_row
    )


def rotate(values, positions):
    half_width = values.shape[-1] // 2
    frequency = ROPE_BASE ** (-2.0 * jnp.arange(half_width, dtype=jnp.float32) / values.shape[-1])
    angles = positions.astype(jnp.float32)[:, None] * frequency[None, :]
    cosine = jnp.cos(angles)
    sine_part = jnp.sin(angles)
    cosine = jnp.concatenate([cosine, cosine], axis=-1)[:, None, :]
    sine_part = jnp.concatenate([sine_part, sine_part], axis=-1)[:, None, :]
    turned = jnp.concatenate([-values[..., half_width:], values[..., :half_width]], axis=-1)
    return values * cosine + turned * sine_part


def lookup(member, lookup_table):
    return jnp.sum(jnp.where(member, lookup_table[None, :], 0), axis=1)


def project(
    hidden,
    input_gain,
    query_weight,
    key_weight,
    value_weight,
    query_gain,
    key_gain,
    prompt_keys,
    prompt_values,
    positions,
    rope_offset,
):
    tok_rows = hidden.shape[0]
    kv_local = key_weight.shape[1] // HD
    normed = rms_scale(hidden, input_gain).astype(jnp.bfloat16)
    query_rows = jnp.dot(normed, query_weight, preferred_element_type=jnp.float32).reshape(
        tok_rows, -1, HD
    )
    query_rows = rotate(rms_scale(query_rows, query_gain), positions + rope_offset).astype(
        jnp.bfloat16
    )
    key_rows = jnp.dot(normed, key_weight, preferred_element_type=jnp.float32).reshape(
        tok_rows, kv_local, HD
    )
    key_rows = (
        rotate(rms_scale(key_rows, key_gain), positions + rope_offset)
        .astype(jnp.bfloat16)
        .reshape(tok_rows, kv_local * HD)
    )
    value_rows = jnp.dot(normed, value_weight, preferred_element_type=jnp.float32).astype(
        jnp.bfloat16
    )
    key_block = jnp.concatenate([key_rows, prompt_keys.reshape(-1, kv_local * HD)], axis=0)
    value_block = jnp.concatenate([value_rows, prompt_values.reshape(-1, kv_local * HD)], axis=0)
    stacked = jnp.concatenate([key_block, value_block], axis=1)
    return (query_rows.reshape(tok_rows, kv_local, -1, HD), stacked)


def empty_state(query_rows):
    tok_rows, kv_local, group_size = (query_rows.shape[0], query_rows.shape[1], query_rows.shape[2])
    running_max = jnp.full((kv_local, group_size, tok_rows), NEGATIVE_FILL, jnp.float32)
    weight_sum = jnp.zeros((kv_local, group_size, tok_rows), jnp.float32)
    accumulated = jnp.zeros((tok_rows, kv_local, group_size, HD), jnp.float32)
    return (running_max, weight_sum, accumulated)


def update_state(model_state, query_rows, stacked, visible):
    running_max, weight_sum, accumulated = model_state
    half_columns = stacked.shape[1] // 2
    kv_local = query_rows.shape[1]
    key_part = stacked[:, :half_columns].reshape(-1, kv_local, HD)
    value_part = stacked[:, half_columns:].reshape(-1, kv_local, HD)
    scores = jnp.einsum(
        "qkgd,skd->kgqs", query_rows, key_part, preferred_element_type=jnp.float32
    ) * HD ** (-0.5)
    masked = jnp.where(visible[None, None], scores, NEGATIVE_FILL)
    new_max = jnp.maximum(running_max, jnp.max(masked, axis=-1))
    weights = jnp.where(visible[None, None], jnp.exp(scores - new_max[..., None]), 0.0)
    factor = jnp.exp(running_max - new_max)
    new_sum = weight_sum * factor + jnp.sum(weights, axis=-1)
    product = jnp.einsum(
        "kgqs,skd->qkgd",
        weights.astype(jnp.bfloat16),
        value_part,
        preferred_element_type=jnp.float32,
    )
    new_accumulated = accumulated * jnp.transpose(factor, (2, 0, 1))[..., None] + product
    return (new_max, new_sum, new_accumulated)


def attend(states, queries, pieces, query_tag, query_position, query_prompt):
    stacked_list = pieces[:-2]
    key_tag = pieces[-2]
    key_position = pieces[-1]
    visible = (key_tag[None, :] == query_tag[:, None]) & (
        key_position[None, :] <= query_position[:, None]
    ) | (key_tag[None, :] == -1 - query_prompt[:, None])

    def compute(current):
        updated = []
        for model_state, query_rows, stacked in zip(current, queries, stacked_list):
            updated.append(update_state(model_state, query_rows, stacked, visible))
        return tuple(updated)

    def unchanged(current):
        return current

    return lax.cond(jnp.any(visible), compute, unchanged, states)


def make_fold(queries, query_tag, query_position, query_prompt, shard_rows):

    def fold_pieces(states, pieces, start_row):
        rows_here = pieces[0].shape[0]
        shard_count = rows_here // shard_rows
        split_pieces = tuple(
            (
                member_piece.reshape((shard_count, shard_rows) + member_piece.shape[1:])
                for member_piece in pieces
            )
        )

        def scan_step(carry_states, piece_item):
            return (
                attend(carry_states, queries, piece_item, query_tag, query_position, query_prompt),
                None,
            )

        return lax.scan(scan_step, states, split_pieces)[0]

    return fold_pieces


Q_TILE = 512
K_TILE = 1024
CODE_STRIDE = 65536


def flash_kernel(flags_ref, q_ref, kv_ref, kcode_ref, qlo_ref, qhi_ref, out_ref, m_sc, l_sc, acc_sc):
    j = pl.program_id(1)

    @pl.when(j == 0)
    def _():
        m_sc[...] = jnp.full(m_sc.shape, NEGATIVE_FILL, jnp.float32)
        l_sc[...] = jnp.zeros(l_sc.shape, jnp.float32)
        acc_sc[...] = jnp.zeros(acc_sc.shape, jnp.float32)

    @pl.when(flags_ref[j] > 0)
    def _():
        kv = kv_ref[...]
        scores = lax.dot_general(
            q_ref[...], kv[:, :HD], (((1,), (1,)), ((), ())), preferred_element_type=jnp.float32
        ) * HD ** (-0.5)
        key_code = kcode_ref[...]
        visible = (key_code >= qlo_ref[...]) & (key_code <= qhi_ref[...])
        masked = jnp.where(visible, scores, NEGATIVE_FILL)
        old_max = m_sc[...]
        new_max = jnp.maximum(old_max, jnp.max(masked, axis=1, keepdims=True))
        weights = jnp.where(visible, jnp.exp(scores - new_max), 0.0)
        factor = jnp.exp(old_max - new_max)
        l_sc[...] = l_sc[...] * factor + jnp.sum(weights, axis=1, keepdims=True)
        acc_sc[...] = acc_sc[...] * factor + jnp.dot(
            weights.astype(jnp.bfloat16), kv[:, HD:], preferred_element_type=jnp.float32
        )
        m_sc[...] = new_max

    @pl.when(j == pl.num_programs(1) - 1)
    def _():
        out_ref[...] = (acc_sc[...] / l_sc[...]).astype(out_ref.dtype)


def flash_attend(flags, queries, stacked, key_code, query_low, query_high):
    q_rows = queries.shape[0]
    k_rows = stacked.shape[0]
    grid_spec = pltpu.PrefetchScalarGridSpec(
        num_scalar_prefetch=1,
        grid=(q_rows // Q_TILE, k_rows // K_TILE),
        in_specs=[
            pl.BlockSpec((Q_TILE, HD), lambda i, j, f: (i, 0)),
            pl.BlockSpec((K_TILE, 2 * HD), lambda i, j, f: (j, 0)),
            pl.BlockSpec((1, K_TILE), lambda i, j, f: (0, j)),
            pl.BlockSpec((Q_TILE, 1), lambda i, j, f: (i, 0)),
            pl.BlockSpec((Q_TILE, 1), lambda i, j, f: (i, 0)),
        ],
        out_specs=pl.BlockSpec((Q_TILE, HD), lambda i, j, f: (i, 0)),
        scratch_shapes=[
            pltpu.VMEM((Q_TILE, 1), jnp.float32),
            pltpu.VMEM((Q_TILE, 1), jnp.float32),
            pltpu.VMEM((Q_TILE, HD), jnp.float32),
        ],
    )
    return pl.pallas_call(
        flash_kernel,
        grid_spec=grid_spec,
        out_shape=jax.ShapeDtypeStruct((q_rows, HD), jnp.bfloat16),
        compiler_params=pltpu.CompilerParams(dimension_semantics=("arbitrary", "arbitrary")),
    )(flags, queries, stacked, key_code, query_low, query_high)


def exchange_sum(values, axis_name):
    count = lax.axis_size(axis_name)
    stride = 1
    while stride < count:
        received = lax.ppermute(values, axis_name, [(i, i ^ stride) for i in range(count)])
        values = (values.astype(jnp.float32) + received.astype(jnp.float32)).astype(values.dtype)
        stride *= 2
    return values


def tile_flags(key_code, query_low, query_high):
    seen = (key_code[None, :] >= query_low[:, None]) & (key_code[None, :] <= query_high[:, None])
    return jnp.any(seen.reshape(query_low.shape[0], -1, K_TILE), axis=(0, 2)).astype(jnp.int32)


def attend_model(query_rows, gathered, flags, key_code, query_low, query_high, out_weight):
    tok_rows, kv_local, group_size = query_rows.shape[:3]
    flat_query = jnp.transpose(query_rows, (1, 2, 0, 3)).reshape(-1, HD)
    tiled_low = jnp.tile(query_low, kv_local * group_size)[:, None]
    tiled_high = jnp.tile(query_high, kv_local * group_size)[:, None]
    attended = flash_attend(flags, flat_query, gathered, key_code[None, :], tiled_low, tiled_high)
    attended = jnp.transpose(attended.reshape(kv_local, group_size, tok_rows, HD), (2, 0, 1, 3))
    attended = attended.reshape(tok_rows, -1)
    return jnp.dot(attended, out_weight, preferred_element_type=jnp.float32)


def finish(model_state, out_weight):
    running_max, weight_sum, accumulated = model_state
    attended = accumulated / jnp.transpose(weight_sum, (2, 0, 1))[..., None]
    attended = attended.reshape(accumulated.shape[0], -1).astype(jnp.bfloat16)
    return jnp.dot(attended, out_weight, preferred_element_type=jnp.float32)


def head_terms(final_rows, head_weight, targets, vocab_start):
    logits = jnp.dot(final_rows, head_weight, preferred_element_type=jnp.float32)
    local_max = jnp.max(logits, axis=-1)
    word_ids = vocab_start + jnp.arange(logits.shape[1], dtype=jnp.int32)
    target_logit = jnp.sum(jnp.where(word_ids[None, :] == targets[:, None], logits, 0.0), axis=-1)
    return (logits, local_max, target_logit)


def local(
    policy_hidden,
    reference_hidden,
    targets,
    lengths,
    block_source,
    rollout_prompt,
    rollout_slot,
    policy_input_gain,
    policy_query_weight,
    policy_key_weight,
    policy_value_weight,
    policy_query_gain,
    policy_key_gain,
    policy_out_weight,
    policy_final_gain,
    policy_head,
    policy_prompt_keys,
    policy_prompt_values,
    reference_input_gain,
    reference_query_weight,
    reference_key_weight,
    reference_value_weight,
    reference_query_gain,
    reference_key_gain,
    reference_out_weight,
    reference_final_gain,
    reference_head,
    reference_prompt_keys,
    reference_prompt_values,
):
    tok_rows = policy_hidden.shape[0]
    roll_ids = jnp.arange(lengths.shape[0], dtype=jnp.int32)
    slot_ids = jnp.arange(tok_rows, dtype=jnp.int32)
    packed = jnp.repeat(block_source, BLOCK) * BLOCK + slot_ids % BLOCK
    end_points = jnp.cumsum(lengths)
    rollout = jnp.sum((packed[:, None] >= end_points[None, :]).astype(jnp.int32), axis=1)
    member = rollout[:, None] == roll_ids[None, :]
    position = packed - lookup(member, end_points - lengths)
    query_prompt = lookup(member, rollout_prompt)
    slot_of = lookup(member, rollout_slot)
    length_of = lookup(member, lengths)
    prompt_count = policy_prompt_keys.shape[0]
    prefix_local = policy_prompt_keys.shape[1]
    prompt_rows = prompt_count * prefix_local
    rope_offset = prefix_local * lax.axis_size("seq")
    prompt_ids = jnp.arange(prompt_rows, dtype=jnp.int32) // prefix_local
    seq_count = lax.axis_size("seq")
    shard_rows = tok_rows + prompt_rows
    policy_query, policy_stack = project(
        policy_hidden,
        policy_input_gain,
        policy_query_weight,
        policy_key_weight,
        policy_value_weight,
        policy_query_gain,
        policy_key_gain,
        policy_prompt_keys,
        policy_prompt_values,
        position,
        rope_offset,
    )
    reference_query, reference_stack = project(
        reference_hidden,
        reference_input_gain,
        reference_query_weight,
        reference_key_weight,
        reference_value_weight,
        reference_query_gain,
        reference_key_gain,
        reference_prompt_keys,
        reference_prompt_values,
        position,
        rope_offset,
    )
    pad_rows = prompt_rows
    carrier = jnp.zeros((pad_rows, policy_stack.shape[1]), jnp.bfloat16)
    carrier = carrier.at[0, : block_source.shape[0]].set(block_source.astype(jnp.bfloat16))
    policy_gathered = lax.all_gather(
        jnp.concatenate([policy_stack, carrier], axis=0), "seq", axis=0, tiled=True
    )
    policy_rows = policy_stack.shape[0] + pad_rows
    all_source = (
        policy_gathered.reshape(seq_count, policy_rows, -1)[:, policy_stack.shape[0], : block_source.shape[0]]
        .astype(jnp.int32)
        .reshape(-1)
    )
    all_ids = jnp.arange(tok_rows * seq_count, dtype=jnp.int32)
    all_packed = jnp.repeat(all_source, BLOCK) * BLOCK + all_ids % BLOCK
    all_rollout = jnp.sum((all_packed[:, None] >= end_points[None, :]).astype(jnp.int32), axis=1)
    all_member = all_rollout[:, None] == roll_ids[None, :]
    all_position = all_packed - lookup(all_member, end_points - lengths)
    owner = lookup(rollout_prompt[None, :] == jnp.arange(prompt_count, dtype=jnp.int32)[:, None], roll_ids)
    token_code = (all_rollout * CODE_STRIDE + all_position).reshape(seq_count, tok_rows)
    prompt_code = jnp.broadcast_to(owner[prompt_ids] * CODE_STRIDE - 1, (seq_count, prompt_rows))
    never_code = jnp.full((seq_count, pad_rows), -(1 << 30), jnp.int32)
    key_code = jnp.concatenate([token_code, prompt_code], axis=1).reshape(-1)
    policy_code = jnp.concatenate([token_code, prompt_code, never_code], axis=1).reshape(-1)
    query_low = rollout * CODE_STRIDE - 1
    query_high = rollout * CODE_STRIDE + position
    flags = tile_flags(key_code, query_low, query_high)
    policy_flags = tile_flags(policy_code, query_low, query_high)
    policy_part = attend_model(
        policy_query,
        policy_gathered,
        policy_flags,
        policy_code,
        query_low,
        query_high,
        policy_out_weight,
    )
    policy_summed = exchange_sum(policy_part.astype(jnp.bfloat16), "vocab")
    policy_mixed = policy_summed.astype(jnp.float32)
    reference_gathered = lax.all_gather(reference_stack, "seq", axis=0, tiled=True)
    _, reference_gathered = lax.optimization_barrier((policy_part, reference_gathered))
    half = tok_rows // 2
    reference_halves = []
    for lo in (0, half):
        half_low = query_low[lo : lo + half]
        half_high = query_high[lo : lo + half]
        half_part = attend_model(
            reference_query[lo : lo + half],
            reference_gathered,
            tile_flags(key_code, half_low, half_high),
            key_code,
            half_low,
            half_high,
            reference_out_weight,
        )
        reference_halves.append(exchange_sum(half_part.astype(jnp.bfloat16), "vocab"))
    reference_mixed = jnp.concatenate(reference_halves, axis=0).astype(jnp.float32)
    policy_final = rms_scale(
        policy_hidden.astype(jnp.float32) + policy_mixed, policy_final_gain
    ).astype(jnp.bfloat16)
    reference_final = rms_scale(
        reference_hidden.astype(jnp.float32) + reference_mixed, reference_final_gain
    ).astype(jnp.bfloat16)
    vocab_start = lax.axis_index("vocab") * policy_head.shape[1]
    policy_logits, policy_max, policy_target = head_terms(
        policy_final, policy_head, targets, vocab_start
    )
    reference_logits, reference_max, reference_target = head_terms(
        reference_final, reference_head, targets, vocab_start
    )
    policy_top, reference_top = lax.pmax((policy_max, reference_max), "vocab")
    policy_local = jnp.sum(jnp.exp(policy_logits - policy_top[:, None]), axis=-1)
    reference_local = jnp.sum(jnp.exp(reference_logits - reference_top[:, None]), axis=-1)
    totals = lax.psum((policy_local, reference_local, policy_target, reference_target), "vocab")
    policy_score = totals[2] - (policy_top + jnp.log(totals[0]))
    reference_score = totals[3] - (reference_top + jnp.log(totals[1]))
    token_diff = policy_score - reference_score
    per_token = token_diff / length_of.astype(jnp.float32)
    partial_sums = jnp.sum(
        jnp.where(slot_of[:, None] == roll_ids[None, :], per_token[:, None], 0.0), axis=0
    )
    rollout_mean = partial_sums
    stride = 1
    while stride < seq_count:
        rollout_mean = rollout_mean + lax.ppermute(
            rollout_mean, "seq", [(i, i ^ stride) for i in range(seq_count)]
        )
        stride *= 2
    return (token_diff, rollout_mean)


def solution(mesh):
    return jax.shard_map(
        local,
        mesh=mesh,
        in_specs=(
            P("seq", None),
            P("seq", None),
            P("seq"),
            P(),
            P("seq"),
            P(),
            P(),
            P(),
            P(None, "vocab"),
            P(None, "vocab"),
            P(None, "vocab"),
            P(),
            P(),
            P("vocab", None),
            P(),
            P(None, "vocab"),
            P(None, "seq", "vocab"),
            P(None, "seq", "vocab"),
            P(),
            P(None, "vocab"),
            P(None, "vocab"),
            P(None, "vocab"),
            P(),
            P(),
            P("vocab", None),
            P(),
            P(None, "vocab"),
            P(None, "seq", "vocab"),
            P(None, "seq", "vocab"),
        ),
        out_specs=(P("seq"), P()),
        check_vma=False,
    )
```

```python
import jax
import jax.numpy as jnp
from jax import lax
from jax.sharding import PartitionSpec as P
from jax.experimental import pallas as pl
from jax.experimental.pallas import tpu as pltpu

HD = 128
BLOCK = 128


EPSILON = 1e-06
ROPE_BASE = 1000000.0
NEGATIVE_FILL = -1e30


def rms_scale(values, gain_row):
    values = values.astype(jnp.float32)
    return (
        values * lax.rsqrt(jnp.mean(values * values, axis=-1, keepdims=True) + EPSILON) * gain_row
    )


def rotate(values, positions):
    half_width = values.shape[-1] // 2
    frequency = ROPE_BASE ** (-2.0 * jnp.arange(half_width, dtype=jnp.float32) / values.shape[-1])
    angles = positions.astype(jnp.float32)[:, None] * frequency[None, :]
    cosine = jnp.cos(angles)
    sine_part = jnp.sin(angles)
    cosine = jnp.concatenate([cosine, cosine], axis=-1)[:, None, :]
    sine_part = jnp.concatenate([sine_part, sine_part], axis=-1)[:, None, :]
    turned = jnp.concatenate([-values[..., half_width:], values[..., :half_width]], axis=-1)
    return values * cosine + turned * sine_part


def lookup(member, lookup_table):
    return jnp.sum(jnp.where(member, lookup_table[None, :], 0), axis=1)


def project(
    hidden,
    input_gain,
    query_weight,
    key_weight,
    value_weight,
    query_gain,
    key_gain,
    prompt_keys,
    prompt_values,
    positions,
    rope_offset,
):
    tok_rows = hidden.shape[0]
    kv_local = key_weight.shape[1] // HD
    normed = rms_scale(hidden, input_gain).astype(jnp.bfloat16)
    query_rows = jnp.dot(normed, query_weight, preferred_element_type=jnp.float32).reshape(
        tok_rows, -1, HD
    )
    query_rows = rotate(rms_scale(query_rows, query_gain), positions + rope_offset).astype(
        jnp.bfloat16
    )
    key_rows = jnp.dot(normed, key_weight, preferred_element_type=jnp.float32).reshape(
        tok_rows, kv_local, HD
    )
    key_rows = (
        rotate(rms_scale(key_rows, key_gain), positions + rope_offset)
        .astype(jnp.bfloat16)
        .reshape(tok_rows, kv_local * HD)
    )
    value_rows = jnp.dot(normed, value_weight, preferred_element_type=jnp.float32).astype(
        jnp.bfloat16
    )
    key_block = jnp.concatenate([key_rows, prompt_keys.reshape(-1, kv_local * HD)], axis=0)
    value_block = jnp.concatenate([value_rows, prompt_values.reshape(-1, kv_local * HD)], axis=0)
    stacked = jnp.concatenate([key_block, value_block], axis=1)
    return (query_rows.reshape(tok_rows, kv_local, -1, HD), stacked)


def empty_state(query_rows):
    tok_rows, kv_local, group_size = (query_rows.shape[0], query_rows.shape[1], query_rows.shape[2])
    running_max = jnp.full((kv_local, group_size, tok_rows), NEGATIVE_FILL, jnp.float32)
    weight_sum = jnp.zeros((kv_local, group_size, tok_rows), jnp.float32)
    accumulated = jnp.zeros((tok_rows, kv_local, group_size, HD), jnp.float32)
    return (running_max, weight_sum, accumulated)


def update_state(model_state, query_rows, stacked, visible):
    running_max, weight_sum, accumulated = model_state
    half_columns = stacked.shape[1] // 2
    kv_local = query_rows.shape[1]
    key_part = stacked[:, :half_columns].reshape(-1, kv_local, HD)
    value_part = stacked[:, half_columns:].reshape(-1, kv_local, HD)
    scores = jnp.einsum(
        "qkgd,skd->kgqs", query_rows, key_part, preferred_element_type=jnp.float32
    ) * HD ** (-0.5)
    masked = jnp.where(visible[None, None], scores, NEGATIVE_FILL)
    new_max = jnp.maximum(running_max, jnp.max(masked, axis=-1))
    weights = jnp.where(visible[None, None], jnp.exp(scores - new_max[..., None]), 0.0)
    factor = jnp.exp(running_max - new_max)
    new_sum = weight_sum * factor + jnp.sum(weights, axis=-1)
    product = jnp.einsum(
        "kgqs,skd->qkgd",
        weights.astype(jnp.bfloat16),
        value_part,
        preferred_element_type=jnp.float32,
    )
    new_accumulated = accumulated * jnp.transpose(factor, (2, 0, 1))[..., None] + product
    return (new_max, new_sum, new_accumulated)


def attend(states, queries, pieces, query_tag, query_position, query_prompt):
    stacked_list = pieces[:-2]
    key_tag = pieces[-2]
    key_position = pieces[-1]
    visible = (key_tag[None, :] == query_tag[:, None]) & (
        key_position[None, :] <= query_position[:, None]
    ) | (key_tag[None, :] == -1 - query_prompt[:, None])

    def compute(current):
        updated = []
        for model_state, query_rows, stacked in zip(current, queries, stacked_list):
            updated.append(update_state(model_state, query_rows, stacked, visible))
        return tuple(updated)

    def unchanged(current):
        return current

    return lax.cond(jnp.any(visible), compute, unchanged, states)


def make_fold(queries, query_tag, query_position, query_prompt, shard_rows):

    def fold_pieces(states, pieces, start_row):
        rows_here = pieces[0].shape[0]
        shard_count = rows_here // shard_rows
        split_pieces = tuple(
            (
                member_piece.reshape((shard_count, shard_rows) + member_piece.shape[1:])
                for member_piece in pieces
            )
        )

        def scan_step(carry_states, piece_item):
            return (
                attend(carry_states, queries, piece_item, query_tag, query_position, query_prompt),
                None,
            )

        return lax.scan(scan_step, states, split_pieces)[0]

    return fold_pieces


Q_TILE = 512
K_TILE = 1024
CODE_STRIDE = 65536


def flash_kernel(flags_ref, q_ref, kv_ref, kcode_ref, qlo_ref, qhi_ref, out_ref, m_sc, l_sc, acc_sc):
    j = pl.program_id(1)

    @pl.when(j == 0)
    def _():
        m_sc[...] = jnp.full(m_sc.shape, NEGATIVE_FILL, jnp.float32)
        l_sc[...] = jnp.zeros(l_sc.shape, jnp.float32)
        acc_sc[...] = jnp.zeros(acc_sc.shape, jnp.float32)

    @pl.when(flags_ref[j] > 0)
    def _():
        kv = kv_ref[...]
        scores = lax.dot_general(
            q_ref[...], kv[:, :HD], (((1,), (1,)), ((), ())), preferred_element_type=jnp.float32
        ) * HD ** (-0.5)
        key_code = kcode_ref[...]
        visible = (key_code >= qlo_ref[...]) & (key_code <= qhi_ref[...])
        masked = jnp.where(visible, scores, NEGATIVE_FILL)
        old_max = m_sc[...]
        new_max = jnp.maximum(old_max, jnp.max(masked, axis=1, keepdims=True))
        weights = jnp.where(visible, jnp.exp(scores - new_max), 0.0)
        factor = jnp.exp(old_max - new_max)
        l_sc[...] = l_sc[...] * factor + jnp.sum(weights, axis=1, keepdims=True)
        acc_sc[...] = acc_sc[...] * factor + jnp.dot(
            weights.astype(jnp.bfloat16), kv[:, HD:], preferred_element_type=jnp.float32
        )
        m_sc[...] = new_max

    @pl.when(j == pl.num_programs(1) - 1)
    def _():
        out_ref[...] = (acc_sc[...] / l_sc[...]).astype(out_ref.dtype)


def flash_attend(flags, queries, stacked, key_code, query_low, query_high):
    q_rows = queries.shape[0]
    k_rows = stacked.shape[0]
    grid_spec = pltpu.PrefetchScalarGridSpec(
        num_scalar_prefetch=1,
        grid=(q_rows // Q_TILE, k_rows // K_TILE),
        in_specs=[
            pl.BlockSpec((Q_TILE, HD), lambda i, j, f: (i, 0)),
            pl.BlockSpec((K_TILE, 2 * HD), lambda i, j, f: (j, 0)),
            pl.BlockSpec((1, K_TILE), lambda i, j, f: (0, j)),
            pl.BlockSpec((Q_TILE, 1), lambda i, j, f: (i, 0)),
            pl.BlockSpec((Q_TILE, 1), lambda i, j, f: (i, 0)),
        ],
        out_specs=pl.BlockSpec((Q_TILE, HD), lambda i, j, f: (i, 0)),
        scratch_shapes=[
            pltpu.VMEM((Q_TILE, 1), jnp.float32),
            pltpu.VMEM((Q_TILE, 1), jnp.float32),
            pltpu.VMEM((Q_TILE, HD), jnp.float32),
        ],
    )
    return pl.pallas_call(
        flash_kernel,
        grid_spec=grid_spec,
        out_shape=jax.ShapeDtypeStruct((q_rows, HD), jnp.bfloat16),
        compiler_params=pltpu.CompilerParams(dimension_semantics=("arbitrary", "arbitrary")),
    )(flags, queries, stacked, key_code, query_low, query_high)


def exchange_sum(values, axis_name):
    count = lax.axis_size(axis_name)
    stride = 1
    while stride < count:
        received = lax.ppermute(values, axis_name, [(i, i ^ stride) for i in range(count)])
        values = (values.astype(jnp.float32) + received.astype(jnp.float32)).astype(values.dtype)
        stride *= 2
    return values


def tile_flags(key_code, query_low, query_high):
    seen = (key_code[None, :] >= query_low[:, None]) & (key_code[None, :] <= query_high[:, None])
    return jnp.any(seen.reshape(query_low.shape[0], -1, K_TILE), axis=(0, 2)).astype(jnp.int32)


def attend_model(query_rows, gathered, flags, key_code, query_low, query_high, out_weight):
    tok_rows, kv_local, group_size = query_rows.shape[:3]
    flat_query = jnp.transpose(query_rows, (1, 2, 0, 3)).reshape(-1, HD)
    tiled_low = jnp.tile(query_low, kv_local * group_size)[:, None]
    tiled_high = jnp.tile(query_high, kv_local * group_size)[:, None]
    attended = flash_attend(flags, flat_query, gathered, key_code[None, :], tiled_low, tiled_high)
    attended = jnp.transpose(attended.reshape(kv_local, group_size, tok_rows, HD), (2, 0, 1, 3))
    attended = attended.reshape(tok_rows, -1)
    return jnp.dot(attended, out_weight, preferred_element_type=jnp.float32)


def finish(model_state, out_weight):
    running_max, weight_sum, accumulated = model_state
    attended = accumulated / jnp.transpose(weight_sum, (2, 0, 1))[..., None]
    attended = attended.reshape(accumulated.shape[0], -1).astype(jnp.bfloat16)
    return jnp.dot(attended, out_weight, preferred_element_type=jnp.float32)


def head_terms(final_rows, head_weight, targets, vocab_start):
    logits = jnp.dot(final_rows, head_weight, preferred_element_type=jnp.float32)
    local_max = jnp.max(logits, axis=-1)
    word_ids = vocab_start + jnp.arange(logits.shape[1], dtype=jnp.int32)
    target_logit = jnp.sum(jnp.where(word_ids[None, :] == targets[:, None], logits, 0.0), axis=-1)
    return (logits, local_max, target_logit)


def local(
    policy_hidden,
    reference_hidden,
    targets,
    lengths,
    block_source,
    rollout_prompt,
    rollout_slot,
    policy_input_gain,
    policy_query_weight,
    policy_key_weight,
    policy_value_weight,
    policy_query_gain,
    policy_key_gain,
    policy_out_weight,
    policy_final_gain,
    policy_head,
    policy_prompt_keys,
    policy_prompt_values,
    reference_input_gain,
    reference_query_weight,
    reference_key_weight,
    reference_value_weight,
    reference_query_gain,
    reference_key_gain,
    reference_out_weight,
    reference_final_gain,
    reference_head,
    reference_prompt_keys,
    reference_prompt_values,
):
    tok_rows = policy_hidden.shape[0]
    roll_ids = jnp.arange(lengths.shape[0], dtype=jnp.int32)
    slot_ids = jnp.arange(tok_rows, dtype=jnp.int32)
    packed = jnp.repeat(block_source, BLOCK) * BLOCK + slot_ids % BLOCK
    end_points = jnp.cumsum(lengths)
    rollout = jnp.sum((packed[:, None] >= end_points[None, :]).astype(jnp.int32), axis=1)
    member = rollout[:, None] == roll_ids[None, :]
    position = packed - lookup(member, end_points - lengths)
    query_prompt = lookup(member, rollout_prompt)
    slot_of = lookup(member, rollout_slot)
    length_of = lookup(member, lengths)
    prompt_count = policy_prompt_keys.shape[0]
    prefix_local = policy_prompt_keys.shape[1]
    prompt_rows = prompt_count * prefix_local
    rope_offset = prefix_local * lax.axis_size("seq")
    prompt_ids = jnp.arange(prompt_rows, dtype=jnp.int32) // prefix_local
    seq_count = lax.axis_size("seq")
    shard_rows = tok_rows + prompt_rows
    policy_query, policy_stack = project(
        policy_hidden,
        policy_input_gain,
        policy_query_weight,
        policy_key_weight,
        policy_value_weight,
        policy_query_gain,
        policy_key_gain,
        policy_prompt_keys,
        policy_prompt_values,
        position,
        rope_offset,
    )
    reference_query, reference_stack = project(
        reference_hidden,
        reference_input_gain,
        reference_query_weight,
        reference_key_weight,
        reference_value_weight,
        reference_query_gain,
        reference_key_gain,
        reference_prompt_keys,
        reference_prompt_values,
        position,
        rope_offset,
    )
    pad_rows = prompt_rows
    carrier = jnp.zeros((pad_rows, policy_stack.shape[1]), jnp.bfloat16)
    carrier = carrier.at[0, : block_source.shape[0]].set(block_source.astype(jnp.bfloat16))
    policy_gathered = lax.all_gather(
        jnp.concatenate([policy_stack, carrier], axis=0), "seq", axis=0, tiled=True
    )
    policy_rows = policy_stack.shape[0] + pad_rows
    all_source = (
        policy_gathered.reshape(seq_count, policy_rows, -1)[:, policy_stack.shape[0], : block_source.shape[0]]
        .astype(jnp.int32)
        .reshape(-1)
    )
    all_ids = jnp.arange(tok_rows * seq_count, dtype=jnp.int32)
    all_packed = jnp.repeat(all_source, BLOCK) * BLOCK + all_ids % BLOCK
    all_rollout = jnp.sum((all_packed[:, None] >= end_points[None, :]).astype(jnp.int32), axis=1)
    all_member = all_rollout[:, None] == roll_ids[None, :]
    all_position = all_packed - lookup(all_member, end_points - lengths)
    owner = lookup(rollout_prompt[None, :] == jnp.arange(prompt_count, dtype=jnp.int32)[:, None], roll_ids)
    token_code = (all_rollout * CODE_STRIDE + all_position).reshape(seq_count, tok_rows)
    prompt_code = jnp.broadcast_to(owner[prompt_ids] * CODE_STRIDE - 1, (seq_count, prompt_rows))
    never_code = jnp.full((seq_count, pad_rows), -(1 << 30), jnp.int32)
    key_code = jnp.concatenate([token_code, prompt_code], axis=1).reshape(-1)
    policy_code = jnp.concatenate([token_code, prompt_code, never_code], axis=1).reshape(-1)
    query_low = rollout * CODE_STRIDE - 1
    query_high = rollout * CODE_STRIDE + position
    flags = tile_flags(key_code, query_low, query_high)
    policy_flags = tile_flags(policy_code, query_low, query_high)
    policy_part = attend_model(
        policy_query,
        policy_gathered,
        policy_flags,
        policy_code,
        query_low,
        query_high,
        policy_out_weight,
    )
    reference_part = attend_model(
        reference_query,
        lax.all_gather(reference_stack, "seq", axis=0, tiled=True),
        flags,
        key_code,
        query_low,
        query_high,
        reference_out_weight,
    )
    policy_summed = lax.psum(policy_part.astype(jnp.bfloat16), "vocab")
    policy_summed, reference_part = lax.optimization_barrier((policy_summed, reference_part))
    policy_mixed = policy_summed.astype(jnp.float32)
    reference_mixed = exchange_sum(reference_part.astype(jnp.bfloat16), "vocab").astype(jnp.float32)
    policy_final = rms_scale(
        policy_hidden.astype(jnp.float32) + policy_mixed, policy_final_gain
    ).astype(jnp.bfloat16)
    reference_final = rms_scale(
        reference_hidden.astype(jnp.float32) + reference_mixed, reference_final_gain
    ).astype(jnp.bfloat16)
    vocab_start = lax.axis_index("vocab") * policy_head.shape[1]
    policy_logits, policy_max, policy_target = head_terms(
        policy_final, policy_head, targets, vocab_start
    )
    reference_logits, reference_max, reference_target = head_terms(
        reference_final, reference_head, targets, vocab_start
    )
    policy_local = jnp.sum(jnp.exp(policy_logits - policy_max[:, None]), axis=-1)
    reference_local = jnp.sum(jnp.exp(reference_logits - reference_max[:, None]), axis=-1)
    terms = lax.all_gather(
        jnp.stack(
            [policy_max, reference_max, policy_local, reference_local, policy_target, reference_target]
        ),
        "vocab",
        axis=0,
    )
    policy_top = jnp.max(terms[:, 0], axis=0)
    reference_top = jnp.max(terms[:, 1], axis=0)
    policy_total = jnp.sum(terms[:, 2] * jnp.exp(terms[:, 0] - policy_top[None]), axis=0)
    reference_total = jnp.sum(terms[:, 3] * jnp.exp(terms[:, 1] - reference_top[None]), axis=0)
    policy_score = jnp.sum(terms[:, 4], axis=0) - (policy_top + jnp.log(policy_total))
    reference_score = jnp.sum(terms[:, 5], axis=0) - (reference_top + jnp.log(reference_total))
    token_diff = policy_score - reference_score
    per_token = token_diff / length_of.astype(jnp.float32)
    partial_sums = jnp.sum(
        jnp.where(slot_of[:, None] == roll_ids[None, :], per_token[:, None], 0.0), axis=0
    )
    rollout_mean = partial_sums
    stride = 1
    while stride < seq_count:
        rollout_mean = rollout_mean + lax.ppermute(
            rollout_mean, "seq", [(i, i ^ stride) for i in range(seq_count)]
        )
        stride *= 2
    return (token_diff, rollout_mean)


def solution(mesh):
    return jax.shard_map(
        local,
        mesh=mesh,
        in_specs=(
            P("seq", None),
            P("seq", None),
            P("seq"),
            P(),
            P("seq"),
            P(),
            P(),
            P(),
            P(None, "vocab"),
            P(None, "vocab"),
            P(None, "vocab"),
            P(),
            P(),
            P("vocab", None),
            P(),
            P(None, "vocab"),
            P(None, "seq", "vocab"),
            P(None, "seq", "vocab"),
            P(),
            P(None, "vocab"),
            P(None, "vocab"),
            P(None, "vocab"),
            P(),
            P(),
            P("vocab", None),
            P(),
            P(None, "vocab"),
            P(None, "seq", "vocab"),
            P(None, "seq", "vocab"),
        ),
        out_specs=(P("seq"), P()),
        check_vma=False,
    )
```

```python
import jax
import jax.numpy as jnp
from jax import lax
from jax.sharding import PartitionSpec as P
from jax.experimental import pallas as pl
from jax.experimental.pallas import tpu as pltpu

HD = 128
BLOCK = 128


EPSILON = 1e-06
ROPE_BASE = 1000000.0
NEGATIVE_FILL = -1e30


def rms_scale(values, gain_row):
    values = values.astype(jnp.float32)
    return (
        values * lax.rsqrt(jnp.mean(values * values, axis=-1, keepdims=True) + EPSILON) * gain_row
    )


def rotate(values, positions):
    half_width = values.shape[-1] // 2
    frequency = ROPE_BASE ** (-2.0 * jnp.arange(half_width, dtype=jnp.float32) / values.shape[-1])
    angles = positions.astype(jnp.float32)[:, None] * frequency[None, :]
    cosine = jnp.cos(angles)
    sine_part = jnp.sin(angles)
    cosine = jnp.concatenate([cosine, cosine], axis=-1)[:, None, :]
    sine_part = jnp.concatenate([sine_part, sine_part], axis=-1)[:, None, :]
    turned = jnp.concatenate([-values[..., half_width:], values[..., :half_width]], axis=-1)
    return values * cosine + turned * sine_part


def lookup(member, lookup_table):
    return jnp.sum(jnp.where(member, lookup_table[None, :], 0), axis=1)


def project(
    hidden,
    input_gain,
    query_weight,
    key_weight,
    value_weight,
    query_gain,
    key_gain,
    prompt_keys,
    prompt_values,
    positions,
    rope_offset,
):
    tok_rows = hidden.shape[0]
    kv_local = key_weight.shape[1] // HD
    normed = rms_scale(hidden, input_gain).astype(jnp.bfloat16)
    query_rows = jnp.dot(normed, query_weight, preferred_element_type=jnp.float32).reshape(
        tok_rows, -1, HD
    )
    query_rows = rotate(rms_scale(query_rows, query_gain), positions + rope_offset).astype(
        jnp.bfloat16
    )
    key_rows = jnp.dot(normed, key_weight, preferred_element_type=jnp.float32).reshape(
        tok_rows, kv_local, HD
    )
    key_rows = (
        rotate(rms_scale(key_rows, key_gain), positions + rope_offset)
        .astype(jnp.bfloat16)
        .reshape(tok_rows, kv_local * HD)
    )
    value_rows = jnp.dot(normed, value_weight, preferred_element_type=jnp.float32).astype(
        jnp.bfloat16
    )
    key_block = jnp.concatenate([key_rows, prompt_keys.reshape(-1, kv_local * HD)], axis=0)
    value_block = jnp.concatenate([value_rows, prompt_values.reshape(-1, kv_local * HD)], axis=0)
    stacked = jnp.concatenate([key_block, value_block], axis=1)
    return (query_rows.reshape(tok_rows, kv_local, -1, HD), stacked)


def empty_state(query_rows):
    tok_rows, kv_local, group_size = (query_rows.shape[0], query_rows.shape[1], query_rows.shape[2])
    running_max = jnp.full((kv_local, group_size, tok_rows), NEGATIVE_FILL, jnp.float32)
    weight_sum = jnp.zeros((kv_local, group_size, tok_rows), jnp.float32)
    accumulated = jnp.zeros((tok_rows, kv_local, group_size, HD), jnp.float32)
    return (running_max, weight_sum, accumulated)


def update_state(model_state, query_rows, stacked, visible):
    running_max, weight_sum, accumulated = model_state
    half_columns = stacked.shape[1] // 2
    kv_local = query_rows.shape[1]
    key_part = stacked[:, :half_columns].reshape(-1, kv_local, HD)
    value_part = stacked[:, half_columns:].reshape(-1, kv_local, HD)
    scores = jnp.einsum(
        "qkgd,skd->kgqs", query_rows, key_part, preferred_element_type=jnp.float32
    ) * HD ** (-0.5)
    masked = jnp.where(visible[None, None], scores, NEGATIVE_FILL)
    new_max = jnp.maximum(running_max, jnp.max(masked, axis=-1))
    weights = jnp.where(visible[None, None], jnp.exp(scores - new_max[..., None]), 0.0)
    factor = jnp.exp(running_max - new_max)
    new_sum = weight_sum * factor + jnp.sum(weights, axis=-1)
    product = jnp.einsum(
        "kgqs,skd->qkgd",
        weights.astype(jnp.bfloat16),
        value_part,
        preferred_element_type=jnp.float32,
    )
    new_accumulated = accumulated * jnp.transpose(factor, (2, 0, 1))[..., None] + product
    return (new_max, new_sum, new_accumulated)


def attend(states, queries, pieces, query_tag, query_position, query_prompt):
    stacked_list = pieces[:-2]
    key_tag = pieces[-2]
    key_position = pieces[-1]
    visible = (key_tag[None, :] == query_tag[:, None]) & (
        key_position[None, :] <= query_position[:, None]
    ) | (key_tag[None, :] == -1 - query_prompt[:, None])

    def compute(current):
        updated = []
        for model_state, query_rows, stacked in zip(current, queries, stacked_list):
            updated.append(update_state(model_state, query_rows, stacked, visible))
        return tuple(updated)

    def unchanged(current):
        return current

    return lax.cond(jnp.any(visible), compute, unchanged, states)


def make_fold(queries, query_tag, query_position, query_prompt, shard_rows):

    def fold_pieces(states, pieces, start_row):
        rows_here = pieces[0].shape[0]
        shard_count = rows_here // shard_rows
        split_pieces = tuple(
            (
                member_piece.reshape((shard_count, shard_rows) + member_piece.shape[1:])
                for member_piece in pieces
            )
        )

        def scan_step(carry_states, piece_item):
            return (
                attend(carry_states, queries, piece_item, query_tag, query_position, query_prompt),
                None,
            )

        return lax.scan(scan_step, states, split_pieces)[0]

    return fold_pieces


Q_TILE = 512
K_TILE = 1024
CODE_STRIDE = 65536


def flash_kernel(flags_ref, q_ref, kv_ref, kcode_ref, qlo_ref, qhi_ref, out_ref, m_sc, l_sc, acc_sc):
    j = pl.program_id(1)

    @pl.when(j == 0)
    def _():
        m_sc[...] = jnp.full(m_sc.shape, NEGATIVE_FILL, jnp.float32)
        l_sc[...] = jnp.zeros(l_sc.shape, jnp.float32)
        acc_sc[...] = jnp.zeros(acc_sc.shape, jnp.float32)

    @pl.when(flags_ref[j] > 0)
    def _():
        kv = kv_ref[...]
        scores = lax.dot_general(
            q_ref[...], kv[:, :HD], (((1,), (1,)), ((), ())), preferred_element_type=jnp.float32
        ) * HD ** (-0.5)
        key_code = kcode_ref[...]
        visible = (key_code >= qlo_ref[...]) & (key_code <= qhi_ref[...])
        masked = jnp.where(visible, scores, NEGATIVE_FILL)
        old_max = m_sc[...]
        new_max = jnp.maximum(old_max, jnp.max(masked, axis=1, keepdims=True))
        weights = jnp.where(visible, jnp.exp(scores - new_max), 0.0)
        factor = jnp.exp(old_max - new_max)
        l_sc[...] = l_sc[...] * factor + jnp.sum(weights, axis=1, keepdims=True)
        acc_sc[...] = acc_sc[...] * factor + jnp.dot(
            weights.astype(jnp.bfloat16), kv[:, HD:], preferred_element_type=jnp.float32
        )
        m_sc[...] = new_max

    @pl.when(j == pl.num_programs(1) - 1)
    def _():
        out_ref[...] = (acc_sc[...] / l_sc[...]).astype(out_ref.dtype)


def flash_attend(flags, queries, stacked, key_code, query_low, query_high):
    q_rows = queries.shape[0]
    k_rows = stacked.shape[0]
    grid_spec = pltpu.PrefetchScalarGridSpec(
        num_scalar_prefetch=1,
        grid=(q_rows // Q_TILE, k_rows // K_TILE),
        in_specs=[
            pl.BlockSpec((Q_TILE, HD), lambda i, j, f: (i, 0)),
            pl.BlockSpec((K_TILE, 2 * HD), lambda i, j, f: (j, 0)),
            pl.BlockSpec((1, K_TILE), lambda i, j, f: (0, j)),
            pl.BlockSpec((Q_TILE, 1), lambda i, j, f: (i, 0)),
            pl.BlockSpec((Q_TILE, 1), lambda i, j, f: (i, 0)),
        ],
        out_specs=pl.BlockSpec((Q_TILE, HD), lambda i, j, f: (i, 0)),
        scratch_shapes=[
            pltpu.VMEM((Q_TILE, 1), jnp.float32),
            pltpu.VMEM((Q_TILE, 1), jnp.float32),
            pltpu.VMEM((Q_TILE, HD), jnp.float32),
        ],
    )
    return pl.pallas_call(
        flash_kernel,
        grid_spec=grid_spec,
        out_shape=jax.ShapeDtypeStruct((q_rows, HD), jnp.bfloat16),
        compiler_params=pltpu.CompilerParams(dimension_semantics=("arbitrary", "arbitrary")),
    )(flags, queries, stacked, key_code, query_low, query_high)


def exchange_sum(values, axis_name):
    count = lax.axis_size(axis_name)
    stride = 1
    while stride < count:
        received = lax.ppermute(values, axis_name, [(i, i ^ stride) for i in range(count)])
        values = (values.astype(jnp.float32) + received.astype(jnp.float32)).astype(values.dtype)
        stride *= 2
    return values


def tile_flags(key_code, query_low, query_high):
    seen = (key_code[None, :] >= query_low[:, None]) & (key_code[None, :] <= query_high[:, None])
    return jnp.any(seen.reshape(query_low.shape[0], -1, K_TILE), axis=(0, 2)).astype(jnp.int32)


def attend_model(query_rows, gathered, flags, key_code, query_low, query_high, out_weight):
    tok_rows, kv_local, group_size = query_rows.shape[:3]
    flat_query = jnp.transpose(query_rows, (1, 2, 0, 3)).reshape(-1, HD)
    tiled_low = jnp.tile(query_low, kv_local * group_size)[:, None]
    tiled_high = jnp.tile(query_high, kv_local * group_size)[:, None]
    attended = flash_attend(flags, flat_query, gathered, key_code[None, :], tiled_low, tiled_high)
    attended = jnp.transpose(attended.reshape(kv_local, group_size, tok_rows, HD), (2, 0, 1, 3))
    attended = attended.reshape(tok_rows, -1)
    return jnp.dot(attended, out_weight, preferred_element_type=jnp.float32)


def finish(model_state, out_weight):
    running_max, weight_sum, accumulated = model_state
    attended = accumulated / jnp.transpose(weight_sum, (2, 0, 1))[..., None]
    attended = attended.reshape(accumulated.shape[0], -1).astype(jnp.bfloat16)
    return jnp.dot(attended, out_weight, preferred_element_type=jnp.float32)


def head_terms(final_rows, head_weight, targets, vocab_start):
    logits = jnp.dot(final_rows, head_weight, preferred_element_type=jnp.float32)
    local_max = jnp.max(logits, axis=-1)
    word_ids = vocab_start + jnp.arange(logits.shape[1], dtype=jnp.int32)
    target_logit = jnp.sum(jnp.where(word_ids[None, :] == targets[:, None], logits, 0.0), axis=-1)
    return (logits, local_max, target_logit)


def local(
    policy_hidden,
    reference_hidden,
    targets,
    lengths,
    block_source,
    rollout_prompt,
    rollout_slot,
    policy_input_gain,
    policy_query_weight,
    policy_key_weight,
    policy_value_weight,
    policy_query_gain,
    policy_key_gain,
    policy_out_weight,
    policy_final_gain,
    policy_head,
    policy_prompt_keys,
    policy_prompt_values,
    reference_input_gain,
    reference_query_weight,
    reference_key_weight,
    reference_value_weight,
    reference_query_gain,
    reference_key_gain,
    reference_out_weight,
    reference_final_gain,
    reference_head,
    reference_prompt_keys,
    reference_prompt_values,
):
    tok_rows = policy_hidden.shape[0]
    roll_ids = jnp.arange(lengths.shape[0], dtype=jnp.int32)
    slot_ids = jnp.arange(tok_rows, dtype=jnp.int32)
    packed = jnp.repeat(block_source, BLOCK) * BLOCK + slot_ids % BLOCK
    end_points = jnp.cumsum(lengths)
    rollout = jnp.sum((packed[:, None] >= end_points[None, :]).astype(jnp.int32), axis=1)
    member = rollout[:, None] == roll_ids[None, :]
    position = packed - lookup(member, end_points - lengths)
    query_prompt = lookup(member, rollout_prompt)
    slot_of = lookup(member, rollout_slot)
    length_of = lookup(member, lengths)
    prompt_count = policy_prompt_keys.shape[0]
    prefix_local = policy_prompt_keys.shape[1]
    prompt_rows = prompt_count * prefix_local
    rope_offset = prefix_local * lax.axis_size("seq")
    prompt_ids = jnp.arange(prompt_rows, dtype=jnp.int32) // prefix_local
    seq_count = lax.axis_size("seq")
    shard_rows = tok_rows + prompt_rows
    policy_query, policy_stack = project(
        policy_hidden,
        policy_input_gain,
        policy_query_weight,
        policy_key_weight,
        policy_value_weight,
        policy_query_gain,
        policy_key_gain,
        policy_prompt_keys,
        policy_prompt_values,
        position,
        rope_offset,
    )
    reference_query, reference_stack = project(
        reference_hidden,
        reference_input_gain,
        reference_query_weight,
        reference_key_weight,
        reference_value_weight,
        reference_query_gain,
        reference_key_gain,
        reference_prompt_keys,
        reference_prompt_values,
        position,
        rope_offset,
    )
    pad_rows = prompt_rows
    carrier = jnp.zeros((pad_rows, policy_stack.shape[1]), jnp.bfloat16)
    carrier = carrier.at[0, : block_source.shape[0]].set(block_source.astype(jnp.bfloat16))
    policy_gathered = lax.all_gather(
        jnp.concatenate([policy_stack, carrier], axis=0), "seq", axis=0, tiled=True
    )
    policy_rows = policy_stack.shape[0] + pad_rows
    all_source = (
        policy_gathered.reshape(seq_count, policy_rows, -1)[:, policy_stack.shape[0], : block_source.shape[0]]
        .astype(jnp.int32)
        .reshape(-1)
    )
    all_ids = jnp.arange(tok_rows * seq_count, dtype=jnp.int32)
    all_packed = jnp.repeat(all_source, BLOCK) * BLOCK + all_ids % BLOCK
    all_rollout = jnp.sum((all_packed[:, None] >= end_points[None, :]).astype(jnp.int32), axis=1)
    all_member = all_rollout[:, None] == roll_ids[None, :]
    all_position = all_packed - lookup(all_member, end_points - lengths)
    owner = lookup(rollout_prompt[None, :] == jnp.arange(prompt_count, dtype=jnp.int32)[:, None], roll_ids)
    token_code = (all_rollout * CODE_STRIDE + all_position).reshape(seq_count, tok_rows)
    prompt_code = jnp.broadcast_to(owner[prompt_ids] * CODE_STRIDE - 1, (seq_count, prompt_rows))
    never_code = jnp.full((seq_count, pad_rows), -(1 << 30), jnp.int32)
    key_code = jnp.concatenate([token_code, prompt_code], axis=1).reshape(-1)
    policy_code = jnp.concatenate([token_code, prompt_code, never_code], axis=1).reshape(-1)
    query_low = rollout * CODE_STRIDE - 1
    query_high = rollout * CODE_STRIDE + position
    flags = tile_flags(key_code, query_low, query_high)
    policy_flags = tile_flags(policy_code, query_low, query_high)
    policy_part = attend_model(
        policy_query,
        policy_gathered,
        policy_flags,
        policy_code,
        query_low,
        query_high,
        policy_out_weight,
    )
    reference_part = attend_model(
        reference_query,
        lax.all_gather(reference_stack, "seq", axis=0, tiled=True),
        flags,
        key_code,
        query_low,
        query_high,
        reference_out_weight,
    )
    policy_summed = lax.psum(policy_part.astype(jnp.bfloat16), "vocab")
    policy_summed, reference_part = lax.optimization_barrier((policy_summed, reference_part))
    policy_mixed = policy_summed.astype(jnp.float32)
    reference_mixed = exchange_sum(reference_part.astype(jnp.bfloat16), "vocab").astype(jnp.float32)
    policy_final = rms_scale(
        policy_hidden.astype(jnp.float32) + policy_mixed, policy_final_gain
    ).astype(jnp.bfloat16)
    reference_final = rms_scale(
        reference_hidden.astype(jnp.float32) + reference_mixed, reference_final_gain
    ).astype(jnp.bfloat16)
    vocab_start = lax.axis_index("vocab") * policy_head.shape[1]
    policy_logits, policy_max, policy_target = head_terms(
        policy_final, policy_head, targets, vocab_start
    )
    reference_logits, reference_max, reference_target = head_terms(
        reference_final, reference_head, targets, vocab_start
    )
    policy_local = jnp.sum(jnp.exp(policy_logits - policy_max[:, None]), axis=-1)
    reference_local = jnp.sum(jnp.exp(reference_logits - reference_max[:, None]), axis=-1)
    terms = lax.all_gather(
        jnp.stack(
            [policy_max, reference_max, policy_local, reference_local, policy_target, reference_target]
        ),
        "vocab",
        axis=0,
    )
    policy_top = jnp.max(terms[:, 0], axis=0)
    reference_top = jnp.max(terms[:, 1], axis=0)
    policy_total = jnp.sum(terms[:, 2] * jnp.exp(terms[:, 0] - policy_top[None]), axis=0)
    reference_total = jnp.sum(terms[:, 3] * jnp.exp(terms[:, 1] - reference_top[None]), axis=0)
    policy_score = jnp.sum(terms[:, 4], axis=0) - (policy_top + jnp.log(policy_total))
    reference_score = jnp.sum(terms[:, 5], axis=0) - (reference_top + jnp.log(reference_total))
    token_diff = policy_score - reference_score
    per_token = token_diff / length_of.astype(jnp.float32)
    partial_sums = jnp.sum(
        jnp.where(slot_of[:, None] == roll_ids[None, :], per_token[:, None], 0.0), axis=0
    )
    rollout_mean = partial_sums
    stride = 1
    while stride < seq_count:
        radix = 4 if seq_count % (stride * 4) == 0 else 2
        digit = (lax.axis_index("seq") // stride) % radix
        slots = [jnp.where(digit == k, rollout_mean, 0.0) for k in range(radix)]
        for offset in range(1, radix):
            pairs = [
                (i, i + (((i // stride) % radix + offset) % radix - (i // stride) % radix) * stride)
                for i in range(seq_count)
            ]
            received = lax.ppermute(rollout_mean, "seq", pairs)
            source = (digit - offset) % radix
            slots = [slots[k] + jnp.where(source == k, received, 0.0) for k in range(radix)]
        if radix == 4:
            rollout_mean = (slots[0] + slots[1]) + (slots[2] + slots[3])
        else:
            rollout_mean = slots[0] + slots[1]
        stride *= radix
    return (token_diff, rollout_mean)


def solution(mesh):
    return jax.shard_map(
        local,
        mesh=mesh,
        in_specs=(
            P("seq", None),
            P("seq", None),
            P("seq"),
            P(),
            P("seq"),
            P(),
            P(),
            P(),
            P(None, "vocab"),
            P(None, "vocab"),
            P(None, "vocab"),
            P(),
            P(),
            P("vocab", None),
            P(),
            P(None, "vocab"),
            P(None, "seq", "vocab"),
            P(None, "seq", "vocab"),
            P(),
            P(None, "vocab"),
            P(None, "vocab"),
            P(None, "vocab"),
            P(),
            P(),
            P("vocab", None),
            P(),
            P(None, "vocab"),
            P(None, "seq", "vocab"),
            P(None, "seq", "vocab"),
        ),
        out_specs=(P("seq"), P()),
        check_vma=False,
    )
```

```python
import jax
import jax.numpy as jnp
from jax import lax
from jax.sharding import PartitionSpec as P
from jax.experimental import pallas as pl
from jax.experimental.pallas import tpu as pltpu

HD = 128
BLOCK = 128


EPSILON = 1e-06
ROPE_BASE = 1000000.0
NEGATIVE_FILL = -1e30


def rms_scale(values, gain_row):
    values = values.astype(jnp.float32)
    return (
        values * lax.rsqrt(jnp.mean(values * values, axis=-1, keepdims=True) + EPSILON) * gain_row
    )


def rotate(values, positions):
    half_width = values.shape[-1] // 2
    frequency = ROPE_BASE ** (-2.0 * jnp.arange(half_width, dtype=jnp.float32) / values.shape[-1])
    angles = positions.astype(jnp.float32)[:, None] * frequency[None, :]
    cosine = jnp.cos(angles)
    sine_part = jnp.sin(angles)
    cosine = jnp.concatenate([cosine, cosine], axis=-1)[:, None, :]
    sine_part = jnp.concatenate([sine_part, sine_part], axis=-1)[:, None, :]
    turned = jnp.concatenate([-values[..., half_width:], values[..., :half_width]], axis=-1)
    return values * cosine + turned * sine_part


def lookup(member, lookup_table):
    return jnp.sum(jnp.where(member, lookup_table[None, :], 0), axis=1)


def project(
    hidden,
    input_gain,
    query_weight,
    key_weight,
    value_weight,
    query_gain,
    key_gain,
    prompt_keys,
    prompt_values,
    positions,
    rope_offset,
):
    tok_rows = hidden.shape[0]
    kv_local = key_weight.shape[1] // HD
    normed = rms_scale(hidden, input_gain).astype(jnp.bfloat16)
    query_rows = jnp.dot(normed, query_weight, preferred_element_type=jnp.float32).reshape(
        tok_rows, -1, HD
    )
    query_rows = rotate(rms_scale(query_rows, query_gain), positions + rope_offset).astype(
        jnp.bfloat16
    )
    key_rows = jnp.dot(normed, key_weight, preferred_element_type=jnp.float32).reshape(
        tok_rows, kv_local, HD
    )
    key_rows = (
        rotate(rms_scale(key_rows, key_gain), positions + rope_offset)
        .astype(jnp.bfloat16)
        .reshape(tok_rows, kv_local * HD)
    )
    value_rows = jnp.dot(normed, value_weight, preferred_element_type=jnp.float32).astype(
        jnp.bfloat16
    )
    key_block = jnp.concatenate([key_rows, prompt_keys.reshape(-1, kv_local * HD)], axis=0)
    value_block = jnp.concatenate([value_rows, prompt_values.reshape(-1, kv_local * HD)], axis=0)
    stacked = jnp.concatenate([key_block, value_block], axis=1)
    return (query_rows.reshape(tok_rows, kv_local, -1, HD), stacked)


def empty_state(query_rows):
    tok_rows, kv_local, group_size = (query_rows.shape[0], query_rows.shape[1], query_rows.shape[2])
    running_max = jnp.full((kv_local, group_size, tok_rows), NEGATIVE_FILL, jnp.float32)
    weight_sum = jnp.zeros((kv_local, group_size, tok_rows), jnp.float32)
    accumulated = jnp.zeros((tok_rows, kv_local, group_size, HD), jnp.float32)
    return (running_max, weight_sum, accumulated)


def update_state(model_state, query_rows, stacked, visible):
    running_max, weight_sum, accumulated = model_state
    half_columns = stacked.shape[1] // 2
    kv_local = query_rows.shape[1]
    key_part = stacked[:, :half_columns].reshape(-1, kv_local, HD)
    value_part = stacked[:, half_columns:].reshape(-1, kv_local, HD)
    scores = jnp.einsum(
        "qkgd,skd->kgqs", query_rows, key_part, preferred_element_type=jnp.float32
    ) * HD ** (-0.5)
    masked = jnp.where(visible[None, None], scores, NEGATIVE_FILL)
    new_max = jnp.maximum(running_max, jnp.max(masked, axis=-1))
    weights = jnp.where(visible[None, None], jnp.exp(scores - new_max[..., None]), 0.0)
    factor = jnp.exp(running_max - new_max)
    new_sum = weight_sum * factor + jnp.sum(weights, axis=-1)
    product = jnp.einsum(
        "kgqs,skd->qkgd",
        weights.astype(jnp.bfloat16),
        value_part,
        preferred_element_type=jnp.float32,
    )
    new_accumulated = accumulated * jnp.transpose(factor, (2, 0, 1))[..., None] + product
    return (new_max, new_sum, new_accumulated)


def attend(states, queries, pieces, query_tag, query_position, query_prompt):
    stacked_list = pieces[:-2]
    key_tag = pieces[-2]
    key_position = pieces[-1]
    visible = (key_tag[None, :] == query_tag[:, None]) & (
        key_position[None, :] <= query_position[:, None]
    ) | (key_tag[None, :] == -1 - query_prompt[:, None])

    def compute(current):
        updated = []
        for model_state, query_rows, stacked in zip(current, queries, stacked_list):
            updated.append(update_state(model_state, query_rows, stacked, visible))
        return tuple(updated)

    def unchanged(current):
        return current

    return lax.cond(jnp.any(visible), compute, unchanged, states)


def make_fold(queries, query_tag, query_position, query_prompt, shard_rows):

    def fold_pieces(states, pieces, start_row):
        rows_here = pieces[0].shape[0]
        shard_count = rows_here // shard_rows
        split_pieces = tuple(
            (
                member_piece.reshape((shard_count, shard_rows) + member_piece.shape[1:])
                for member_piece in pieces
            )
        )

        def scan_step(carry_states, piece_item):
            return (
                attend(carry_states, queries, piece_item, query_tag, query_position, query_prompt),
                None,
            )

        return lax.scan(scan_step, states, split_pieces)[0]

    return fold_pieces


Q_TILE = 1024
K_TILE = 1024
CODE_STRIDE = 65536


def flash_kernel(flags_ref, q_ref, kv_ref, kcode_ref, qlo_ref, qhi_ref, out_ref, m_sc, l_sc, acc_sc):
    j = pl.program_id(1)

    @pl.when(j == 0)
    def _():
        m_sc[...] = jnp.full(m_sc.shape, NEGATIVE_FILL, jnp.float32)
        l_sc[...] = jnp.zeros(l_sc.shape, jnp.float32)
        acc_sc[...] = jnp.zeros(acc_sc.shape, jnp.float32)

    @pl.when(flags_ref[j] > 0)
    def _():
        kv = kv_ref[...]
        scores = lax.dot_general(
            q_ref[...], kv[:, :HD], (((1,), (1,)), ((), ())), preferred_element_type=jnp.float32
        ) * HD ** (-0.5)
        key_code = kcode_ref[...]
        visible = (key_code >= qlo_ref[...]) & (key_code <= qhi_ref[...])
        masked = jnp.where(visible, scores, NEGATIVE_FILL)
        old_max = m_sc[...]
        new_max = jnp.maximum(old_max, jnp.max(masked, axis=1, keepdims=True))
        weights = jnp.where(visible, jnp.exp(scores - new_max), 0.0)
        factor = jnp.exp(old_max - new_max)
        l_sc[...] = l_sc[...] * factor + jnp.sum(weights, axis=1, keepdims=True)
        acc_sc[...] = acc_sc[...] * factor + jnp.dot(
            weights.astype(jnp.bfloat16), kv[:, HD:], preferred_element_type=jnp.float32
        )
        m_sc[...] = new_max

    @pl.when(j == pl.num_programs(1) - 1)
    def _():
        out_ref[...] = (acc_sc[...] / l_sc[...]).astype(out_ref.dtype)


def flash_attend(flags, queries, stacked, key_code, query_low, query_high):
    q_rows = queries.shape[0]
    k_rows = stacked.shape[0]
    grid_spec = pltpu.PrefetchScalarGridSpec(
        num_scalar_prefetch=1,
        grid=(q_rows // Q_TILE, k_rows // K_TILE),
        in_specs=[
            pl.BlockSpec((Q_TILE, HD), lambda i, j, f: (i, 0)),
            pl.BlockSpec((K_TILE, 2 * HD), lambda i, j, f: (j, 0)),
            pl.BlockSpec((1, K_TILE), lambda i, j, f: (0, j)),
            pl.BlockSpec((Q_TILE, 1), lambda i, j, f: (i, 0)),
            pl.BlockSpec((Q_TILE, 1), lambda i, j, f: (i, 0)),
        ],
        out_specs=pl.BlockSpec((Q_TILE, HD), lambda i, j, f: (i, 0)),
        scratch_shapes=[
            pltpu.VMEM((Q_TILE, 1), jnp.float32),
            pltpu.VMEM((Q_TILE, 1), jnp.float32),
            pltpu.VMEM((Q_TILE, HD), jnp.float32),
        ],
    )
    return pl.pallas_call(
        flash_kernel,
        grid_spec=grid_spec,
        out_shape=jax.ShapeDtypeStruct((q_rows, HD), jnp.bfloat16),
        compiler_params=pltpu.CompilerParams(dimension_semantics=("arbitrary", "arbitrary")),
    )(flags, queries, stacked, key_code, query_low, query_high)


def exchange_sum(values, axis_name):
    count = lax.axis_size(axis_name)
    stride = 1
    while stride < count:
        received = lax.ppermute(values, axis_name, [(i, i ^ stride) for i in range(count)])
        values = (values.astype(jnp.float32) + received.astype(jnp.float32)).astype(values.dtype)
        stride *= 2
    return values


def tile_flags(key_code, query_low, query_high):
    seen = (key_code[None, :] >= query_low[:, None]) & (key_code[None, :] <= query_high[:, None])
    return jnp.any(seen.reshape(query_low.shape[0], -1, K_TILE), axis=(0, 2)).astype(jnp.int32)


def attend_model(query_rows, gathered, flags, key_code, query_low, query_high, out_weight):
    tok_rows, kv_local, group_size = query_rows.shape[:3]
    flat_query = jnp.transpose(query_rows, (1, 2, 0, 3)).reshape(-1, HD)
    tiled_low = jnp.tile(query_low, kv_local * group_size)[:, None]
    tiled_high = jnp.tile(query_high, kv_local * group_size)[:, None]
    attended = flash_attend(flags, flat_query, gathered, key_code[None, :], tiled_low, tiled_high)
    attended = jnp.transpose(attended.reshape(kv_local, group_size, tok_rows, HD), (2, 0, 1, 3))
    attended = attended.reshape(tok_rows, -1)
    return jnp.dot(attended, out_weight, preferred_element_type=jnp.float32)


def finish(model_state, out_weight):
    running_max, weight_sum, accumulated = model_state
    attended = accumulated / jnp.transpose(weight_sum, (2, 0, 1))[..., None]
    attended = attended.reshape(accumulated.shape[0], -1).astype(jnp.bfloat16)
    return jnp.dot(attended, out_weight, preferred_element_type=jnp.float32)


def head_terms(final_rows, head_weight, targets, vocab_start):
    logits = jnp.dot(final_rows, head_weight, preferred_element_type=jnp.float32)
    local_max = jnp.max(logits, axis=-1)
    word_ids = vocab_start + jnp.arange(logits.shape[1], dtype=jnp.int32)
    target_logit = jnp.sum(jnp.where(word_ids[None, :] == targets[:, None], logits, 0.0), axis=-1)
    return (logits, local_max, target_logit)


def local(
    policy_hidden,
    reference_hidden,
    targets,
    lengths,
    block_source,
    rollout_prompt,
    rollout_slot,
    policy_input_gain,
    policy_query_weight,
    policy_key_weight,
    policy_value_weight,
    policy_query_gain,
    policy_key_gain,
    policy_out_weight,
    policy_final_gain,
    policy_head,
    policy_prompt_keys,
    policy_prompt_values,
    reference_input_gain,
    reference_query_weight,
    reference_key_weight,
    reference_value_weight,
    reference_query_gain,
    reference_key_gain,
    reference_out_weight,
    reference_final_gain,
    reference_head,
    reference_prompt_keys,
    reference_prompt_values,
):
    tok_rows = policy_hidden.shape[0]
    roll_ids = jnp.arange(lengths.shape[0], dtype=jnp.int32)
    slot_ids = jnp.arange(tok_rows, dtype=jnp.int32)
    packed = jnp.repeat(block_source, BLOCK) * BLOCK + slot_ids % BLOCK
    end_points = jnp.cumsum(lengths)
    rollout = jnp.sum((packed[:, None] >= end_points[None, :]).astype(jnp.int32), axis=1)
    member = rollout[:, None] == roll_ids[None, :]
    position = packed - lookup(member, end_points - lengths)
    query_prompt = lookup(member, rollout_prompt)
    slot_of = lookup(member, rollout_slot)
    length_of = lookup(member, lengths)
    prompt_count = policy_prompt_keys.shape[0]
    prefix_local = policy_prompt_keys.shape[1]
    prompt_rows = prompt_count * prefix_local
    rope_offset = prefix_local * lax.axis_size("seq")
    prompt_ids = jnp.arange(prompt_rows, dtype=jnp.int32) // prefix_local
    seq_count = lax.axis_size("seq")
    shard_rows = tok_rows + prompt_rows
    policy_query, policy_stack = project(
        policy_hidden,
        policy_input_gain,
        policy_query_weight,
        policy_key_weight,
        policy_value_weight,
        policy_query_gain,
        policy_key_gain,
        policy_prompt_keys,
        policy_prompt_values,
        position,
        rope_offset,
    )
    reference_query, reference_stack = project(
        reference_hidden,
        reference_input_gain,
        reference_query_weight,
        reference_key_weight,
        reference_value_weight,
        reference_query_gain,
        reference_key_gain,
        reference_prompt_keys,
        reference_prompt_values,
        position,
        rope_offset,
    )
    pad_rows = prompt_rows
    carrier = jnp.zeros((pad_rows, policy_stack.shape[1]), jnp.bfloat16)
    carrier = carrier.at[0, : block_source.shape[0]].set(block_source.astype(jnp.bfloat16))
    policy_gathered = lax.all_gather(
        jnp.concatenate([policy_stack, carrier], axis=0), "seq", axis=0, tiled=True
    )
    policy_rows = policy_stack.shape[0] + pad_rows
    all_source = (
        policy_gathered.reshape(seq_count, policy_rows, -1)[:, policy_stack.shape[0], : block_source.shape[0]]
        .astype(jnp.int32)
        .reshape(-1)
    )
    all_ids = jnp.arange(tok_rows * seq_count, dtype=jnp.int32)
    all_packed = jnp.repeat(all_source, BLOCK) * BLOCK + all_ids % BLOCK
    all_rollout = jnp.sum((all_packed[:, None] >= end_points[None, :]).astype(jnp.int32), axis=1)
    all_member = all_rollout[:, None] == roll_ids[None, :]
    all_position = all_packed - lookup(all_member, end_points - lengths)
    owner = lookup(rollout_prompt[None, :] == jnp.arange(prompt_count, dtype=jnp.int32)[:, None], roll_ids)
    token_code = (all_rollout * CODE_STRIDE + all_position).reshape(seq_count, tok_rows)
    prompt_code = jnp.broadcast_to(owner[prompt_ids] * CODE_STRIDE - 1, (seq_count, prompt_rows))
    never_code = jnp.full((seq_count, pad_rows), -(1 << 30), jnp.int32)
    key_code = jnp.concatenate([token_code, prompt_code], axis=1).reshape(-1)
    policy_code = jnp.concatenate([token_code, prompt_code, never_code], axis=1).reshape(-1)
    query_low = rollout * CODE_STRIDE - 1
    query_high = rollout * CODE_STRIDE + position
    flags = tile_flags(key_code, query_low, query_high)
    policy_flags = tile_flags(policy_code, query_low, query_high)
    policy_part = attend_model(
        policy_query,
        policy_gathered,
        policy_flags,
        policy_code,
        query_low,
        query_high,
        policy_out_weight,
    )
    reference_part = attend_model(
        reference_query,
        lax.all_gather(reference_stack, "seq", axis=0, tiled=True),
        flags,
        key_code,
        query_low,
        query_high,
        reference_out_weight,
    )
    policy_summed = lax.psum(policy_part.astype(jnp.bfloat16), "vocab")
    policy_summed, reference_part = lax.optimization_barrier((policy_summed, reference_part))
    policy_mixed = policy_summed.astype(jnp.float32)
    reference_mixed = exchange_sum(reference_part.astype(jnp.bfloat16), "vocab").astype(jnp.float32)
    policy_final = rms_scale(
        policy_hidden.astype(jnp.float32) + policy_mixed, policy_final_gain
    ).astype(jnp.bfloat16)
    reference_final = rms_scale(
        reference_hidden.astype(jnp.float32) + reference_mixed, reference_final_gain
    ).astype(jnp.bfloat16)
    vocab_start = lax.axis_index("vocab") * policy_head.shape[1]
    policy_logits, policy_max, policy_target = head_terms(
        policy_final, policy_head, targets, vocab_start
    )
    reference_logits, reference_max, reference_target = head_terms(
        reference_final, reference_head, targets, vocab_start
    )
    policy_local = jnp.sum(jnp.exp(policy_logits - policy_max[:, None]), axis=-1)
    reference_local = jnp.sum(jnp.exp(reference_logits - reference_max[:, None]), axis=-1)
    terms = lax.all_gather(
        jnp.stack(
            [policy_max, reference_max, policy_local, reference_local, policy_target, reference_target]
        ),
        "vocab",
        axis=0,
    )
    policy_top = jnp.max(terms[:, 0], axis=0)
    reference_top = jnp.max(terms[:, 1], axis=0)
    policy_total = jnp.sum(terms[:, 2] * jnp.exp(terms[:, 0] - policy_top[None]), axis=0)
    reference_total = jnp.sum(terms[:, 3] * jnp.exp(terms[:, 1] - reference_top[None]), axis=0)
    policy_score = jnp.sum(terms[:, 4], axis=0) - (policy_top + jnp.log(policy_total))
    reference_score = jnp.sum(terms[:, 5], axis=0) - (reference_top + jnp.log(reference_total))
    token_diff = policy_score - reference_score
    per_token = token_diff / length_of.astype(jnp.float32)
    partial_sums = jnp.sum(
        jnp.where(slot_of[:, None] == roll_ids[None, :], per_token[:, None], 0.0), axis=0
    )
    rollout_mean = partial_sums
    stride = 1
    while stride < seq_count:
        radix = 4 if seq_count % (stride * 4) == 0 else 2
        digit = (lax.axis_index("seq") // stride) % radix
        slots = [jnp.where(digit == k, rollout_mean, 0.0) for k in range(radix)]
        for offset in range(1, radix):
            pairs = [
                (i, i + (((i // stride) % radix + offset) % radix - (i // stride) % radix) * stride)
                for i in range(seq_count)
            ]
            received = lax.ppermute(rollout_mean, "seq", pairs)
            source = (digit - offset) % radix
            slots = [slots[k] + jnp.where(source == k, received, 0.0) for k in range(radix)]
        if radix == 4:
            rollout_mean = (slots[0] + slots[1]) + (slots[2] + slots[3])
        else:
            rollout_mean = slots[0] + slots[1]
        stride *= radix
    return (token_diff, rollout_mean)


def solution(mesh):
    return jax.shard_map(
        local,
        mesh=mesh,
        in_specs=(
            P("seq", None),
            P("seq", None),
            P("seq"),
            P(),
            P("seq"),
            P(),
            P(),
            P(),
            P(None, "vocab"),
            P(None, "vocab"),
            P(None, "vocab"),
            P(),
            P(),
            P("vocab", None),
            P(),
            P(None, "vocab"),
            P(None, "seq", "vocab"),
            P(None, "seq", "vocab"),
            P(),
            P(None, "vocab"),
            P(None, "vocab"),
            P(None, "vocab"),
            P(),
            P(),
            P("vocab", None),
            P(),
            P(None, "vocab"),
            P(None, "seq", "vocab"),
            P(None, "seq", "vocab"),
        ),
        out_specs=(P("seq"), P()),
        check_vma=False,
    )
```
